32 devices in a mesh: shard: 4 (over y, x), ctx: 4 (over z), tp: 2 (over core).
Axes of the slice: x: 2, y: 2, z: 4, core: 2. Of those that a mesh axis runs over, the one named last changes fastest.
Arguments:
- tokens: bfloat16 [10240, 768], P(('shard', 'ctx')), may hold values from -6 to 6
- seq_lengths: int32 [4], P('shard'), may hold values from 2240 to 2560
- query_weight: bfloat16 [768, 768], P('shard', 'tp'), may hold values from -0.21875 to 0.21875
- query_bias: bfloat16 [768], P(('shard', 'tp')), may hold values from -0.59765625 to 0.59765625
- key_weight: bfloat16 [768, 768], P('shard', 'tp'), may hold values from -0.21875 to 0.21875
- value_weight: bfloat16 [768, 768], P('shard', 'tp'), may hold values from -0.21875 to 0.21875
- value_bias: bfloat16 [768], P(('shard', 'tp')), may hold values from -0.119628906 to 0.119628906
- output_weight: bfloat16 [768, 768], P('shard', 'tp'), may hold values from -6 to 6
- output_bias: bfloat16 [768], P('shard'), may hold values from -0.59765625 to 0.59765625
- attn_gain: bfloat16 [768], P('shard'), may hold values from 0.5 to 1.5
- attn_shift: bfloat16 [768], P('shard'), may hold values from -0.59765625 to 0.59765625
- inner_weight: bfloat16 [768, 3072], P('shard', 'tp'), may hold values from -0.21875 to 0.21875
- inner_bias: bfloat16 [3072], P(('shard', 'tp')), may hold values from -0.59765625 to 0.59765625
- outer_weight: bfloat16 [768, 3072], P('shard', 'tp'), may hold values from -0.109375 to 0.109375
- outer_bias: bfloat16 [768], P('shard'), may hold values from -0.59765625 to 0.59765625
- final_gain: bfloat16 [768], P('shard'), may hold values from 0.5 to 1.5
- final_shift: bfloat16 [768], P('shard'), may hold values from -0.59765625 to 0.59765625
- upstream: bfloat16 [10240, 768], P(('shard', 'ctx')), may hold values from -6 to 6
Outputs:
- layer_out: bfloat16 [10240, 768], P(('shard', 'ctx'))
- tokens_gradient: float32 [10240, 768], P(('shard', 'ctx'))
- query_weight_gradient: float32 [768, 768], P('shard', 'tp')
- query_bias_gradient: float32 [768], P(('shard', 'tp'))
- key_weight_gradient: float32 [768, 768], P('shard', 'tp')
- value_weight_gradient: float32 [768, 768], P('shard', 'tp')
- value_bias_gradient: float32 [768], P(('shard', 'tp'))
- output_weight_gradient: float32 [768, 768], P('shard', 'tp')
- output_bias_gradient: float32 [768], P('shard')
- attn_gain_gradient: float32 [768], P('shard')
- attn_shift_gradient: float32 [768], P('shard')
- inner_weight_gradient: float32 [768, 3072], P('shard', 'tp')
- inner_bias_gradient: float32 [3072], P(('shard', 'tp'))
- outer_weight_gradient: float32 [768, 3072], P('shard', 'tp')
- outer_bias_gradient: float32 [768], P('shard')
- final_gain_gradient: float32 [768], P('shard')
- final_shift_gradient: float32 [768], P('shard')
The draws below stay inside these ranges and needn't reach their ends.
All inputs are finite; a program needn't handle non-finite values.
Results may differ from the reference program's by a relative error of at most 0.014.
Values may be sent and summed in bfloat16 or wider, within the bound.
No kernel may reach another device: no remote copies, remote signals or barrier semaphores. Data moves between devices by JAX's collectives and lax.ppermute only.
A program may use at most 128 MiB of HBM per device.

```python
import jax
import jax.numpy as jnp
from jax import lax

D = 768
HEADS = 12
HEAD_DIM = 64
FF = 3072
SEQ_LEN = 2560
SEQS = 4
TOKENS = 10240


def place_ends(entries, stream_key, low, largest):
    longest = entries.shape.index(max(entries.shape))
    spots = []
    for shift in (0, 1):
        where = [jax.random.randint(jax.random.fold_in(stream_key, axis), (), 0, length) for axis, length in enumerate(entries.shape)]
        where[longest] = (where[longest] + shift) % entries.shape[longest]
        spots.append(tuple(where))
    return entries.at[spots[0]].set(low).at[spots[1]].set(largest)


def steps_of(own_key, dims, cuts, low, largest):
    loudness, own = 1.0, jax.random.fold_in(own_key, 6)
    for axis_at, parts in cuts:
        heights = jnp.exp(jax.random.uniform(jax.random.fold_in(own, axis_at), (parts,), jnp.float32, low / len(cuts), largest / len(cuts)))
        loudness = loudness * jnp.repeat(heights, dims[axis_at] // parts).reshape([-1 if axis == axis_at else 1 for axis in range(len(dims))])
    return loudness


def normal_values(key, dims, spread, bound, cuts=(), held_as=jnp.bfloat16):
    result = jax.random.normal(key, dims, jnp.float32) * spread
    if len(cuts) > 0:
        result = steps_of(key, dims, cuts, -0.22, 0.18) * result
    return jnp.clip(result, min=-bound, max=bound).astype(held_as)


def setup_inputs(seed: int = 0) -> dict:
    key_of = jax.random.split(jax.random.key(seed), 19)
    tokens = normal_values(key_of[0], (TOKENS, D), 1.0, 6.0, ((0, 16),))
    seq_lengths = place_ends(jax.random.randint(key_of[1], (SEQS,), SEQ_LEN * 7 // 8, SEQ_LEN + 1), jax.random.fold_in(key_of[1], 1), SEQ_LEN * 7 // 8, SEQ_LEN).astype(jnp.int32)
    query_weight = normal_values(key_of[2], (D, D), D ** -0.5, 0.21875, ((0, 4), (1, 2)))
    query_bias = normal_values(key_of[3], (D,), 0.1, 0.59765625, ((0, 8),))
    key_weight = normal_values(key_of[4], (D, D), D ** -0.5, 0.21875, ((0, 4), (1, 2)))
    value_weight = normal_values(key_of[5], (D, D), D ** -0.5, 0.21875, ((0, 4), (1, 2)))
    value_bias = normal_values(key_of[6], (D,), 0.02, 0.119628906, ((0, 8),))
    output_weight = normal_values(key_of[7], (D, D), (max(1, 4 * D // SEQ_LEN)) ** -0.5, 6.0, ((0, 4), (1, 2)))
    output_bias = normal_values(key_of[8], (D,), 0.1, 0.59765625, ((0, 4),))
    attn_gain = jnp.clip(1.0 + 0.1 * jax.random.normal(key_of[9], (D,), jnp.float32), 0.5, 1.5).astype(jnp.bfloat16)
    attn_shift = normal_values(key_of[10], (D,), 0.1, 0.59765625, ((0, 4),))
    inner_weight = normal_values(key_of[11], (D, FF), D ** -0.5, 0.21875, ((0, 4), (1, 2)))
    inner_bias = normal_values(key_of[12], (FF,), 0.1, 0.59765625, ((0, 8),))
    outer_weight = normal_values(key_of[13], (D, FF), FF ** -0.5, 0.109375, ((0, 4), (1, 2)))
    outer_bias = normal_values(key_of[14], (D,), 0.1, 0.59765625, ((0, 4),))
    final_gain = jnp.clip(1.0 + 0.1 * jax.random.normal(key_of[15], (D,), jnp.float32), 0.5, 1.5).astype(jnp.bfloat16)
    final_shift = normal_values(key_of[16], (D,), 0.1, 0.59765625, ((0, 4),))
    upstream = normal_values(key_of[17], (TOKENS, D), 1.0, 6.0, ((0, 16),))
    return {"tokens": tokens, "seq_lengths": seq_lengths, "query_weight": query_weight, "query_bias": query_bias, "key_weight": key_weight, "value_weight": value_weight, "value_bias": value_bias, "output_weight": output_weight, "output_bias": output_bias, "attn_gain": attn_gain, "attn_shift": attn_shift, "inner_weight": inner_weight, "inner_bias": inner_bias, "outer_weight": outer_weight, "outer_bias": outer_bias, "final_gain": final_gain, "final_shift": final_shift, "upstream": upstream}


EPSILON = 1e-12
HIGH = lax.Precision.HIGHEST

@jax.custom_vjp
def low(v):
    return lax.optimization_barrier(v.astype(jnp.bfloat16)).astype(jnp.float32)

@jax.custom_vjp
def low_back(v):
    return v

def low_keep(v):
    return (low(v), None)

def low_pass(kept, grad):
    return (grad,)

def back_keep(v):
    return (v, None)

def back_low(kept, grad):
    return (low(grad),)
low.defvjp(low_keep, low_pass)
low_back.defvjp(back_keep, back_low)

def matmul(left, right):
    return jnp.dot(left, right, precision=HIGH, preferred_element_type=jnp.float32)

def layer_norm(hidden, gain, shift):
    center = hidden - lax.optimization_barrier(jnp.mean(hidden, -1, keepdims=True))
    variance = lax.optimization_barrier(jnp.mean(center * center, -1, keepdims=True))
    return center * lax.rsqrt(variance + EPSILON) * gain + shift

def split_heads(matrix):
    return matrix.reshape(matrix.shape[0], HEADS, HEAD_DIM).transpose(1, 0, 2)

def forward(inputs, params, length):
    query_weight, query_bias, key_weight, value_weight, value_bias, output_weight, output_bias, attn_gain, attn_shift, inner_weight, inner_bias, outer_weight, outer_bias, final_gain, final_shift = params
    query = low(low_back(matmul(inputs, query_weight) + query_bias))
    keys = low(low_back(matmul(inputs, key_weight)))
    values = low(low_back(matmul(inputs, value_weight) + value_bias))
    allowed = jnp.arange(SEQ_LEN) < length
    factor = HEAD_DIM ** (-0.5)

    def one_head(triple):
        query_head, key_head, value_head = triple
        scores = low_back(matmul(query_head, key_head.T) * factor)
        scores = jnp.where(allowed[None, :], scores, -1e+30)
        shifted = jnp.exp(scores - lax.optimization_barrier(jnp.max(scores, -1, keepdims=True)))
        portion = shifted / lax.optimization_barrier(jnp.sum(shifted, -1, keepdims=True))
        return matmul(low(portion), value_head)
    heads_out = lax.map(jax.checkpoint(one_head), (split_heads(query), split_heads(keys), split_heads(values)))
    context = low(low_back(heads_out.transpose(1, 0, 2).reshape(SEQ_LEN, D)))
    attended = low_back(matmul(context, output_weight.T) + output_bias)
    normed = layer_norm(inputs + attended, attn_gain, attn_shift)
    hidden = low_back(matmul(low(normed), inner_weight) + inner_bias)
    active = low(jax.nn.gelu(hidden, approximate=False))
    branch = low_back(matmul(active, outer_weight.T) + outer_bias)
    return layer_norm(normed + branch, final_gain, final_shift)

def reference(tokens, seq_lengths, query_weight, query_bias, key_weight, value_weight, value_bias, output_weight, output_bias, attn_gain, attn_shift, inner_weight, inner_bias, outer_weight, outer_bias, final_gain, final_shift, upstream):
    params = tuple((param.astype(jnp.float32) for param in (query_weight, query_bias, key_weight, value_weight, value_bias, output_weight, output_bias, attn_gain, attn_shift, inner_weight, inner_bias, outer_weight, outer_bias, final_gain, final_shift)))
    sequences = tokens.reshape(SEQS, SEQ_LEN, D)
    cotangents = upstream.reshape(SEQS, SEQ_LEN, D)
    starting = tuple((jnp.zeros(param.shape, jnp.float32) for param in params))

    def per_sequence(running, sequence_item):
        inputs, length, cotangent = sequence_item
        output, pullback = jax.vjp(lambda source, weights: forward(source, weights, length), inputs.astype(jnp.float32), params)
        input_gradient, weight_gradients = pullback(cotangent.astype(jnp.float32))
        running = tuple((before + gradient for before, gradient in zip(running, weight_gradients)))
        return (running, (output.astype(jnp.bfloat16), input_gradient))
    totals, (outputs, input_gradients) = lax.scan(per_sequence, starting, (sequences, seq_lengths, cotangents))
    return (outputs.reshape(TOKENS, D), input_gradients.reshape(TOKENS, D), totals[0], totals[1], totals[2], totals[3], totals[4], totals[5], totals[6], totals[7], totals[8], totals[9], totals[10], totals[11], totals[12], totals[13], totals[14])
```

```python
import jax
import jax.numpy as jnp
from jax import lax
from jax.sharding import PartitionSpec as P

HEAD_DIM = 64


EPSILON = 1e-12


def norm_parts(hidden):
    center = hidden - jnp.mean(hidden, -1, keepdims=True)
    inverse = lax.rsqrt(jnp.mean(center * center, -1, keepdims=True) + EPSILON)
    return (center * inverse, inverse)


def norm_back(gradient, normal_form, inverse, gain):
    scaled = gradient * gain
    inner = (
        scaled
        - jnp.mean(scaled, -1, keepdims=True)
        - normal_form * jnp.mean(scaled * normal_form, -1, keepdims=True)
    )
    return (inner * inverse, jnp.sum(gradient * normal_form, 0), jnp.sum(gradient, 0))


def exact_gelu(values):
    return jax.nn.gelu(values, approximate=False)


def tp_sum(value):
    if lax.axis_size("tp") == 2:
        return value + lax.ppermute(value, "tp", [(0, 1), (1, 0)])
    return lax.psum(value, "tp")


def on_device(
    tokens,
    seq_lengths,
    query_weight,
    query_bias,
    key_weight,
    value_weight,
    value_bias,
    output_weight,
    output_bias,
    attn_gain,
    attn_shift,
    inner_weight,
    inner_bias,
    outer_weight,
    outer_bias,
    final_gain,
    final_shift,
    upstream,
):
    row_count, model_width = tokens.shape
    tensor_place = lax.axis_index("tp")
    tensor_count = lax.axis_size("tp")
    head_width = query_weight.shape[1]
    hidden_width = inner_weight.shape[1]
    head_count = head_width // HEAD_DIM
    factor = HEAD_DIM ** (-0.5)
    f32 = jnp.float32

    qkv_full = lax.all_gather(
        jnp.concatenate([query_weight, key_weight, value_weight], axis=1),
        "shard", axis=0, tiled=True,
    )
    query_full = qkv_full[:, :head_width]
    key_full = qkv_full[:, head_width : 2 * head_width]
    value_full = qkv_full[:, 2 * head_width :]
    rest_full = lax.all_gather(
        jnp.concatenate([output_weight, inner_weight, outer_weight], axis=1),
        "shard", axis=0, tiled=True,
    )
    output_full = rest_full[:, :head_width]
    inner_full = rest_full[:, head_width : head_width + hidden_width]
    outer_full = rest_full[:, head_width + hidden_width :]

    shard_vectors = (output_bias, attn_gain, attn_shift, outer_bias, final_gain, final_shift)
    piece = output_bias.shape[0]
    packed = jnp.concatenate(shard_vectors + (query_bias, value_bias, inner_bias))
    gathered = lax.all_gather(packed, ("shard", "tp"), axis=0)
    by_shard = gathered[::tensor_count, : 6 * piece].reshape(-1, 6, piece)
    full_vectors = by_shard.transpose(1, 0, 2).reshape(6, -1).astype(f32)
    outbias_full, gain_first, shift_first, outerbias_full, gain_second, shift_second = full_vectors
    offset = 6 * piece
    qb = query_bias.shape[0]
    ib = inner_bias.shape[0]
    qbias_all = gathered[:, offset : offset + qb].reshape(-1)
    vbias_all = gathered[:, offset + qb : offset + 2 * qb].reshape(-1)
    ibias_all = gathered[:, offset + 2 * qb : offset + 2 * qb + ib].reshape(-1)
    query_shift = lax.dynamic_slice_in_dim(qbias_all, tensor_place * head_width, head_width).astype(f32)
    value_shift = lax.dynamic_slice_in_dim(vbias_all, tensor_place * head_width, head_width).astype(f32)
    inner_shift = lax.dynamic_slice_in_dim(ibias_all, tensor_place * hidden_width, hidden_width).astype(f32)

    projected = jnp.dot(tokens, qkv_full, preferred_element_type=f32)
    query = (projected[:, :head_width] + query_shift).astype(jnp.bfloat16)
    key_local = projected[:, head_width : 2 * head_width].astype(jnp.bfloat16)
    value_local = (projected[:, 2 * head_width :] + value_shift).astype(jnp.bfloat16)
    kv = lax.all_gather(
        jnp.concatenate([key_local, value_local], axis=1), "ctx", axis=0, tiled=True
    )
    keys = kv[:, :head_width]
    values = kv[:, head_width:]
    allowed = jnp.arange(keys.shape[0]) < seq_lengths[0]

    def split_heads(matrix):
        return matrix.reshape(matrix.shape[0], head_count, HEAD_DIM).transpose(1, 0, 2)

    def join_heads(stacked):
        return stacked.transpose(1, 0, 2).reshape(stacked.shape[1], head_width)

    def scores_of(query_head, key_head):
        scores = (
            jnp.einsum("qd,kd->qk", query_head, key_head, preferred_element_type=f32)
            * factor
        )
        return jnp.where(allowed[None, :], scores, -1e30)

    def head_forward(triple):
        query_head, key_head, value_head = triple
        scores = scores_of(query_head, key_head)
        highest = jnp.max(scores, -1, keepdims=True)
        shifted = jnp.exp(scores - highest)
        summed = jnp.sum(shifted, -1, keepdims=True)
        portion = (shifted / summed).astype(jnp.bfloat16)
        mixed = jnp.dot(portion, value_head, preferred_element_type=f32)
        return (mixed.astype(jnp.bfloat16), (highest + jnp.log(summed))[:, 0])

    query_heads = split_heads(query)
    key_heads = split_heads(keys)
    value_heads = split_heads(values)
    context_heads, log_sums = lax.map(head_forward, (query_heads, key_heads, value_heads))
    context = join_heads(context_heads)
    attn_part = jnp.einsum("th,oh->to", context, output_full, preferred_element_type=f32)
    attended = tp_sum(attn_part) + outbias_full
    normal_first, inverse_first = norm_parts(tokens.astype(f32) + attended)
    normed = normal_first * gain_first + shift_first
    normed_low = normed.astype(jnp.bfloat16)
    hidden = jnp.dot(normed_low, inner_full, preferred_element_type=f32) + inner_shift
    active = exact_gelu(hidden).astype(jnp.bfloat16)
    branch_part = jnp.einsum("tf,of->to", active, outer_full, preferred_element_type=f32)
    branch = tp_sum(branch_part) + outerbias_full
    normal_second, inverse_second = norm_parts(normed + branch)
    layer_out = (normal_second * gain_second + shift_second).astype(jnp.bfloat16)

    dres_second, final_gain_part, final_shift_part = norm_back(
        upstream.astype(f32), normal_second, inverse_second, gain_second
    )
    dbranch = dres_second.astype(jnp.bfloat16)
    outer_bias_part = jnp.sum(dbranch.astype(f32), 0)
    outer_weight_part = jnp.einsum("to,tf->of", dbranch, active, preferred_element_type=f32)
    dactive = jnp.dot(dbranch, outer_full, preferred_element_type=f32)
    unused, gelu_pull = jax.vjp(exact_gelu, hidden)
    dhidden = gelu_pull(dactive)[0].astype(jnp.bfloat16)
    inner_weight_part = jnp.einsum("td,tf->df", normed_low, dhidden, preferred_element_type=f32)
    inner_bias_part = jnp.sum(dhidden.astype(f32), 0)
    dnormed_part = jnp.einsum("tf,df->td", dhidden, inner_full, preferred_element_type=f32)
    dnormed = dres_second + tp_sum(dnormed_part)
    dres_first, attn_gain_part, attn_shift_part = norm_back(
        dnormed, normal_first, inverse_first, gain_first
    )
    dattended = dres_first.astype(jnp.bfloat16)
    output_bias_part = jnp.sum(dattended.astype(f32), 0)
    output_weight_part = jnp.einsum("to,th->oh", dattended, context, preferred_element_type=f32)
    dcontext = jnp.dot(dattended, output_full, preferred_element_type=f32).astype(jnp.bfloat16)

    rest_piece = lax.psum(
        lax.psum_scatter(
            jnp.concatenate([output_weight_part, inner_weight_part, outer_weight_part], axis=1),
            "shard", scatter_dimension=0, tiled=True,
        ),
        "ctx",
    )
    output_total = rest_piece[:, :head_width]
    inner_total = rest_piece[:, head_width : head_width + hidden_width]
    outer_total = rest_piece[:, head_width + hidden_width :]

    def head_backward(quintet):
        query_head, key_head, value_head, dcontext_head, log_sum = quintet
        portion = jnp.exp(scores_of(query_head, key_head) - log_sum[:, None])
        dportion = jnp.einsum("qd,kd->qk", dcontext_head, value_head, preferred_element_type=f32)
        dvalue_head = jnp.einsum(
            "qk,qd->kd", portion.astype(jnp.bfloat16), dcontext_head, preferred_element_type=f32
        )
        centering = jnp.sum(portion * dportion, -1, keepdims=True)
        dscores = (portion * (dportion - centering)).astype(jnp.bfloat16)
        dquery_head = jnp.dot(dscores, key_head, preferred_element_type=f32) * factor
        dkey_head = (
            jnp.einsum("qk,qd->kd", dscores, query_head, preferred_element_type=f32) * factor
        )
        return (dquery_head.astype(jnp.bfloat16), dkey_head, dvalue_head)

    dquery_heads, dkey_heads, dvalue_heads = lax.map(
        head_backward, (query_heads, key_heads, value_heads, split_heads(dcontext), log_sums)
    )
    dquery = join_heads(dquery_heads)
    dkv = lax.psum_scatter(
        jnp.concatenate([join_heads(dkey_heads), join_heads(dvalue_heads)], axis=1),
        "ctx", scatter_dimension=0, tiled=True,
    ).astype(jnp.bfloat16)
    dkeys = dkv[:, :head_width]
    dvalues = dkv[:, head_width:]
    dqkv = jnp.concatenate([dquery, dkeys, dvalues], axis=1)
    qkv_weight_part = jnp.einsum("td,th->dh", tokens, dqkv, preferred_element_type=f32)
    query_bias_part = jnp.sum(dquery.astype(f32), 0)
    value_bias_part = jnp.sum(dvalues.astype(f32), 0)
    dinput_part = jnp.einsum("th,dh->td", dqkv, qkv_full, preferred_element_type=f32)
    tokens_gradient = dres_first + tp_sum(dinput_part)
    qkv_piece = lax.psum(
        lax.psum_scatter(qkv_weight_part, "shard", scatter_dimension=0, tiled=True), "ctx"
    )
    query_total = qkv_piece[:, :head_width]
    key_total = qkv_piece[:, head_width : 2 * head_width]
    value_total = qkv_piece[:, 2 * head_width :]

    first_core = (tensor_place == 0).astype(f32)
    spread = lambda part, width: lax.dynamic_update_slice_in_dim(
        jnp.zeros((width * tensor_count,), f32), part, tensor_place * width, 0
    )
    vector_parts = jnp.concatenate(
        [
            first_core * jnp.stack(
                [output_bias_part, attn_gain_part, attn_shift_part, outer_bias_part,
                 final_gain_part, final_shift_part]
            ).reshape(-1),
            spread(query_bias_part, head_width),
            spread(value_bias_part, head_width),
            spread(inner_bias_part, hidden_width),
        ]
    )
    vector_sums = lax.psum(vector_parts, ("shard", "ctx", "tp"))
    shard_place = lax.axis_index("shard")
    shard_sums = vector_sums[: 6 * model_width].reshape(6, model_width)
    shard_sums = lax.dynamic_slice_in_dim(shard_sums, shard_place * piece, piece, 1)
    outbias_total, attn_gain_total, attn_shift_total, outerbias_total, final_gain_total, final_shift_total = shard_sums
    block = shard_place * tensor_count + tensor_place
    start = 6 * model_width
    qbias_total = lax.dynamic_slice_in_dim(vector_sums, start + block * qb, qb)
    vbias_total = lax.dynamic_slice_in_dim(vector_sums, start + model_width + block * qb, qb)
    ibias_total = lax.dynamic_slice_in_dim(vector_sums, start + 2 * model_width + block * ib, ib)
    return (
        layer_out,
        tokens_gradient,
        query_total,
        qbias_total,
        key_total,
        value_total,
        vbias_total,
        output_total,
        outbias_total,
        attn_gain_total,
        attn_shift_total,
        inner_total,
        ibias_total,
        outer_total,
        outerbias_total,
        final_gain_total,
        final_shift_total,
    )


def solution(mesh):
    placed = (
        P(("shard", "ctx"), None),
        P("shard"),
        P("shard", "tp"),
        P(("shard", "tp")),
        P("shard", "tp"),
        P("shard", "tp"),
        P(("shard", "tp")),
        P("shard", "tp"),
        P("shard"),
        P("shard"),
        P("shard"),
        P("shard", "tp"),
        P(("shard", "tp")),
        P("shard", "tp"),
        P("shard"),
        P("shard"),
        P("shard"),
        P(("shard", "ctx"), None),
    )
    return jax.shard_map(
        on_device,
        mesh=mesh,
        in_specs=placed,
        out_specs=(
            P(("shard", "ctx"), None),
            P(("shard", "ctx"), None),
            P("shard", "tp"),
            P(("shard", "tp")),
            P("shard", "tp"),
            P("shard", "tp"),
            P(("shard", "tp")),
            P("shard", "tp"),
            P("shard"),
            P("shard"),
            P("shard"),
            P("shard", "tp"),
            P(("shard", "tp")),
            P("shard", "tp"),
            P("shard"),
            P("shard"),
            P("shard"),
        ),
        check_vma=False,
    )
```

```python
import jax
import jax.numpy as jnp
from jax import lax
from jax.sharding import PartitionSpec as P

HEAD_DIM = 64


EPSILON = 1e-12


def norm_parts(hidden):
    center = hidden - jnp.mean(hidden, -1, keepdims=True)
    inverse = lax.rsqrt(jnp.mean(center * center, -1, keepdims=True) + EPSILON)
    return (center * inverse, inverse)


def norm_back(gradient, normal_form, inverse, gain):
    scaled = gradient * gain
    inner = (
        scaled
        - jnp.mean(scaled, -1, keepdims=True)
        - normal_form * jnp.mean(scaled * normal_form, -1, keepdims=True)
    )
    return (inner * inverse, jnp.sum(gradient * normal_form, 0), jnp.sum(gradient, 0))


def exact_gelu(values):
    return jax.nn.gelu(values, approximate=False)


def tp_sum(value):
    if lax.axis_size("tp") == 2:
        return value + lax.ppermute(value, "tp", [(0, 1), (1, 0)])
    return lax.psum(value, "tp")


def tp_gather(value):
    if lax.axis_size("tp") == 2:
        other = lax.ppermute(value, "tp", [(0, 1), (1, 0)])
        first = lax.axis_index("tp") == 0
        return jnp.stack([jnp.where(first, value, other), jnp.where(first, other, value)])
    return lax.all_gather(value, "tp")


def on_device(
    tokens,
    seq_lengths,
    query_weight,
    query_bias,
    key_weight,
    value_weight,
    value_bias,
    output_weight,
    output_bias,
    attn_gain,
    attn_shift,
    inner_weight,
    inner_bias,
    outer_weight,
    outer_bias,
    final_gain,
    final_shift,
    upstream,
):
    row_count, model_width = tokens.shape
    tensor_place = lax.axis_index("tp")
    tensor_count = lax.axis_size("tp")
    head_width = query_weight.shape[1]
    hidden_width = inner_weight.shape[1]
    head_count = head_width // HEAD_DIM
    factor = HEAD_DIM ** (-0.5)
    f32 = jnp.float32

    qb = query_bias.shape[0]
    ib = inner_bias.shape[0]
    piece = output_bias.shape[0]
    tp_blocks = tp_gather(jnp.concatenate([query_bias, value_bias, inner_bias]))
    bias_columns = jnp.concatenate(
        [
            tp_blocks[:, :qb].reshape(piece, 1),
            tp_blocks[:, qb : 2 * qb].reshape(piece, 1),
            tp_blocks[:, 2 * qb :].reshape(piece, -1),
        ],
        axis=1,
    )
    shard_columns = jnp.stack(
        [output_bias, attn_gain, attn_shift, outer_bias, final_gain, final_shift], axis=1
    )
    qkv_full = lax.all_gather(
        jnp.concatenate(
            [query_weight, key_weight, value_weight, shard_columns, bias_columns], axis=1
        ),
        "shard", axis=0, tiled=True,
    )
    vector_full = qkv_full[:, 3 * head_width :]
    qkv_full = qkv_full[:, : 3 * head_width]
    query_full = qkv_full[:, :head_width]
    key_full = qkv_full[:, head_width : 2 * head_width]
    value_full = qkv_full[:, 2 * head_width :]
    rest_full = lax.all_gather(
        jnp.concatenate([output_weight, inner_weight, outer_weight], axis=1),
        "shard", axis=0, tiled=True,
    )
    output_full = rest_full[:, :head_width]
    inner_full = rest_full[:, head_width : head_width + hidden_width]
    outer_full = rest_full[:, head_width + hidden_width :]

    full_vectors = vector_full[:, :6].T.astype(f32)
    outbias_full, gain_first, shift_first, outerbias_full, gain_second, shift_second = full_vectors
    qbias_all = vector_full[:, 6]
    vbias_all = vector_full[:, 7]
    ibias_all = vector_full[:, 8:].reshape(-1)
    query_shift = lax.dynamic_slice_in_dim(qbias_all, tensor_place * head_width, head_width).astype(f32)
    value_shift = lax.dynamic_slice_in_dim(vbias_all, tensor_place * head_width, head_width).astype(f32)
    inner_shift = lax.dynamic_slice_in_dim(ibias_all, tensor_place * hidden_width, hidden_width).astype(f32)

    projected = jnp.dot(tokens, qkv_full, preferred_element_type=f32)
    query = (projected[:, :head_width] + query_shift).astype(jnp.bfloat16)
    key_local = projected[:, head_width : 2 * head_width].astype(jnp.bfloat16)
    value_local = (projected[:, 2 * head_width :] + value_shift).astype(jnp.bfloat16)
    kv = lax.all_gather(
        jnp.concatenate([key_local, value_local], axis=1), "ctx", axis=0, tiled=True
    )
    keys = kv[:, :head_width]
    values = kv[:, head_width:]
    allowed = jnp.arange(keys.shape[0]) < seq_lengths[0]

    def split_heads(matrix):
        return matrix.reshape(matrix.shape[0], head_count, HEAD_DIM).transpose(1, 0, 2)

    def join_heads(stacked):
        return stacked.transpose(1, 0, 2).reshape(stacked.shape[1], head_width)

    def scores_of(query_head, key_head):
        scores = (
            jnp.einsum("qd,kd->qk", query_head, key_head, preferred_element_type=f32)
            * factor
        )
        return jnp.where(allowed[None, :], scores, -1e30)

    def head_forward(triple):
        query_head, key_head, value_head = triple
        scores = scores_of(query_head, key_head)
        highest = jnp.max(scores, -1, keepdims=True)
        shifted = jnp.exp(scores - highest)
        summed = jnp.sum(shifted, -1, keepdims=True)
        portion = (shifted / summed).astype(jnp.bfloat16)
        mixed = jnp.dot(portion, value_head, preferred_element_type=f32)
        return (mixed.astype(jnp.bfloat16), (highest + jnp.log(summed))[:, 0])

    query_heads = split_heads(query)
    key_heads = split_heads(keys)
    value_heads = split_heads(values)
    context_heads, log_sums = lax.map(head_forward, (query_heads, key_heads, value_heads))
    context = join_heads(context_heads)
    attn_part = jnp.einsum("th,oh->to", context, output_full, preferred_element_type=f32)
    attended = tp_sum(attn_part) + outbias_full
    normal_first, inverse_first = norm_parts(tokens.astype(f32) + attended)
    normed = normal_first * gain_first + shift_first
    normed_low = normed.astype(jnp.bfloat16)
    hidden = jnp.dot(normed_low, inner_full, preferred_element_type=f32) + inner_shift
    active = exact_gelu(hidden).astype(jnp.bfloat16)
    branch_part = jnp.einsum("tf,of->to", active, outer_full, preferred_element_type=f32)
    branch = tp_sum(branch_part) + outerbias_full
    normal_second, inverse_second = norm_parts(normed + branch)
    layer_out = (normal_second * gain_second + shift_second).astype(jnp.bfloat16)

    dres_second, final_gain_part, final_shift_part = norm_back(
        upstream.astype(f32), normal_second, inverse_second, gain_second
    )
    dbranch = dres_second.astype(jnp.bfloat16)
    outer_bias_part = jnp.sum(dbranch.astype(f32), 0)
    outer_weight_part = jnp.einsum("to,tf->of", dbranch, active, preferred_element_type=f32)
    dactive = jnp.dot(dbranch, outer_full, preferred_element_type=f32)
    unused, gelu_pull = jax.vjp(exact_gelu, hidden)
    dhidden = gelu_pull(dactive)[0].astype(jnp.bfloat16)
    inner_weight_part = jnp.einsum("td,tf->df", normed_low, dhidden, preferred_element_type=f32)
    inner_bias_part = jnp.sum(dhidden.astype(f32), 0)
    dnormed_part = jnp.einsum("tf,df->td", dhidden, inner_full, preferred_element_type=f32)
    dnormed = dres_second + tp_sum(dnormed_part)
    dres_first, attn_gain_part, attn_shift_part = norm_back(
        dnormed, normal_first, inverse_first, gain_first
    )
    dattended = dres_first.astype(jnp.bfloat16)
    output_bias_part = jnp.sum(dattended.astype(f32), 0)
    output_weight_part = jnp.einsum("to,th->oh", dattended, context, preferred_element_type=f32)
    dcontext = jnp.dot(dattended, output_full, preferred_element_type=f32).astype(jnp.bfloat16)

    low = jnp.bfloat16
    rows = model_width
    early = jnp.concatenate(
        [
            output_weight_part,
            inner_weight_part,
            outer_weight_part,
            jnp.stack(
                [output_bias_part, attn_gain_part, attn_shift_part, outer_bias_part,
                 final_gain_part, final_shift_part],
                axis=1,
            ),
            tp_gather(inner_bias_part).reshape(rows, -1),
        ],
        axis=1,
    ).astype(low)
    early, dcontext = lax.optimization_barrier((early, dcontext))
    early_piece = lax.psum(
        lax.psum_scatter(early, "shard", scatter_dimension=0, tiled=True), "ctx"
    ).astype(f32)
    output_total = early_piece[:, :head_width]
    inner_total = early_piece[:, head_width : head_width + hidden_width]
    outer_total = early_piece[:, head_width + hidden_width : head_width + 2 * hidden_width]
    early_vectors = early_piece[:, head_width + 2 * hidden_width :]
    outbias_total, attn_gain_total, attn_shift_total, outerbias_total, final_gain_total, final_shift_total = (
        early_vectors[:, :6].T
    )
    local_rows = piece // tensor_count
    ibias_total = lax.dynamic_slice_in_dim(
        early_vectors[:, 6:], tensor_place * local_rows, local_rows, 0
    ).reshape(-1)

    def head_backward(quintet):
        query_head, key_head, value_head, dcontext_head, log_sum = quintet
        portion = jnp.exp(scores_of(query_head, key_head) - log_sum[:, None])
        dportion = jnp.einsum("qd,kd->qk", dcontext_head, value_head, preferred_element_type=f32)
        dvalue_head = jnp.einsum(
            "qk,qd->kd", portion.astype(jnp.bfloat16), dcontext_head, preferred_element_type=f32
        )
        centering = jnp.sum(portion * dportion, -1, keepdims=True)
        dscores = (portion * (dportion - centering)).astype(jnp.bfloat16)
        dquery_head = jnp.dot(dscores, key_head, preferred_element_type=f32) * factor
        dkey_head = (
            jnp.einsum("qk,qd->kd", dscores, query_head, preferred_element_type=f32) * factor
        )
        return (dquery_head.astype(jnp.bfloat16), dkey_head, dvalue_head)

    dquery_heads, dkey_heads, dvalue_heads = lax.map(
        head_backward, (query_heads, key_heads, value_heads, split_heads(dcontext), log_sums)
    )
    dquery = join_heads(dquery_heads)
    dkv = lax.psum_scatter(
        jnp.concatenate([join_heads(dkey_heads), join_heads(dvalue_heads)], axis=1).astype(low),
        "ctx", scatter_dimension=0, tiled=True,
    ).astype(jnp.bfloat16)
    dkeys = dkv[:, :head_width]
    dvalues = dkv[:, head_width:]
    dqkv = jnp.concatenate([dquery, dkeys, dvalues], axis=1)
    qkv_weight_part = jnp.einsum("td,th->dh", tokens, dqkv, preferred_element_type=f32)
    query_bias_part = jnp.sum(dquery.astype(f32), 0)
    value_bias_part = jnp.sum(dvalues.astype(f32), 0)
    dinput_part = jnp.einsum("th,dh->td", dqkv, qkv_full, preferred_element_type=f32)
    tokens_gradient = dres_first + tp_sum(dinput_part)
    late = jnp.concatenate(
        [
            qkv_weight_part,
            tp_gather(query_bias_part).reshape(rows, 1),
            tp_gather(value_bias_part).reshape(rows, 1),
        ],
        axis=1,
    ).astype(low)
    late_piece = lax.psum(
        lax.psum_scatter(late, "shard", scatter_dimension=0, tiled=True), "ctx"
    ).astype(f32)
    query_total = late_piece[:, :head_width]
    key_total = late_piece[:, head_width : 2 * head_width]
    value_total = late_piece[:, 2 * head_width : 3 * head_width]
    qbias_total = lax.dynamic_slice_in_dim(
        late_piece[:, 3 * head_width], tensor_place * local_rows, local_rows
    )
    vbias_total = lax.dynamic_slice_in_dim(
        late_piece[:, 3 * head_width + 1], tensor_place * local_rows, local_rows
    )
    return (
        layer_out,
        tokens_gradient,
        query_total,
        qbias_total,
        key_total,
        value_total,
        vbias_total,
        output_total,
        outbias_total,
        attn_gain_total,
        attn_shift_total,
        inner_total,
        ibias_total,
        outer_total,
        outerbias_total,
        final_gain_total,
        final_shift_total,
    )


def solution(mesh):
    placed = (
        P(("shard", "ctx"), None),
        P("shard"),
        P("shard", "tp"),
        P(("shard", "tp")),
        P("shard", "tp"),
        P("shard", "tp"),
        P(("shard", "tp")),
        P("shard", "tp"),
        P("shard"),
        P("shard"),
        P("shard"),
        P("shard", "tp"),
        P(("shard", "tp")),
        P("shard", "tp"),
        P("shard"),
        P("shard"),
        P("shard"),
        P(("shard", "ctx"), None),
    )
    return jax.shard_map(
        on_device,
        mesh=mesh,
        in_specs=placed,
        out_specs=(
            P(("shard", "ctx"), None),
            P(("shard", "ctx"), None),
            P("shard", "tp"),
            P(("shard", "tp")),
            P("shard", "tp"),
            P("shard", "tp"),
            P(("shard", "tp")),
            P("shard", "tp"),
            P("shard"),
            P("shard"),
            P("shard"),
            P("shard", "tp"),
            P(("shard", "tp")),
            P("shard", "tp"),
            P("shard"),
            P("shard"),
            P("shard"),
        ),
        check_vma=False,
    )
```

```python
import jax
import jax.numpy as jnp
from jax import lax
from jax.sharding import PartitionSpec as P

HEAD_DIM = 64


EPSILON = 1e-12


def norm_parts(hidden):
    center = hidden - jnp.mean(hidden, -1, keepdims=True)
    inverse = lax.rsqrt(jnp.mean(center * center, -1, keepdims=True) + EPSILON)
    return (center * inverse, inverse)


def norm_back(gradient, normal_form, inverse, gain):
    scaled = gradient * gain
    inner = (
        scaled
        - jnp.mean(scaled, -1, keepdims=True)
        - normal_form * jnp.mean(scaled * normal_form, -1, keepdims=True)
    )
    return (inner * inverse, jnp.sum(gradient * normal_form, 0), jnp.sum(gradient, 0))


def exact_gelu(values):
    return jax.nn.gelu(values, approximate=False)


def tp_sum(value):
    if lax.axis_size("tp") == 2:
        return value + lax.ppermute(value, "tp", [(0, 1), (1, 0)])
    return lax.psum(value, "tp")


def tp_gather(value):
    if lax.axis_size("tp") == 2:
        other = lax.ppermute(value, "tp", [(0, 1), (1, 0)])
        first = lax.axis_index("tp") == 0
        return jnp.stack([jnp.where(first, value, other), jnp.where(first, other, value)])
    return lax.all_gather(value, "tp")


def on_device(
    tokens,
    seq_lengths,
    query_weight,
    query_bias,
    key_weight,
    value_weight,
    value_bias,
    output_weight,
    output_bias,
    attn_gain,
    attn_shift,
    inner_weight,
    inner_bias,
    outer_weight,
    outer_bias,
    final_gain,
    final_shift,
    upstream,
):
    row_count, model_width = tokens.shape
    tensor_place = lax.axis_index("tp")
    tensor_count = lax.axis_size("tp")
    head_width = query_weight.shape[1]
    hidden_width = inner_weight.shape[1]
    head_count = head_width // HEAD_DIM
    factor = HEAD_DIM ** (-0.5)
    f32 = jnp.float32

    qb = query_bias.shape[0]
    ib = inner_bias.shape[0]
    piece = output_bias.shape[0]
    tp_blocks = tp_gather(jnp.concatenate([query_bias, value_bias, inner_bias]))
    bias_columns = jnp.concatenate(
        [
            tp_blocks[:, :qb].reshape(piece, 1),
            tp_blocks[:, qb : 2 * qb].reshape(piece, 1),
            tp_blocks[:, 2 * qb :].reshape(piece, -1),
        ],
        axis=1,
    )
    shard_columns = jnp.stack(
        [output_bias, attn_gain, attn_shift, outer_bias, final_gain, final_shift], axis=1
    )
    kv_vec_full = lax.all_gather(
        jnp.concatenate([key_weight, value_weight, shard_columns, bias_columns], axis=1),
        "shard", axis=0, tiled=True,
    )
    query_full = lax.all_gather(query_weight, "shard", axis=0, tiled=True)
    vector_full = kv_vec_full[:, 2 * head_width :]
    key_full = kv_vec_full[:, :head_width]
    value_full = kv_vec_full[:, head_width : 2 * head_width]
    qkv_full = jnp.concatenate([query_full, kv_vec_full[:, : 2 * head_width]], axis=1)
    rest_full = lax.all_gather(
        jnp.concatenate([output_weight, inner_weight, outer_weight], axis=1),
        "shard", axis=0, tiled=True,
    )
    output_full = rest_full[:, :head_width]
    inner_full = rest_full[:, head_width : head_width + hidden_width]
    outer_full = rest_full[:, head_width + hidden_width :]

    full_vectors = vector_full[:, :6].T.astype(f32)
    outbias_full, gain_first, shift_first, outerbias_full, gain_second, shift_second = full_vectors
    qbias_all = vector_full[:, 6]
    vbias_all = vector_full[:, 7]
    ibias_all = vector_full[:, 8:].reshape(-1)
    query_shift = lax.dynamic_slice_in_dim(qbias_all, tensor_place * head_width, head_width).astype(f32)
    value_shift = lax.dynamic_slice_in_dim(vbias_all, tensor_place * head_width, head_width).astype(f32)
    inner_shift = lax.dynamic_slice_in_dim(ibias_all, tensor_place * hidden_width, hidden_width).astype(f32)

    projected = jnp.dot(tokens, kv_vec_full[:, : 2 * head_width], preferred_element_type=f32)
    key_local = projected[:, :head_width].astype(jnp.bfloat16)
    value_local = (projected[:, head_width:] + value_shift).astype(jnp.bfloat16)
    query = (jnp.dot(tokens, query_full, preferred_element_type=f32) + query_shift).astype(
        jnp.bfloat16
    )
    chunk_heads = 2 if head_count % 2 == 0 else 1
    chunk_width = chunk_heads * HEAD_DIM
    kv_chunks = []
    for c in range(head_count // chunk_heads):
        columns = slice(c * chunk_width, (c + 1) * chunk_width)
        outgoing = jnp.concatenate([key_local[:, columns], value_local[:, columns]], axis=1)
        kv_chunks.append(lax.all_gather(outgoing, "ctx", axis=0, tiled=True))
    keys = jnp.concatenate([chunk[:, :chunk_width] for chunk in kv_chunks], axis=1)
    values = jnp.concatenate([chunk[:, chunk_width:] for chunk in kv_chunks], axis=1)
    allowed = jnp.arange(keys.shape[0]) < seq_lengths[0]

    def split_heads_of(matrix, count):
        return matrix.reshape(matrix.shape[0], count, HEAD_DIM).transpose(1, 0, 2)

    def split_heads(matrix):
        return split_heads_of(matrix, head_count)

    def join_heads(stacked):
        return stacked.transpose(1, 0, 2).reshape(stacked.shape[1], head_width)

    def scores_of(query_head, key_head):
        scores = (
            jnp.einsum("qd,kd->qk", query_head, key_head, preferred_element_type=f32)
            * factor
        )
        return jnp.where(allowed[None, :], scores, -1e30)

    def head_forward(triple):
        query_head, key_head, value_head = triple
        scores = scores_of(query_head, key_head)
        highest = jnp.max(scores, -1, keepdims=True)
        shifted = jnp.exp(scores - highest)
        summed = jnp.sum(shifted, -1, keepdims=True)
        portion = (shifted / summed).astype(jnp.bfloat16)
        mixed = jnp.dot(portion, value_head, preferred_element_type=f32)
        return (mixed.astype(jnp.bfloat16), (highest + jnp.log(summed))[:, 0])

    query_heads = split_heads(query)
    key_heads = split_heads(keys)
    value_heads = split_heads(values)
    chunk_outs = []
    for c, chunk in enumerate(kv_chunks):
        heads = slice(c * chunk_heads, (c + 1) * chunk_heads)
        chunk_outs.append(
            lax.map(
                head_forward,
                (
                    query_heads[heads],
                    split_heads_of(chunk[:, :chunk_width], chunk_heads),
                    split_heads_of(chunk[:, chunk_width:], chunk_heads),
                ),
            )
        )
    context_heads = jnp.concatenate([o[0] for o in chunk_outs])
    log_sums = jnp.concatenate([o[1] for o in chunk_outs])
    context = join_heads(context_heads)
    attn_part = jnp.einsum("th,oh->to", context, output_full, preferred_element_type=f32)
    attended = tp_sum(attn_part) + outbias_full
    normal_first, inverse_first = norm_parts(tokens.astype(f32) + attended)
    normed = normal_first * gain_first + shift_first
    normed_low = normed.astype(jnp.bfloat16)
    hidden = jnp.dot(normed_low, inner_full, preferred_element_type=f32) + inner_shift
    active = exact_gelu(hidden).astype(jnp.bfloat16)
    branch_part = jnp.einsum("tf,of->to", active, outer_full, preferred_element_type=f32)
    branch = tp_sum(branch_part) + outerbias_full
    normal_second, inverse_second = norm_parts(normed + branch)
    layer_out = (normal_second * gain_second + shift_second).astype(jnp.bfloat16)

    dres_second, final_gain_part, final_shift_part = norm_back(
        upstream.astype(f32), normal_second, inverse_second, gain_second
    )
    dbranch = dres_second.astype(jnp.bfloat16)
    outer_bias_part = jnp.sum(dbranch.astype(f32), 0)
    outer_weight_part = jnp.einsum("to,tf->of", dbranch, active, preferred_element_type=f32)
    dactive = jnp.dot(dbranch, outer_full, preferred_element_type=f32)
    unused, gelu_pull = jax.vjp(exact_gelu, hidden)
    dhidden = gelu_pull(dactive)[0].astype(jnp.bfloat16)
    inner_weight_part = jnp.einsum("td,tf->df", normed_low, dhidden, preferred_element_type=f32)
    inner_bias_part = jnp.sum(dhidden.astype(f32), 0)
    dnormed_part = jnp.einsum("tf,df->td", dhidden, inner_full, preferred_element_type=f32)
    dnormed = dres_second + tp_sum(dnormed_part)
    dres_first, attn_gain_part, attn_shift_part = norm_back(
        dnormed, normal_first, inverse_first, gain_first
    )
    dattended = dres_first.astype(jnp.bfloat16)
    output_bias_part = jnp.sum(dattended.astype(f32), 0)
    output_weight_part = jnp.einsum("to,th->oh", dattended, context, preferred_element_type=f32)
    dcontext = jnp.dot(dattended, output_full, preferred_element_type=f32).astype(jnp.bfloat16)

    low = jnp.bfloat16
    rows = model_width
    early = jnp.concatenate(
        [
            output_weight_part,
            inner_weight_part,
            outer_weight_part,
            jnp.stack(
                [output_bias_part, attn_gain_part, attn_shift_part, outer_bias_part,
                 final_gain_part, final_shift_part],
                axis=1,
            ),
            tp_gather(inner_bias_part).reshape(rows, -1),
        ],
        axis=1,
    ).astype(low)
    early_scattered = lax.psum_scatter(early, "shard", scatter_dimension=0, tiled=True)
    local_rows = piece // tensor_count

    def head_backward(quintet):
        query_head, key_head, value_head, dcontext_head, log_sum = quintet
        portion = jnp.exp(scores_of(query_head, key_head) - log_sum[:, None])
        dportion = jnp.einsum("qd,kd->qk", dcontext_head, value_head, preferred_element_type=f32)
        dvalue_head = jnp.einsum(
            "qk,qd->kd", portion.astype(jnp.bfloat16), dcontext_head, preferred_element_type=f32
        )
        centering = jnp.sum(portion * dportion, -1, keepdims=True)
        dscores = (portion * (dportion - centering)).astype(jnp.bfloat16)
        dquery_head = jnp.dot(dscores, key_head, preferred_element_type=f32) * factor
        dkey_head = (
            jnp.einsum("qk,qd->kd", dscores, query_head, preferred_element_type=f32) * factor
        )
        return (dquery_head.astype(jnp.bfloat16), dkey_head, dvalue_head)

    dquery_heads, dkey_heads, dvalue_heads = lax.map(
        head_backward, (query_heads, key_heads, value_heads, split_heads(dcontext), log_sums)
    )
    dquery = join_heads(dquery_heads)
    dkv_partial = jnp.concatenate(
        [join_heads(dkey_heads), join_heads(dvalue_heads)], axis=1
    ).astype(low)
    dkv_partial, early_scattered = lax.optimization_barrier((dkv_partial, early_scattered))
    dkv = lax.psum_scatter(dkv_partial, "ctx", scatter_dimension=0, tiled=True).astype(
        jnp.bfloat16
    )
    early_piece = lax.psum(early_scattered, "ctx").astype(f32)
    output_total = early_piece[:, :head_width]
    inner_total = early_piece[:, head_width : head_width + hidden_width]
    outer_total = early_piece[:, head_width + hidden_width : head_width + 2 * hidden_width]
    early_vectors = early_piece[:, head_width + 2 * hidden_width :]
    outbias_total, attn_gain_total, attn_shift_total, outerbias_total, final_gain_total, final_shift_total = (
        early_vectors[:, :6].T
    )
    ibias_total = lax.dynamic_slice_in_dim(
        early_vectors[:, 6:], tensor_place * local_rows, local_rows, 0
    ).reshape(-1)
    dkeys = dkv[:, :head_width]
    dvalues = dkv[:, head_width:]
    dqkv = jnp.concatenate([dquery, dkeys, dvalues], axis=1)
    qkv_weight_part = jnp.einsum("td,th->dh", tokens, dqkv, preferred_element_type=f32)
    query_bias_part = jnp.sum(dquery.astype(f32), 0)
    value_bias_part = jnp.sum(dvalues.astype(f32), 0)
    dinput_part = jnp.einsum("th,dh->td", dqkv, qkv_full, preferred_element_type=f32)
    tokens_gradient = dres_first + tp_sum(dinput_part)
    late = jnp.concatenate(
        [
            qkv_weight_part,
            tp_gather(query_bias_part).reshape(rows, 1),
            tp_gather(value_bias_part).reshape(rows, 1),
        ],
        axis=1,
    ).astype(low)
    late_piece = lax.psum(
        lax.psum_scatter(late, "shard", scatter_dimension=0, tiled=True), "ctx"
    ).astype(f32)
    query_total = late_piece[:, :head_width]
    key_total = late_piece[:, head_width : 2 * head_width]
    value_total = late_piece[:, 2 * head_width : 3 * head_width]
    qbias_total = lax.dynamic_slice_in_dim(
        late_piece[:, 3 * head_width], tensor_place * local_rows, local_rows
    )
    vbias_total = lax.dynamic_slice_in_dim(
        late_piece[:, 3 * head_width + 1], tensor_place * local_rows, local_rows
    )
    return (
        layer_out,
        tokens_gradient,
        query_total,
        qbias_total,
        key_total,
        value_total,
        vbias_total,
        output_total,
        outbias_total,
        attn_gain_total,
        attn_shift_total,
        inner_total,
        ibias_total,
        outer_total,
        outerbias_total,
        final_gain_total,
        final_shift_total,
    )


def solution(mesh):
    placed = (
        P(("shard", "ctx"), None),
        P("shard"),
        P("shard", "tp"),
        P(("shard", "tp")),
        P("shard", "tp"),
        P("shard", "tp"),
        P(("shard", "tp")),
        P("shard", "tp"),
        P("shard"),
        P("shard"),
        P("shard"),
        P("shard", "tp"),
        P(("shard", "tp")),
        P("shard", "tp"),
        P("shard"),
        P("shard"),
        P("shard"),
        P(("shard", "ctx"), None),
    )
    return jax.shard_map(
        on_device,
        mesh=mesh,
        in_specs=placed,
        out_specs=(
            P(("shard", "ctx"), None),
            P(("shard", "ctx"), None),
            P("shard", "tp"),
            P(("shard", "tp")),
            P("shard", "tp"),
            P("shard", "tp"),
            P(("shard", "tp")),
            P("shard", "tp"),
            P("shard"),
            P("shard"),
            P("shard"),
            P("shard", "tp"),
            P(("shard", "tp")),
            P("shard", "tp"),
            P("shard"),
            P("shard"),
            P("shard"),
        ),
        check_vma=False,
    )
```

```python
import functools

import jax
import jax.numpy as jnp
from jax import lax
from jax.experimental import pallas as pl
from jax.experimental.pallas import tpu as pltpu
from jax.sharding import PartitionSpec as P

HEAD_DIM = 64
QUERY_TILE = 128


def _scores(length_ref, q, k, factor):
    s = lax.dot_general(q, k, (((1,), (1,)), ((), ())), preferred_element_type=jnp.float32) * factor
    keys = lax.broadcasted_iota(jnp.int32, s.shape, 1)
    return jnp.where(keys < length_ref[0], s, -1e30)


def _attend_kernel(length_ref, q_ref, kv_ref, o_ref, lse_ref, *, heads, factor):
    for h in range(heads):
        cols = slice(h * HEAD_DIM, (h + 1) * HEAD_DIM)
        vcols = slice((heads + h) * HEAD_DIM, (heads + h + 1) * HEAD_DIM)
        s = _scores(length_ref, q_ref[:, cols], kv_ref[:, cols], factor)
        highest = jnp.max(s, axis=1, keepdims=True)
        shifted = jnp.exp(s - highest)
        summed = jnp.sum(shifted, axis=1, keepdims=True)
        portion = (shifted / summed).astype(jnp.bfloat16)
        mixed = jnp.dot(portion, kv_ref[:, vcols], preferred_element_type=jnp.float32)
        o_ref[:, cols] = mixed.astype(o_ref.dtype)
        lse_ref[:, h : h + 1] = highest + jnp.log(summed)


def attend(length, q, kv, factor):
    n, width = q.shape
    m = kv.shape[0]
    heads = width // HEAD_DIM
    tq = min(QUERY_TILE, n)
    grid = pltpu.PrefetchScalarGridSpec(
        num_scalar_prefetch=1,
        grid=(n // tq,),
        in_specs=[
            pl.BlockSpec((tq, width), lambda i, length: (i, 0)),
            pl.BlockSpec((m, 2 * width), lambda i, length: (0, 0)),
        ],
        out_specs=[
            pl.BlockSpec((tq, width), lambda i, length: (i, 0)),
            pl.BlockSpec((tq, heads), lambda i, length: (i, 0)),
        ],
    )
    flops = 4 * n * m * width
    return pl.pallas_call(
        functools.partial(_attend_kernel, heads=heads, factor=factor),
        grid_spec=grid,
        out_shape=(
            jax.ShapeDtypeStruct((n, width), jnp.bfloat16),
            jax.ShapeDtypeStruct((n, heads), jnp.float32),
        ),
        compiler_params=pltpu.CompilerParams(dimension_semantics=("arbitrary",)),
        cost_estimate=pl.CostEstimate(
            flops=flops, transcendentals=n * m * heads, bytes_accessed=2 * (2 * n * width + 2 * m * width)
        ),
    )(length, q, kv)


def _attend_back_kernel(length_ref, q_ref, kv_ref, do_ref, lse_ref, dq_ref, dkv_ref, *, heads, factor):
    @pl.when(pl.program_id(0) == 0)
    def _():
        dkv_ref[...] = jnp.zeros_like(dkv_ref)

    for h in range(heads):
        cols = slice(h * HEAD_DIM, (h + 1) * HEAD_DIM)
        vcols = slice((heads + h) * HEAD_DIM, (heads + h + 1) * HEAD_DIM)
        q = q_ref[:, cols]
        k = kv_ref[:, cols]
        v = kv_ref[:, vcols]
        do = do_ref[:, cols]
        portion = jnp.exp(_scores(length_ref, q, k, factor) - lse_ref[:, h : h + 1])
        dportion = lax.dot_general(do, v, (((1,), (1,)), ((), ())), preferred_element_type=jnp.float32)
        dkv_ref[:, vcols] += lax.dot_general(
            portion.astype(jnp.bfloat16), do, (((0,), (0,)), ((), ())), preferred_element_type=jnp.float32
        )
        centering = jnp.sum(portion * dportion, axis=1, keepdims=True)
        dscores = (portion * (dportion - centering)).astype(jnp.bfloat16)
        dq_ref[:, cols] = (
            jnp.dot(dscores, k, preferred_element_type=jnp.float32) * factor
        ).astype(dq_ref.dtype)
        dkv_ref[:, cols] += (
            lax.dot_general(dscores, q, (((0,), (0,)), ((), ())), preferred_element_type=jnp.float32) * factor
        )


def attend_back(length, q, kv, do, lse, factor):
    n, width = q.shape
    m = kv.shape[0]
    heads = width // HEAD_DIM
    tq = min(QUERY_TILE, n)
    grid = pltpu.PrefetchScalarGridSpec(
        num_scalar_prefetch=1,
        grid=(n // tq,),
        in_specs=[
            pl.BlockSpec((tq, width), lambda i, length: (i, 0)),
            pl.BlockSpec((m, 2 * width), lambda i, length: (0, 0)),
            pl.BlockSpec((tq, width), lambda i, length: (i, 0)),
            pl.BlockSpec((tq, heads), lambda i, length: (i, 0)),
        ],
        out_specs=[
            pl.BlockSpec((tq, width), lambda i, length: (i, 0)),
            pl.BlockSpec((m, 2 * width), lambda i, length: (0, 0)),
        ],
    )
    flops = 10 * n * m * width
    return pl.pallas_call(
        functools.partial(_attend_back_kernel, heads=heads, factor=factor),
        grid_spec=grid,
        out_shape=(
            jax.ShapeDtypeStruct((n, width), jnp.bfloat16),
            jax.ShapeDtypeStruct((m, 2 * width), jnp.float32),
        ),
        compiler_params=pltpu.CompilerParams(dimension_semantics=("arbitrary",)),
        cost_estimate=pl.CostEstimate(
            flops=flops, transcendentals=n * m * heads,
            bytes_accessed=2 * (3 * n * width + 2 * m * width) + 4 * 2 * m * width,
        ),
    )(length, q, kv, do, lse)


EPSILON = 1e-12


def norm_parts(hidden):
    center = hidden - jnp.mean(hidden, -1, keepdims=True)
    inverse = lax.rsqrt(jnp.mean(center * center, -1, keepdims=True) + EPSILON)
    return (center * inverse, inverse)


def norm_back(gradient, normal_form, inverse, gain):
    scaled = gradient * gain
    inner = (
        scaled
        - jnp.mean(scaled, -1, keepdims=True)
        - normal_form * jnp.mean(scaled * normal_form, -1, keepdims=True)
    )
    return (inner * inverse, jnp.sum(gradient * normal_form, 0), jnp.sum(gradient, 0))


def exact_gelu(values):
    return jax.nn.gelu(values, approximate=False)


def tp_sum(value):
    if lax.axis_size("tp") == 2:
        return value + lax.ppermute(value, "tp", [(0, 1), (1, 0)])
    return lax.psum(value, "tp")


def tp_gather(value):
    if lax.axis_size("tp") == 2:
        other = lax.ppermute(value, "tp", [(0, 1), (1, 0)])
        first = lax.axis_index("tp") == 0
        return jnp.stack([jnp.where(first, value, other), jnp.where(first, other, value)])
    return lax.all_gather(value, "tp")


def on_device(
    tokens,
    seq_lengths,
    query_weight,
    query_bias,
    key_weight,
    value_weight,
    value_bias,
    output_weight,
    output_bias,
    attn_gain,
    attn_shift,
    inner_weight,
    inner_bias,
    outer_weight,
    outer_bias,
    final_gain,
    final_shift,
    upstream,
):
    row_count, model_width = tokens.shape
    tensor_place = lax.axis_index("tp")
    tensor_count = lax.axis_size("tp")
    head_width = query_weight.shape[1]
    hidden_width = inner_weight.shape[1]
    head_count = head_width // HEAD_DIM
    factor = HEAD_DIM ** (-0.5)
    f32 = jnp.float32

    qb = query_bias.shape[0]
    ib = inner_bias.shape[0]
    piece = output_bias.shape[0]
    tp_blocks = tp_gather(jnp.concatenate([query_bias, value_bias, inner_bias]))
    bias_columns = jnp.concatenate(
        [
            tp_blocks[:, :qb].reshape(piece, 1),
            tp_blocks[:, qb : 2 * qb].reshape(piece, 1),
            tp_blocks[:, 2 * qb :].reshape(piece, -1),
        ],
        axis=1,
    )
    shard_columns = jnp.stack(
        [output_bias, attn_gain, attn_shift, outer_bias, final_gain, final_shift], axis=1
    )
    kv_vec_full = lax.all_gather(
        jnp.concatenate([key_weight, value_weight, shard_columns, bias_columns], axis=1),
        "shard", axis=0, tiled=True,
    )
    query_full = lax.all_gather(query_weight, "shard", axis=0, tiled=True)
    vector_full = kv_vec_full[:, 2 * head_width :]
    key_full = kv_vec_full[:, :head_width]
    value_full = kv_vec_full[:, head_width : 2 * head_width]
    qkv_full = jnp.concatenate([query_full, kv_vec_full[:, : 2 * head_width]], axis=1)
    rest_full = lax.all_gather(
        jnp.concatenate([output_weight, inner_weight, outer_weight], axis=1),
        "shard", axis=0, tiled=True,
    )
    output_full = rest_full[:, :head_width]
    inner_full = rest_full[:, head_width : head_width + hidden_width]
    outer_full = rest_full[:, head_width + hidden_width :]

    full_vectors = vector_full[:, :6].T.astype(f32)
    outbias_full, gain_first, shift_first, outerbias_full, gain_second, shift_second = full_vectors
    qbias_all = vector_full[:, 6]
    vbias_all = vector_full[:, 7]
    ibias_all = vector_full[:, 8:].reshape(-1)
    query_shift = lax.dynamic_slice_in_dim(qbias_all, tensor_place * head_width, head_width).astype(f32)
    value_shift = lax.dynamic_slice_in_dim(vbias_all, tensor_place * head_width, head_width).astype(f32)
    inner_shift = lax.dynamic_slice_in_dim(ibias_all, tensor_place * hidden_width, hidden_width).astype(f32)

    projected = jnp.dot(tokens, kv_vec_full[:, : 2 * head_width], preferred_element_type=f32)
    key_local = projected[:, :head_width].astype(jnp.bfloat16)
    value_local = (projected[:, head_width:] + value_shift).astype(jnp.bfloat16)
    query = (jnp.dot(tokens, query_full, preferred_element_type=f32) + query_shift).astype(
        jnp.bfloat16
    )
    chunk_heads = 2 if head_count % 2 == 0 else 1
    chunk_width = chunk_heads * HEAD_DIM
    kv_chunks = []
    for c in range(head_count // chunk_heads):
        columns = slice(c * chunk_width, (c + 1) * chunk_width)
        outgoing = jnp.concatenate([key_local[:, columns], value_local[:, columns]], axis=1)
        kv_chunks.append(lax.all_gather(outgoing, "ctx", axis=0, tiled=True))
    chunk_outs = [
        attend(seq_lengths, query[:, c * chunk_width : (c + 1) * chunk_width], chunk, factor)
        for c, chunk in enumerate(kv_chunks)
    ]
    context = jnp.concatenate([o[0] for o in chunk_outs], axis=1)
    attn_part = jnp.einsum("th,oh->to", context, output_full, preferred_element_type=f32)
    attended = tp_sum(attn_part) + outbias_full
    normal_first, inverse_first = norm_parts(tokens.astype(f32) + attended)
    normed = normal_first * gain_first + shift_first
    normed_low = normed.astype(jnp.bfloat16)
    hidden = jnp.dot(normed_low, inner_full, preferred_element_type=f32) + inner_shift
    active = exact_gelu(hidden).astype(jnp.bfloat16)
    branch_part = jnp.einsum("tf,of->to", active, outer_full, preferred_element_type=f32)
    branch = tp_sum(branch_part) + outerbias_full
    normal_second, inverse_second = norm_parts(normed + branch)
    layer_out = (normal_second * gain_second + shift_second).astype(jnp.bfloat16)

    dres_second, final_gain_part, final_shift_part = norm_back(
        upstream.astype(f32), normal_second, inverse_second, gain_second
    )
    dbranch = dres_second.astype(jnp.bfloat16)
    outer_bias_part = jnp.sum(dbranch.astype(f32), 0)
    outer_weight_part = jnp.einsum("to,tf->of", dbranch, active, preferred_element_type=f32)
    dactive = jnp.dot(dbranch, outer_full, preferred_element_type=f32)
    unused, gelu_pull = jax.vjp(exact_gelu, hidden)
    dhidden = gelu_pull(dactive)[0].astype(jnp.bfloat16)
    inner_weight_part = jnp.einsum("td,tf->df", normed_low, dhidden, preferred_element_type=f32)
    inner_bias_part = jnp.sum(dhidden.astype(f32), 0)
    dnormed_part = jnp.einsum("tf,df->td", dhidden, inner_full, preferred_element_type=f32)
    dnormed = dres_second + tp_sum(dnormed_part)
    dres_first, attn_gain_part, attn_shift_part = norm_back(
        dnormed, normal_first, inverse_first, gain_first
    )
    dattended = dres_first.astype(jnp.bfloat16)
    output_bias_part = jnp.sum(dattended.astype(f32), 0)
    output_weight_part = jnp.einsum("to,th->oh", dattended, context, preferred_element_type=f32)
    dcontext = jnp.dot(dattended, output_full, preferred_element_type=f32).astype(jnp.bfloat16)

    low = jnp.bfloat16
    rows = model_width
    early = jnp.concatenate(
        [
            output_weight_part,
            inner_weight_part,
            outer_weight_part,
            jnp.stack(
                [output_bias_part, attn_gain_part, attn_shift_part, outer_bias_part,
                 final_gain_part, final_shift_part],
                axis=1,
            ),
            tp_gather(inner_bias_part).reshape(rows, -1),
        ],
        axis=1,
    ).astype(low)
    early_scattered = lax.psum_scatter(early, "shard", scatter_dimension=0, tiled=True)
    local_rows = piece // tensor_count

    chunk_backs = [
        attend_back(
            seq_lengths,
            query[:, c * chunk_width : (c + 1) * chunk_width],
            chunk,
            dcontext[:, c * chunk_width : (c + 1) * chunk_width],
            chunk_outs[c][1],
            factor,
        )
        for c, chunk in enumerate(kv_chunks)
    ]
    dquery = jnp.concatenate([back[0] for back in chunk_backs], axis=1)
    dkv_partial = jnp.concatenate([back[1] for back in chunk_backs], axis=1).astype(low)
    dkv_partial, early_scattered = lax.optimization_barrier((dkv_partial, early_scattered))
    dkv = lax.psum_scatter(dkv_partial, "ctx", scatter_dimension=0, tiled=True).astype(
        jnp.bfloat16
    )
    early_piece = lax.psum(early_scattered, "ctx").astype(f32)
    output_total = early_piece[:, :head_width]
    inner_total = early_piece[:, head_width : head_width + hidden_width]
    outer_total = early_piece[:, head_width + hidden_width : head_width + 2 * hidden_width]
    early_vectors = early_piece[:, head_width + 2 * hidden_width :]
    outbias_total, attn_gain_total, attn_shift_total, outerbias_total, final_gain_total, final_shift_total = (
        early_vectors[:, :6].T
    )
    ibias_total = lax.dynamic_slice_in_dim(
        early_vectors[:, 6:], tensor_place * local_rows, local_rows, 0
    ).reshape(-1)
    dkeys = jnp.concatenate(
        [dkv[:, 2 * c * chunk_width : (2 * c + 1) * chunk_width] for c in range(len(kv_chunks))],
        axis=1,
    )
    dvalues = jnp.concatenate(
        [dkv[:, (2 * c + 1) * chunk_width : (2 * c + 2) * chunk_width] for c in range(len(kv_chunks))],
        axis=1,
    )
    dqkv = jnp.concatenate([dquery, dkeys, dvalues], axis=1)
    qkv_weight_part = jnp.einsum("td,th->dh", tokens, dqkv, preferred_element_type=f32)
    query_bias_part = jnp.sum(dquery.astype(f32), 0)
    value_bias_part = jnp.sum(dvalues.astype(f32), 0)
    dinput_part = jnp.einsum("th,dh->td", dqkv, qkv_full, preferred_element_type=f32)
    tokens_gradient = dres_first + tp_sum(dinput_part)
    late = jnp.concatenate(
        [
            qkv_weight_part,
            tp_gather(query_bias_part).reshape(rows, 1),
            tp_gather(value_bias_part).reshape(rows, 1),
        ],
        axis=1,
    ).astype(low)
    late_piece = lax.psum(
        lax.psum_scatter(late, "shard", scatter_dimension=0, tiled=True), "ctx"
    ).astype(f32)
    query_total = late_piece[:, :head_width]
    key_total = late_piece[:, head_width : 2 * head_width]
    value_total = late_piece[:, 2 * head_width : 3 * head_width]
    qbias_total = lax.dynamic_slice_in_dim(
        late_piece[:, 3 * head_width], tensor_place * local_rows, local_rows
    )
    vbias_total = lax.dynamic_slice_in_dim(
        late_piece[:, 3 * head_width + 1], tensor_place * local_rows, local_rows
    )
    return (
        layer_out,
        tokens_gradient,
        query_total,
        qbias_total,
        key_total,
        value_total,
        vbias_total,
        output_total,
        outbias_total,
        attn_gain_total,
        attn_shift_total,
        inner_total,
        ibias_total,
        outer_total,
        outerbias_total,
        final_gain_total,
        final_shift_total,
    )


def solution(mesh):
    placed = (
        P(("shard", "ctx"), None),
        P("shard"),
        P("shard", "tp"),
        P(("shard", "tp")),
        P("shard", "tp"),
        P("shard", "tp"),
        P(("shard", "tp")),
        P("shard", "tp"),
        P("shard"),
        P("shard"),
        P("shard"),
        P("shard", "tp"),
        P(("shard", "tp")),
        P("shard", "tp"),
        P("shard"),
        P("shard"),
        P("shard"),
        P(("shard", "ctx"), None),
    )
    return jax.shard_map(
        on_device,
        mesh=mesh,
        in_specs=placed,
        out_specs=(
            P(("shard", "ctx"), None),
            P(("shard", "ctx"), None),
            P("shard", "tp"),
            P(("shard", "tp")),
            P("shard", "tp"),
            P("shard", "tp"),
            P(("shard", "tp")),
            P("shard", "tp"),
            P("shard"),
            P("shard"),
            P("shard"),
            P("shard", "tp"),
            P(("shard", "tp")),
            P("shard", "tp"),
            P("shard"),
            P("shard"),
            P("shard"),
        ),
        check_vma=False,
    )
```

```python
import functools

import jax
import jax.numpy as jnp
from jax import lax
from jax.experimental import pallas as pl
from jax.experimental.pallas import tpu as pltpu
from jax.sharding import PartitionSpec as P

HEAD_DIM = 64
QUERY_TILE = 128


def _scores(length_ref, q, k, factor):
    s = lax.dot_general(q, k, (((1,), (1,)), ((), ())), preferred_element_type=jnp.float32) * factor
    keys = lax.broadcasted_iota(jnp.int32, s.shape, 1)
    return jnp.where(keys < length_ref[0], s, -1e30)


def _attend_kernel(length_ref, q_ref, kv_ref, o_ref, lse_ref, *, heads, factor):
    for h in range(heads):
        cols = slice(h * HEAD_DIM, (h + 1) * HEAD_DIM)
        vcols = slice((heads + h) * HEAD_DIM, (heads + h + 1) * HEAD_DIM)
        s = _scores(length_ref, q_ref[:, cols], kv_ref[:, cols], factor)
        highest = jnp.max(s, axis=1, keepdims=True)
        shifted = jnp.exp(s - highest)
        summed = jnp.sum(shifted, axis=1, keepdims=True)
        portion = (shifted / summed).astype(jnp.bfloat16)
        mixed = jnp.dot(portion, kv_ref[:, vcols], preferred_element_type=jnp.float32)
        o_ref[:, cols] = mixed.astype(o_ref.dtype)
        lse_ref[:, h : h + 1] = highest + jnp.log(summed)


def attend(length, q, kv, factor):
    n, width = q.shape
    m = kv.shape[0]
    heads = width // HEAD_DIM
    tq = min(QUERY_TILE, n)
    grid = pltpu.PrefetchScalarGridSpec(
        num_scalar_prefetch=1,
        grid=(n // tq,),
        in_specs=[
            pl.BlockSpec((tq, width), lambda i, length: (i, 0)),
            pl.BlockSpec((m, 2 * width), lambda i, length: (0, 0)),
        ],
        out_specs=[
            pl.BlockSpec((tq, width), lambda i, length: (i, 0)),
            pl.BlockSpec((tq, heads), lambda i, length: (i, 0)),
        ],
    )
    flops = 4 * n * m * width
    return pl.pallas_call(
        functools.partial(_attend_kernel, heads=heads, factor=factor),
        grid_spec=grid,
        out_shape=(
            jax.ShapeDtypeStruct((n, width), jnp.bfloat16),
            jax.ShapeDtypeStruct((n, heads), jnp.float32),
        ),
        compiler_params=pltpu.CompilerParams(dimension_semantics=("arbitrary",)),
        cost_estimate=pl.CostEstimate(
            flops=flops, transcendentals=n * m * heads, bytes_accessed=2 * (2 * n * width + 2 * m * width)
        ),
    )(length, q, kv)


def _attend_back_kernel(length_ref, q_ref, kv_ref, do_ref, lse_ref, dq_ref, dkv_ref, *, heads, factor):
    @pl.when(pl.program_id(0) == 0)
    def _():
        dkv_ref[...] = jnp.zeros_like(dkv_ref)

    for h in range(heads):
        cols = slice(h * HEAD_DIM, (h + 1) * HEAD_DIM)
        vcols = slice((heads + h) * HEAD_DIM, (heads + h + 1) * HEAD_DIM)
        q = q_ref[:, cols]
        k = kv_ref[:, cols]
        v = kv_ref[:, vcols]
        do = do_ref[:, cols]
        portion = jnp.exp(_scores(length_ref, q, k, factor) - lse_ref[:, h : h + 1])
        dportion = lax.dot_general(do, v, (((1,), (1,)), ((), ())), preferred_element_type=jnp.float32)
        dkv_ref[:, vcols] += lax.dot_general(
            portion.astype(jnp.bfloat16), do, (((0,), (0,)), ((), ())), preferred_element_type=jnp.float32
        )
        centering = jnp.sum(portion * dportion, axis=1, keepdims=True)
        dscores = (portion * (dportion - centering)).astype(jnp.bfloat16)
        dq_ref[:, cols] = (
            jnp.dot(dscores, k, preferred_element_type=jnp.float32) * factor
        ).astype(dq_ref.dtype)
        dkv_ref[:, cols] += (
            lax.dot_general(dscores, q, (((0,), (0,)), ((), ())), preferred_element_type=jnp.float32) * factor
        )


def attend_back(length, q, kv, do, lse, factor):
    n, width = q.shape
    m = kv.shape[0]
    heads = width // HEAD_DIM
    tq = min(QUERY_TILE, n)
    grid = pltpu.PrefetchScalarGridSpec(
        num_scalar_prefetch=1,
        grid=(n // tq,),
        in_specs=[
            pl.BlockSpec((tq, width), lambda i, length: (i, 0)),
            pl.BlockSpec((m, 2 * width), lambda i, length: (0, 0)),
            pl.BlockSpec((tq, width), lambda i, length: (i, 0)),
            pl.BlockSpec((tq, heads), lambda i, length: (i, 0)),
        ],
        out_specs=[
            pl.BlockSpec((tq, width), lambda i, length: (i, 0)),
            pl.BlockSpec((m, 2 * width), lambda i, length: (0, 0)),
        ],
    )
    flops = 10 * n * m * width
    return pl.pallas_call(
        functools.partial(_attend_back_kernel, heads=heads, factor=factor),
        grid_spec=grid,
        out_shape=(
            jax.ShapeDtypeStruct((n, width), jnp.bfloat16),
            jax.ShapeDtypeStruct((m, 2 * width), jnp.float32),
        ),
        compiler_params=pltpu.CompilerParams(dimension_semantics=("arbitrary",)),
        cost_estimate=pl.CostEstimate(
            flops=flops, transcendentals=n * m * heads,
            bytes_accessed=2 * (3 * n * width + 2 * m * width) + 4 * 2 * m * width,
        ),
    )(length, q, kv, do, lse)


EPSILON = 1e-12


def norm_parts(hidden):
    center = hidden - jnp.mean(hidden, -1, keepdims=True)
    inverse = lax.rsqrt(jnp.mean(center * center, -1, keepdims=True) + EPSILON)
    return (center * inverse, inverse)


def norm_back(gradient, normal_form, inverse, gain):
    scaled = gradient * gain
    inner = (
        scaled
        - jnp.mean(scaled, -1, keepdims=True)
        - normal_form * jnp.mean(scaled * normal_form, -1, keepdims=True)
    )
    return (inner * inverse, jnp.sum(gradient * normal_form, 0), jnp.sum(gradient, 0))


def exact_gelu(values):
    return jax.nn.gelu(values, approximate=False)


def tp_sum(value):
    if lax.axis_size("tp") == 2:
        return value + lax.ppermute(value, "tp", [(0, 1), (1, 0)])
    return lax.psum(value, "tp")


def tp_gather(value):
    if lax.axis_size("tp") == 2:
        other = lax.ppermute(value, "tp", [(0, 1), (1, 0)])
        first = lax.axis_index("tp") == 0
        return jnp.stack([jnp.where(first, value, other), jnp.where(first, other, value)])
    return lax.all_gather(value, "tp")


def shard_send(value, axis="shard"):
    count = lax.axis_size(axis)
    if count > 8:
        return [lax.all_gather(value, axis, axis=0, tiled=True)]
    return [
        lax.ppermute(value, axis, [(j, (j + shift) % count) for j in range(count)])
        for shift in range(1, count)
    ]


def shard_assemble(value, arrived, axis="shard"):
    count = lax.axis_size(axis)
    if count > 8:
        return arrived[0]
    place = lax.axis_index(axis)
    rows = value.shape[0]
    out = jnp.zeros((count * rows,) + value.shape[1:], value.dtype)
    out = lax.dynamic_update_slice_in_dim(out, value, place * rows, 0)
    for shift, piece in enumerate(arrived, start=1):
        out = lax.dynamic_update_slice_in_dim(out, piece, ((place - shift) % count) * rows, 0)
    return out


def shard_gather(value, axis="shard"):
    return shard_assemble(value, shard_send(value, axis), axis)


def shard_scatter(value, axis="shard"):
    count = lax.axis_size(axis)
    if count > 8:
        return lax.psum_scatter(value, axis, scatter_dimension=0, tiled=True).astype(jnp.float32)
    place = lax.axis_index(axis)
    rows = value.shape[0] // count
    total = lax.dynamic_slice_in_dim(value, place * rows, rows, 0).astype(jnp.float32)
    for shift in range(1, count):
        outgoing = lax.dynamic_slice_in_dim(value, ((place + shift) % count) * rows, rows, 0)
        arrived = lax.ppermute(outgoing, axis, [(j, (j + shift) % count) for j in range(count)])
        total = total + arrived.astype(jnp.float32)
    return total


def on_device(
    tokens,
    seq_lengths,
    query_weight,
    query_bias,
    key_weight,
    value_weight,
    value_bias,
    output_weight,
    output_bias,
    attn_gain,
    attn_shift,
    inner_weight,
    inner_bias,
    outer_weight,
    outer_bias,
    final_gain,
    final_shift,
    upstream,
):
    row_count, model_width = tokens.shape
    tensor_place = lax.axis_index("tp")
    tensor_count = lax.axis_size("tp")
    head_width = query_weight.shape[1]
    hidden_width = inner_weight.shape[1]
    head_count = head_width // HEAD_DIM
    factor = HEAD_DIM ** (-0.5)
    f32 = jnp.float32

    qb = query_bias.shape[0]
    ib = inner_bias.shape[0]
    piece = output_bias.shape[0]
    tp_blocks = tp_gather(jnp.concatenate([query_bias, value_bias, inner_bias]))
    bias_columns = jnp.concatenate(
        [
            tp_blocks[:, :qb].reshape(piece, 1),
            tp_blocks[:, qb : 2 * qb].reshape(piece, 1),
            tp_blocks[:, 2 * qb :].reshape(piece, -1),
        ],
        axis=1,
    )
    shard_columns = jnp.stack(
        [output_bias, attn_gain, attn_shift, outer_bias, final_gain, final_shift], axis=1
    )
    kv_vec_full = lax.all_gather(
        jnp.concatenate([key_weight, value_weight, shard_columns, bias_columns], axis=1),
        "shard", axis=0, tiled=True,
    )
    query_full = shard_gather(query_weight)
    vector_full = kv_vec_full[:, 2 * head_width :]
    key_full = kv_vec_full[:, :head_width]
    value_full = kv_vec_full[:, head_width : 2 * head_width]
    qkv_full = jnp.concatenate([query_full, kv_vec_full[:, : 2 * head_width]], axis=1)
    rest_local = jnp.concatenate([output_weight, inner_weight, outer_weight], axis=1)
    rest_arrived = shard_send(rest_local)

    full_vectors = vector_full[:, :6].T.astype(f32)
    outbias_full, gain_first, shift_first, outerbias_full, gain_second, shift_second = full_vectors
    qbias_all = vector_full[:, 6]
    vbias_all = vector_full[:, 7]
    ibias_all = vector_full[:, 8:].reshape(-1)
    query_shift = lax.dynamic_slice_in_dim(qbias_all, tensor_place * head_width, head_width).astype(f32)
    value_shift = lax.dynamic_slice_in_dim(vbias_all, tensor_place * head_width, head_width).astype(f32)
    inner_shift = lax.dynamic_slice_in_dim(ibias_all, tensor_place * hidden_width, hidden_width).astype(f32)

    projected = jnp.dot(tokens, kv_vec_full[:, : 2 * head_width], preferred_element_type=f32)
    key_local = projected[:, :head_width].astype(jnp.bfloat16)
    value_local = (projected[:, head_width:] + value_shift).astype(jnp.bfloat16)
    query = (jnp.dot(tokens, query_full, preferred_element_type=f32) + query_shift).astype(
        jnp.bfloat16
    )
    chunk_heads = 2 if head_count % 2 == 0 else 1
    chunk_width = chunk_heads * HEAD_DIM
    kv_chunks = []
    for c in range(head_count // chunk_heads):
        columns = slice(c * chunk_width, (c + 1) * chunk_width)
        outgoing = jnp.concatenate([key_local[:, columns], value_local[:, columns]], axis=1)
        kv_chunks.append(lax.all_gather(outgoing, "ctx", axis=0, tiled=True))
    chunk_outs = [
        attend(seq_lengths, query[:, c * chunk_width : (c + 1) * chunk_width], chunk, factor)
        for c, chunk in enumerate(kv_chunks)
    ]
    context = jnp.concatenate([o[0] for o in chunk_outs], axis=1)
    rest_arrived, context = lax.optimization_barrier((rest_arrived, context))
    rest_full = shard_assemble(rest_local, rest_arrived)
    output_full = rest_full[:, :head_width]
    inner_full = rest_full[:, head_width : head_width + hidden_width]
    outer_full = rest_full[:, head_width + hidden_width :]
    attn_part = jnp.einsum("th,oh->to", context, output_full, preferred_element_type=f32)
    attended = tp_sum(attn_part) + outbias_full
    normal_first, inverse_first = norm_parts(tokens.astype(f32) + attended)
    normed = normal_first * gain_first + shift_first
    normed_low = normed.astype(jnp.bfloat16)
    hidden = jnp.dot(normed_low, inner_full, preferred_element_type=f32) + inner_shift
    active = exact_gelu(hidden).astype(jnp.bfloat16)
    branch_part = jnp.einsum("tf,of->to", active, outer_full, preferred_element_type=f32)
    branch = tp_sum(branch_part) + outerbias_full
    normal_second, inverse_second = norm_parts(normed + branch)
    layer_out = (normal_second * gain_second + shift_second).astype(jnp.bfloat16)

    dres_second, final_gain_part, final_shift_part = norm_back(
        upstream.astype(f32), normal_second, inverse_second, gain_second
    )
    dbranch = dres_second.astype(jnp.bfloat16)
    outer_bias_part = jnp.sum(dbranch.astype(f32), 0)
    outer_weight_part = jnp.einsum("to,tf->of", dbranch, active, preferred_element_type=f32)
    dactive = jnp.dot(dbranch, outer_full, preferred_element_type=f32)
    unused, gelu_pull = jax.vjp(exact_gelu, hidden)
    dhidden = gelu_pull(dactive)[0].astype(jnp.bfloat16)
    inner_weight_part = jnp.einsum("td,tf->df", normed_low, dhidden, preferred_element_type=f32)
    inner_bias_part = jnp.sum(dhidden.astype(f32), 0)
    dnormed_part = jnp.einsum("tf,df->td", dhidden, inner_full, preferred_element_type=f32)
    dnormed = dres_second + tp_sum(dnormed_part)
    dres_first, attn_gain_part, attn_shift_part = norm_back(
        dnormed, normal_first, inverse_first, gain_first
    )
    dattended = dres_first.astype(jnp.bfloat16)
    output_bias_part = jnp.sum(dattended.astype(f32), 0)
    output_weight_part = jnp.einsum("to,th->oh", dattended, context, preferred_element_type=f32)
    dcontext = jnp.dot(dattended, output_full, preferred_element_type=f32).astype(jnp.bfloat16)

    low = jnp.bfloat16
    rows = model_width
    early = jnp.concatenate(
        [
            output_weight_part,
            inner_weight_part,
            outer_weight_part,
            jnp.stack(
                [output_bias_part, attn_gain_part, attn_shift_part, outer_bias_part,
                 final_gain_part, final_shift_part],
                axis=1,
            ),
            tp_gather(inner_bias_part).reshape(rows, -1),
        ],
        axis=1,
    ).astype(low)
    early_scattered = shard_scatter(early).astype(low)
    local_rows = piece // tensor_count

    chunk_backs = [
        attend_back(
            seq_lengths,
            query[:, c * chunk_width : (c + 1) * chunk_width],
            chunk,
            dcontext[:, c * chunk_width : (c + 1) * chunk_width],
            chunk_outs[c][1],
            factor,
        )
        for c, chunk in enumerate(kv_chunks)
    ]
    dquery = jnp.concatenate([back[0] for back in chunk_backs], axis=1)
    dkv_partial = jnp.concatenate([back[1] for back in chunk_backs], axis=1).astype(low)
    dkv_partial, early_scattered = lax.optimization_barrier((dkv_partial, early_scattered))
    dkv = lax.psum_scatter(dkv_partial, "ctx", scatter_dimension=0, tiled=True).astype(
        jnp.bfloat16
    )
    early_piece = lax.psum(early_scattered, "ctx").astype(f32)
    output_total = early_piece[:, :head_width]
    inner_total = early_piece[:, head_width : head_width + hidden_width]
    outer_total = early_piece[:, head_width + hidden_width : head_width + 2 * hidden_width]
    early_vectors = early_piece[:, head_width + 2 * hidden_width :]
    outbias_total, attn_gain_total, attn_shift_total, outerbias_total, final_gain_total, final_shift_total = (
        early_vectors[:, :6].T
    )
    ibias_total = lax.dynamic_slice_in_dim(
        early_vectors[:, 6:], tensor_place * local_rows, local_rows, 0
    ).reshape(-1)
    dkeys = jnp.concatenate(
        [dkv[:, 2 * c * chunk_width : (2 * c + 1) * chunk_width] for c in range(len(kv_chunks))],
        axis=1,
    )
    dvalues = jnp.concatenate(
        [dkv[:, (2 * c + 1) * chunk_width : (2 * c + 2) * chunk_width] for c in range(len(kv_chunks))],
        axis=1,
    )
    dqkv = jnp.concatenate([dquery, dkeys, dvalues], axis=1)
    qkv_weight_part = jnp.einsum("td,th->dh", tokens, dqkv, preferred_element_type=f32)
    query_bias_part = jnp.sum(dquery.astype(f32), 0)
    value_bias_part = jnp.sum(dvalues.astype(f32), 0)
    dinput_part = jnp.einsum("th,dh->td", dqkv, qkv_full, preferred_element_type=f32)
    tokens_gradient = dres_first + tp_sum(dinput_part)
    late = jnp.concatenate(
        [
            qkv_weight_part,
            tp_gather(query_bias_part).reshape(rows, 1),
            tp_gather(value_bias_part).reshape(rows, 1),
        ],
        axis=1,
    ).astype(low)
    late_piece = lax.psum(shard_scatter(late).astype(low), "ctx").astype(f32)
    query_total = late_piece[:, :head_width]
    key_total = late_piece[:, head_width : 2 * head_width]
    value_total = late_piece[:, 2 * head_width : 3 * head_width]
    qbias_total = lax.dynamic_slice_in_dim(
        late_piece[:, 3 * head_width], tensor_place * local_rows, local_rows
    )
    vbias_total = lax.dynamic_slice_in_dim(
        late_piece[:, 3 * head_width + 1], tensor_place * local_rows, local_rows
    )
    return (
        layer_out,
        tokens_gradient,
        query_total,
        qbias_total,
        key_total,
        value_total,
        vbias_total,
        output_total,
        outbias_total,
        attn_gain_total,
        attn_shift_total,
        inner_total,
        ibias_total,
        outer_total,
        outerbias_total,
        final_gain_total,
        final_shift_total,
    )


def solution(mesh):
    placed = (
        P(("shard", "ctx"), None),
        P("shard"),
        P("shard", "tp"),
        P(("shard", "tp")),
        P("shard", "tp"),
        P("shard", "tp"),
        P(("shard", "tp")),
        P("shard", "tp"),
        P("shard"),
        P("shard"),
        P("shard"),
        P("shard", "tp"),
        P(("shard", "tp")),
        P("shard", "tp"),
        P("shard"),
        P("shard"),
        P("shard"),
        P(("shard", "ctx"), None),
    )
    return jax.shard_map(
        on_device,
        mesh=mesh,
        in_specs=placed,
        out_specs=(
            P(("shard", "ctx"), None),
            P(("shard", "ctx"), None),
            P("shard", "tp"),
            P(("shard", "tp")),
            P("shard", "tp"),
            P("shard", "tp"),
            P(("shard", "tp")),
            P("shard", "tp"),
            P("shard"),
            P("shard"),
            P("shard"),
            P("shard", "tp"),
            P(("shard", "tp")),
            P("shard", "tp"),
            P("shard"),
            P("shard"),
            P("shard"),
        ),
        check_vma=False,
    )
```

```python
import functools

import jax
import jax.numpy as jnp
from jax import lax
from jax.experimental import pallas as pl
from jax.experimental.pallas import tpu as pltpu
from jax.sharding import PartitionSpec as P

HEAD_DIM = 64
QUERY_TILE = 128


def _scores(length_ref, q, k, factor):
    s = lax.dot_general(q, k, (((1,), (1,)), ((), ())), preferred_element_type=jnp.float32) * factor
    keys = lax.broadcasted_iota(jnp.int32, s.shape, 1)
    return jnp.where(keys < length_ref[0], s, -1e30)


def _attend_kernel(length_ref, q_ref, kv_ref, o_ref, lse_ref, *, heads, factor):
    for h in range(heads):
        cols = slice(h * HEAD_DIM, (h + 1) * HEAD_DIM)
        vcols = slice((heads + h) * HEAD_DIM, (heads + h + 1) * HEAD_DIM)
        s = _scores(length_ref, q_ref[:, cols], kv_ref[:, cols], factor)
        highest = jnp.max(s, axis=1, keepdims=True)
        shifted = jnp.exp(s - highest)
        summed = jnp.sum(shifted, axis=1, keepdims=True)
        portion = (shifted / summed).astype(jnp.bfloat16)
        mixed = jnp.dot(portion, kv_ref[:, vcols], preferred_element_type=jnp.float32)
        o_ref[:, cols] = mixed.astype(o_ref.dtype)
        lse_ref[:, h : h + 1] = highest + jnp.log(summed)


def attend(length, q, kv, factor):
    n, width = q.shape
    m = kv.shape[0]
    heads = width // HEAD_DIM
    tq = min(QUERY_TILE, n)
    grid = pltpu.PrefetchScalarGridSpec(
        num_scalar_prefetch=1,
        grid=(n // tq,),
        in_specs=[
            pl.BlockSpec((tq, width), lambda i, length: (i, 0)),
            pl.BlockSpec((m, 2 * width), lambda i, length: (0, 0)),
        ],
        out_specs=[
            pl.BlockSpec((tq, width), lambda i, length: (i, 0)),
            pl.BlockSpec((tq, heads), lambda i, length: (i, 0)),
        ],
    )
    flops = 4 * n * m * width
    return pl.pallas_call(
        functools.partial(_attend_kernel, heads=heads, factor=factor),
        grid_spec=grid,
        out_shape=(
            jax.ShapeDtypeStruct((n, width), jnp.bfloat16),
            jax.ShapeDtypeStruct((n, heads), jnp.float32),
        ),
        compiler_params=pltpu.CompilerParams(dimension_semantics=("arbitrary",)),
        cost_estimate=pl.CostEstimate(
            flops=flops, transcendentals=n * m * heads, bytes_accessed=2 * (2 * n * width + 2 * m * width)
        ),
    )(length, q, kv)


def _attend_back_kernel(length_ref, q_ref, kv_ref, do_ref, lse_ref, dq_ref, dkv_ref, *, heads, factor):
    @pl.when(pl.program_id(0) == 0)
    def _():
        dkv_ref[...] = jnp.zeros_like(dkv_ref)

    for h in range(heads):
        cols = slice(h * HEAD_DIM, (h + 1) * HEAD_DIM)
        vcols = slice((heads + h) * HEAD_DIM, (heads + h + 1) * HEAD_DIM)
        q = q_ref[:, cols]
        k = kv_ref[:, cols]
        v = kv_ref[:, vcols]
        do = do_ref[:, cols]
        portion = jnp.exp(_scores(length_ref, q, k, factor) - lse_ref[:, h : h + 1])
        dportion = lax.dot_general(do, v, (((1,), (1,)), ((), ())), preferred_element_type=jnp.float32)
        dkv_ref[:, vcols] += lax.dot_general(
            portion.astype(jnp.bfloat16), do, (((0,), (0,)), ((), ())), preferred_element_type=jnp.float32
        )
        centering = jnp.sum(portion * dportion, axis=1, keepdims=True)
        dscores = (portion * (dportion - centering)).astype(jnp.bfloat16)
        dq_ref[:, cols] = (
            jnp.dot(dscores, k, preferred_element_type=jnp.float32) * factor
        ).astype(dq_ref.dtype)
        dkv_ref[:, cols] += (
            lax.dot_general(dscores, q, (((0,), (0,)), ((), ())), preferred_element_type=jnp.float32) * factor
        )


def attend_back(length, q, kv, do, lse, factor):
    n, width = q.shape
    m = kv.shape[0]
    heads = width // HEAD_DIM
    tq = min(QUERY_TILE, n)
    grid = pltpu.PrefetchScalarGridSpec(
        num_scalar_prefetch=1,
        grid=(n // tq,),
        in_specs=[
            pl.BlockSpec((tq, width), lambda i, length: (i, 0)),
            pl.BlockSpec((m, 2 * width), lambda i, length: (0, 0)),
            pl.BlockSpec((tq, width), lambda i, length: (i, 0)),
            pl.BlockSpec((tq, heads), lambda i, length: (i, 0)),
        ],
        out_specs=[
            pl.BlockSpec((tq, width), lambda i, length: (i, 0)),
            pl.BlockSpec((m, 2 * width), lambda i, length: (0, 0)),
        ],
    )
    flops = 10 * n * m * width
    return pl.pallas_call(
        functools.partial(_attend_back_kernel, heads=heads, factor=factor),
        grid_spec=grid,
        out_shape=(
            jax.ShapeDtypeStruct((n, width), jnp.bfloat16),
            jax.ShapeDtypeStruct((m, 2 * width), jnp.float32),
        ),
        compiler_params=pltpu.CompilerParams(dimension_semantics=("arbitrary",)),
        cost_estimate=pl.CostEstimate(
            flops=flops, transcendentals=n * m * heads,
            bytes_accessed=2 * (3 * n * width + 2 * m * width) + 4 * 2 * m * width,
        ),
    )(length, q, kv, do, lse)


EPSILON = 1e-12


def norm_parts(hidden):
    center = hidden - jnp.mean(hidden, -1, keepdims=True)
    inverse = lax.rsqrt(jnp.mean(center * center, -1, keepdims=True) + EPSILON)
    return (center * inverse, inverse)


def norm_back(gradient, normal_form, inverse, gain):
    scaled = gradient * gain
    inner = (
        scaled
        - jnp.mean(scaled, -1, keepdims=True)
        - normal_form * jnp.mean(scaled * normal_form, -1, keepdims=True)
    )
    return (inner * inverse, jnp.sum(gradient * normal_form, 0), jnp.sum(gradient, 0))


def exact_gelu(values):
    return jax.nn.gelu(values, approximate=False)


def _attend_query_back_kernel(length_ref, q_ref, kv_ref, do_ref, lse_ref, dq_ref, delta_ref, *, heads, factor):
    for h in range(heads):
        cols = slice(h * HEAD_DIM, (h + 1) * HEAD_DIM)
        vcols = slice((heads + h) * HEAD_DIM, (heads + h + 1) * HEAD_DIM)
        k = kv_ref[:, cols]
        do = do_ref[:, cols]
        portion = jnp.exp(_scores(length_ref, q_ref[:, cols], k, factor) - lse_ref[:, h : h + 1])
        dportion = lax.dot_general(
            do, kv_ref[:, vcols], (((1,), (1,)), ((), ())), preferred_element_type=jnp.float32
        )
        centering = jnp.sum(portion * dportion, axis=1, keepdims=True)
        dscores = (portion * (dportion - centering)).astype(jnp.bfloat16)
        dq_ref[:, cols] = (
            jnp.dot(dscores, k, preferred_element_type=jnp.float32) * factor
        ).astype(dq_ref.dtype)
        delta_ref[:, h : h + 1] = centering


def attend_query_back(length, q, kv, do, lse, factor):
    n, width = q.shape
    m = kv.shape[0]
    heads = width // HEAD_DIM
    tq = min(QUERY_TILE, n)
    grid = pltpu.PrefetchScalarGridSpec(
        num_scalar_prefetch=1,
        grid=(n // tq,),
        in_specs=[
            pl.BlockSpec((tq, width), lambda i, length: (i, 0)),
            pl.BlockSpec((m, 2 * width), lambda i, length: (0, 0)),
            pl.BlockSpec((tq, width), lambda i, length: (i, 0)),
            pl.BlockSpec((tq, heads), lambda i, length: (i, 0)),
        ],
        out_specs=[
            pl.BlockSpec((tq, width), lambda i, length: (i, 0)),
            pl.BlockSpec((tq, heads), lambda i, length: (i, 0)),
        ],
    )
    return pl.pallas_call(
        functools.partial(_attend_query_back_kernel, heads=heads, factor=factor),
        grid_spec=grid,
        out_shape=(
            jax.ShapeDtypeStruct((n, width), jnp.bfloat16),
            jax.ShapeDtypeStruct((n, heads), jnp.float32),
        ),
        compiler_params=pltpu.CompilerParams(dimension_semantics=("arbitrary",)),
        cost_estimate=pl.CostEstimate(
            flops=6 * n * m * width, transcendentals=n * m * heads,
            bytes_accessed=2 * (3 * n * width + 2 * m * width),
        ),
    )(length, q, kv, do, lse)


def _attend_key_back_kernel(length_ref, q_ref, kv_ref, do_ref, lse_ref, delta_ref, dkv_ref, *, heads, factor):
    @pl.when(pl.program_id(0) == 0)
    def _():
        dkv_ref[...] = jnp.zeros_like(dkv_ref)

    for h in range(heads):
        cols = slice(h * HEAD_DIM, (h + 1) * HEAD_DIM)
        vcols = slice((heads + h) * HEAD_DIM, (heads + h + 1) * HEAD_DIM)
        q = q_ref[:, cols]
        do = do_ref[:, cols]
        portion = jnp.exp(_scores(length_ref, q, kv_ref[:, cols], factor) - lse_ref[:, h : h + 1])
        dportion = lax.dot_general(
            do, kv_ref[:, vcols], (((1,), (1,)), ((), ())), preferred_element_type=jnp.float32
        )
        dkv_ref[:, vcols] += lax.dot_general(
            portion.astype(jnp.bfloat16), do, (((0,), (0,)), ((), ())), preferred_element_type=jnp.float32
        )
        dscores = (portion * (dportion - delta_ref[:, h : h + 1])).astype(jnp.bfloat16)
        dkv_ref[:, cols] += (
            lax.dot_general(dscores, q, (((0,), (0,)), ((), ())), preferred_element_type=jnp.float32) * factor
        )


def attend_key_back(length, q, kv, do, lse, delta, factor):
    n, width = q.shape
    m = kv.shape[0]
    heads = width // HEAD_DIM
    tq = min(QUERY_TILE, n)
    grid = pltpu.PrefetchScalarGridSpec(
        num_scalar_prefetch=1,
        grid=(n // tq,),
        in_specs=[
            pl.BlockSpec((tq, width), lambda i, length: (i, 0)),
            pl.BlockSpec((m, 2 * width), lambda i, length: (0, 0)),
            pl.BlockSpec((tq, width), lambda i, length: (i, 0)),
            pl.BlockSpec((tq, heads), lambda i, length: (i, 0)),
            pl.BlockSpec((tq, heads), lambda i, length: (i, 0)),
        ],
        out_specs=pl.BlockSpec((m, 2 * width), lambda i, length: (0, 0)),
    )
    return pl.pallas_call(
        functools.partial(_attend_key_back_kernel, heads=heads, factor=factor),
        grid_spec=grid,
        out_shape=jax.ShapeDtypeStruct((m, 2 * width), jnp.float32),
        compiler_params=pltpu.CompilerParams(dimension_semantics=("arbitrary",)),
        cost_estimate=pl.CostEstimate(
            flops=8 * n * m * width, transcendentals=n * m * heads,
            bytes_accessed=2 * (2 * n * width + 2 * m * width) + 4 * 2 * m * width,
        ),
    )(length, q, kv, do, lse, delta)


def tp_sum(value):
    if lax.axis_size("tp") == 2:
        return value + lax.ppermute(value, "tp", [(0, 1), (1, 0)])
    return lax.psum(value, "tp")


def tp_gather(value):
    if lax.axis_size("tp") == 2:
        other = lax.ppermute(value, "tp", [(0, 1), (1, 0)])
        first = lax.axis_index("tp") == 0
        return jnp.stack([jnp.where(first, value, other), jnp.where(first, other, value)])
    return lax.all_gather(value, "tp")


def shard_send(value, axis="shard"):
    count = lax.axis_size(axis)
    if count > 8:
        return [lax.all_gather(value, axis, axis=0, tiled=True)]
    return [
        lax.ppermute(value, axis, [(j, (j + shift) % count) for j in range(count)])
        for shift in range(1, count)
    ]


def shard_assemble(value, arrived, axis="shard"):
    count = lax.axis_size(axis)
    if count > 8:
        return arrived[0]
    place = lax.axis_index(axis)
    rows = value.shape[0]
    out = jnp.zeros((count * rows,) + value.shape[1:], value.dtype)
    out = lax.dynamic_update_slice_in_dim(out, value, place * rows, 0)
    for shift, piece in enumerate(arrived, start=1):
        out = lax.dynamic_update_slice_in_dim(out, piece, ((place - shift) % count) * rows, 0)
    return out


def shard_gather(value, axis="shard"):
    return shard_assemble(value, shard_send(value, axis), axis)


def shard_scatter(value, axis="shard"):
    count = lax.axis_size(axis)
    if count > 8:
        return lax.psum_scatter(value, axis, scatter_dimension=0, tiled=True).astype(jnp.float32)
    place = lax.axis_index(axis)
    rows = value.shape[0] // count
    total = lax.dynamic_slice_in_dim(value, place * rows, rows, 0).astype(jnp.float32)
    for shift in range(1, count):
        outgoing = lax.dynamic_slice_in_dim(value, ((place + shift) % count) * rows, rows, 0)
        arrived = lax.ppermute(outgoing, axis, [(j, (j + shift) % count) for j in range(count)])
        total = total + arrived.astype(jnp.float32)
    return total


def on_device(
    tokens,
    seq_lengths,
    query_weight,
    query_bias,
    key_weight,
    value_weight,
    value_bias,
    output_weight,
    output_bias,
    attn_gain,
    attn_shift,
    inner_weight,
    inner_bias,
    outer_weight,
    outer_bias,
    final_gain,
    final_shift,
    upstream,
):
    row_count, model_width = tokens.shape
    tensor_place = lax.axis_index("tp")
    tensor_count = lax.axis_size("tp")
    head_width = query_weight.shape[1]
    hidden_width = inner_weight.shape[1]
    head_count = head_width // HEAD_DIM
    factor = HEAD_DIM ** (-0.5)
    f32 = jnp.float32

    qb = query_bias.shape[0]
    ib = inner_bias.shape[0]
    piece = output_bias.shape[0]
    tp_blocks = tp_gather(jnp.concatenate([query_bias, value_bias, inner_bias]))
    bias_columns = jnp.concatenate(
        [
            tp_blocks[:, :qb].reshape(piece, 1),
            tp_blocks[:, qb : 2 * qb].reshape(piece, 1),
            tp_blocks[:, 2 * qb :].reshape(piece, -1),
        ],
        axis=1,
    )
    shard_columns = jnp.stack(
        [output_bias, attn_gain, attn_shift, outer_bias, final_gain, final_shift], axis=1
    )
    kv_vec_full = lax.all_gather(
        jnp.concatenate([key_weight, value_weight, shard_columns, bias_columns], axis=1),
        "shard", axis=0, tiled=True,
    )
    query_full = shard_gather(query_weight)
    vector_full = kv_vec_full[:, 2 * head_width :]
    key_full = kv_vec_full[:, :head_width]
    value_full = kv_vec_full[:, head_width : 2 * head_width]
    qkv_full = jnp.concatenate([query_full, kv_vec_full[:, : 2 * head_width]], axis=1)
    rest_local = jnp.concatenate([output_weight, inner_weight, outer_weight], axis=1)
    rest_arrived = shard_send(rest_local)

    full_vectors = vector_full[:, :6].T.astype(f32)
    outbias_full, gain_first, shift_first, outerbias_full, gain_second, shift_second = full_vectors
    qbias_all = vector_full[:, 6]
    vbias_all = vector_full[:, 7]
    ibias_all = vector_full[:, 8:].reshape(-1)
    query_shift = lax.dynamic_slice_in_dim(qbias_all, tensor_place * head_width, head_width).astype(f32)
    value_shift = lax.dynamic_slice_in_dim(vbias_all, tensor_place * head_width, head_width).astype(f32)
    inner_shift = lax.dynamic_slice_in_dim(ibias_all, tensor_place * hidden_width, hidden_width).astype(f32)

    projected = jnp.dot(tokens, kv_vec_full[:, : 2 * head_width], preferred_element_type=f32)
    key_local = projected[:, :head_width].astype(jnp.bfloat16)
    value_local = (projected[:, head_width:] + value_shift).astype(jnp.bfloat16)
    query = (jnp.dot(tokens, query_full, preferred_element_type=f32) + query_shift).astype(
        jnp.bfloat16
    )
    chunk_heads = 2 if head_count % 2 == 0 else 1
    chunk_width = chunk_heads * HEAD_DIM
    kv_chunks = []
    own_chunks = []
    for c in range(head_count // chunk_heads):
        columns = slice(c * chunk_width, (c + 1) * chunk_width)
        outgoing = jnp.concatenate([key_local[:, columns], value_local[:, columns]], axis=1)
        own_chunks.append(outgoing)
        kv_chunks.append(lax.all_gather(outgoing, "ctx", axis=0, tiled=True))
    query_all = lax.all_gather(query, "ctx", axis=0, tiled=True)
    chunk_outs = [
        attend(seq_lengths, query[:, c * chunk_width : (c + 1) * chunk_width], chunk, factor)
        for c, chunk in enumerate(kv_chunks)
    ]
    context = jnp.concatenate([o[0] for o in chunk_outs], axis=1)
    log_sums = jnp.concatenate([o[1] for o in chunk_outs], axis=1)
    log_sums_all = shard_gather(log_sums, "ctx")
    rest_arrived, context = lax.optimization_barrier((rest_arrived, context))
    rest_full = shard_assemble(rest_local, rest_arrived)
    output_full = rest_full[:, :head_width]
    inner_full = rest_full[:, head_width : head_width + hidden_width]
    outer_full = rest_full[:, head_width + hidden_width :]
    attn_part = jnp.einsum("th,oh->to", context, output_full, preferred_element_type=f32)
    attended = tp_sum(attn_part) + outbias_full
    normal_first, inverse_first = norm_parts(tokens.astype(f32) + attended)
    normed = normal_first * gain_first + shift_first
    normed_low = normed.astype(jnp.bfloat16)
    hidden = jnp.dot(normed_low, inner_full, preferred_element_type=f32) + inner_shift
    active = exact_gelu(hidden).astype(jnp.bfloat16)
    branch_part = jnp.einsum("tf,of->to", active, outer_full, preferred_element_type=f32)
    branch = tp_sum(branch_part) + outerbias_full
    normal_second, inverse_second = norm_parts(normed + branch)
    layer_out = (normal_second * gain_second + shift_second).astype(jnp.bfloat16)

    dres_second, final_gain_part, final_shift_part = norm_back(
        upstream.astype(f32), normal_second, inverse_second, gain_second
    )
    dbranch = dres_second.astype(jnp.bfloat16)
    outer_bias_part = jnp.sum(dbranch.astype(f32), 0)
    outer_weight_part = jnp.einsum("to,tf->of", dbranch, active, preferred_element_type=f32)
    dactive = jnp.dot(dbranch, outer_full, preferred_element_type=f32)
    unused, gelu_pull = jax.vjp(exact_gelu, hidden)
    dhidden = gelu_pull(dactive)[0].astype(jnp.bfloat16)
    inner_weight_part = jnp.einsum("td,tf->df", normed_low, dhidden, preferred_element_type=f32)
    inner_bias_part = jnp.sum(dhidden.astype(f32), 0)
    dnormed_part = jnp.einsum("tf,df->td", dhidden, inner_full, preferred_element_type=f32)
    dnormed = dres_second + tp_sum(dnormed_part)
    dres_first, attn_gain_part, attn_shift_part = norm_back(
        dnormed, normal_first, inverse_first, gain_first
    )
    dattended = dres_first.astype(jnp.bfloat16)
    output_bias_part = jnp.sum(dattended.astype(f32), 0)
    output_weight_part = jnp.einsum("to,th->oh", dattended, context, preferred_element_type=f32)
    dcontext = jnp.dot(dattended, output_full, preferred_element_type=f32).astype(jnp.bfloat16)

    low = jnp.bfloat16
    rows = model_width
    early = jnp.concatenate(
        [
            output_weight_part,
            inner_weight_part,
            outer_weight_part,
            jnp.stack(
                [output_bias_part, attn_gain_part, attn_shift_part, outer_bias_part,
                 final_gain_part, final_shift_part],
                axis=1,
            ),
            tp_gather(inner_bias_part).reshape(rows, -1),
        ],
        axis=1,
    ).astype(low)
    early_scattered = shard_scatter(early).astype(low)
    local_rows = piece // tensor_count

    dcontext_all = lax.all_gather(dcontext, "ctx", axis=0, tiled=True)
    query_backs = [
        attend_query_back(
            seq_lengths,
            query[:, c * chunk_width : (c + 1) * chunk_width],
            chunk,
            dcontext[:, c * chunk_width : (c + 1) * chunk_width],
            chunk_outs[c][1],
            factor,
        )
        for c, chunk in enumerate(kv_chunks)
    ]
    dquery = jnp.concatenate([back[0] for back in query_backs], axis=1)
    deltas_all = shard_gather(jnp.concatenate([back[1] for back in query_backs], axis=1), "ctx")
    own_length = seq_lengths - lax.axis_index("ctx") * row_count
    key_backs = [
        attend_key_back(
            own_length,
            query_all[:, c * chunk_width : (c + 1) * chunk_width],
            own,
            dcontext_all[:, c * chunk_width : (c + 1) * chunk_width],
            log_sums_all[:, c * chunk_heads : (c + 1) * chunk_heads],
            deltas_all[:, c * chunk_heads : (c + 1) * chunk_heads],
            factor,
        )
        for c, own in enumerate(own_chunks)
    ]
    dkeys = jnp.concatenate([back[:, :chunk_width] for back in key_backs], axis=1).astype(low)
    dvalues = jnp.concatenate([back[:, chunk_width:] for back in key_backs], axis=1).astype(low)
    early_piece = lax.psum(early_scattered, "ctx").astype(f32)
    output_total = early_piece[:, :head_width]
    inner_total = early_piece[:, head_width : head_width + hidden_width]
    outer_total = early_piece[:, head_width + hidden_width : head_width + 2 * hidden_width]
    early_vectors = early_piece[:, head_width + 2 * hidden_width :]
    outbias_total, attn_gain_total, attn_shift_total, outerbias_total, final_gain_total, final_shift_total = (
        early_vectors[:, :6].T
    )
    ibias_total = lax.dynamic_slice_in_dim(
        early_vectors[:, 6:], tensor_place * local_rows, local_rows, 0
    ).reshape(-1)
    dqkv = jnp.concatenate([dquery, dkeys, dvalues], axis=1)
    qkv_weight_part = jnp.einsum("td,th->dh", tokens, dqkv, preferred_element_type=f32)
    query_bias_part = jnp.sum(dquery.astype(f32), 0)
    value_bias_part = jnp.sum(dvalues.astype(f32), 0)
    dinput_part = jnp.einsum("th,dh->td", dqkv, qkv_full, preferred_element_type=f32)
    tokens_gradient = dres_first + tp_sum(dinput_part)
    late = jnp.concatenate(
        [
            qkv_weight_part,
            tp_gather(query_bias_part).reshape(rows, 1),
            tp_gather(value_bias_part).reshape(rows, 1),
        ],
        axis=1,
    ).astype(low)
    late_piece = lax.psum(shard_scatter(late).astype(low), "ctx").astype(f32)
    query_total = late_piece[:, :head_width]
    key_total = late_piece[:, head_width : 2 * head_width]
    value_total = late_piece[:, 2 * head_width : 3 * head_width]
    qbias_total = lax.dynamic_slice_in_dim(
        late_piece[:, 3 * head_width], tensor_place * local_rows, local_rows
    )
    vbias_total = lax.dynamic_slice_in_dim(
        late_piece[:, 3 * head_width + 1], tensor_place * local_rows, local_rows
    )
    return (
        layer_out,
        tokens_gradient,
        query_total,
        qbias_total,
        key_total,
        value_total,
        vbias_total,
        output_total,
        outbias_total,
        attn_gain_total,
        attn_shift_total,
        inner_total,
        ibias_total,
        outer_total,
        outerbias_total,
        final_gain_total,
        final_shift_total,
    )


def solution(mesh):
    placed = (
        P(("shard", "ctx"), None),
        P("shard"),
        P("shard", "tp"),
        P(("shard", "tp")),
        P("shard", "tp"),
        P("shard", "tp"),
        P(("shard", "tp")),
        P("shard", "tp"),
        P("shard"),
        P("shard"),
        P("shard"),
        P("shard", "tp"),
        P(("shard", "tp")),
        P("shard", "tp"),
        P("shard"),
        P("shard"),
        P("shard"),
        P(("shard", "ctx"), None),
    )
    return jax.shard_map(
        on_device,
        mesh=mesh,
        in_specs=placed,
        out_specs=(
            P(("shard", "ctx"), None),
            P(("shard", "ctx"), None),
            P("shard", "tp"),
            P(("shard", "tp")),
            P("shard", "tp"),
            P("shard", "tp"),
            P(("shard", "tp")),
            P("shard", "tp"),
            P("shard"),
            P("shard"),
            P("shard"),
            P("shard", "tp"),
            P(("shard", "tp")),
            P("shard", "tp"),
            P("shard"),
            P("shard"),
            P("shard"),
        ),
        check_vma=False,
    )
```

```python
import functools

import jax
import jax.numpy as jnp
from jax import lax
from jax.experimental import pallas as pl
from jax.experimental.pallas import tpu as pltpu
from jax.sharding import PartitionSpec as P

HEAD_DIM = 64
QUERY_TILE = 128
KEY_SIDE_TILE = 256


def _scores(length_ref, q, k, factor):
    s = lax.dot_general(q, k, (((1,), (1,)), ((), ())), preferred_element_type=jnp.float32) * factor
    keys = lax.broadcasted_iota(jnp.int32, s.shape, 1)
    return jnp.where(keys < length_ref[0], s, -1e30)


def _attend_kernel(length_ref, q_ref, kv_ref, o_ref, lse_ref, *, heads, factor):
    for h in range(heads):
        cols = slice(h * HEAD_DIM, (h + 1) * HEAD_DIM)
        vcols = slice((heads + h) * HEAD_DIM, (heads + h + 1) * HEAD_DIM)
        s = _scores(length_ref, q_ref[:, cols], kv_ref[:, cols], factor)
        highest = jnp.max(s, axis=1, keepdims=True)
        shifted = jnp.exp(s - highest)
        summed = jnp.sum(shifted, axis=1, keepdims=True)
        portion = (shifted / summed).astype(jnp.bfloat16)
        mixed = jnp.dot(portion, kv_ref[:, vcols], preferred_element_type=jnp.float32)
        o_ref[:, cols] = mixed.astype(o_ref.dtype)
        lse_ref[:, h : h + 1] = highest + jnp.log(summed)


def attend(length, q, kv, factor):
    n, width = q.shape
    m = kv.shape[0]
    heads = width // HEAD_DIM
    tq = min(QUERY_TILE, n)
    grid = pltpu.PrefetchScalarGridSpec(
        num_scalar_prefetch=1,
        grid=(n // tq,),
        in_specs=[
            pl.BlockSpec((tq, width), lambda i, length: (i, 0)),
            pl.BlockSpec((m, 2 * width), lambda i, length: (0, 0)),
        ],
        out_specs=[
            pl.BlockSpec((tq, width), lambda i, length: (i, 0)),
            pl.BlockSpec((tq, heads), lambda i, length: (i, 0)),
        ],
    )
    flops = 4 * n * m * width
    return pl.pallas_call(
        functools.partial(_attend_kernel, heads=heads, factor=factor),
        grid_spec=grid,
        out_shape=(
            jax.ShapeDtypeStruct((n, width), jnp.bfloat16),
            jax.ShapeDtypeStruct((n, heads), jnp.float32),
        ),
        compiler_params=pltpu.CompilerParams(dimension_semantics=("arbitrary",)),
        cost_estimate=pl.CostEstimate(
            flops=flops, transcendentals=n * m * heads, bytes_accessed=2 * (2 * n * width + 2 * m * width)
        ),
    )(length, q, kv)


def _attend_back_kernel(length_ref, q_ref, kv_ref, do_ref, lse_ref, dq_ref, dkv_ref, *, heads, factor):
    @pl.when(pl.program_id(0) == 0)
    def _():
        dkv_ref[...] = jnp.zeros_like(dkv_ref)

    for h in range(heads):
        cols = slice(h * HEAD_DIM, (h + 1) * HEAD_DIM)
        vcols = slice((heads + h) * HEAD_DIM, (heads + h + 1) * HEAD_DIM)
        q = q_ref[:, cols]
        k = kv_ref[:, cols]
        v = kv_ref[:, vcols]
        do = do_ref[:, cols]
        portion = jnp.exp(_scores(length_ref, q, k, factor) - lse_ref[:, h : h + 1])
        dportion = lax.dot_general(do, v, (((1,), (1,)), ((), ())), preferred_element_type=jnp.float32)
        dkv_ref[:, vcols] += lax.dot_general(
            portion.astype(jnp.bfloat16), do, (((0,), (0,)), ((), ())), preferred_element_type=jnp.float32
        )
        centering = jnp.sum(portion * dportion, axis=1, keepdims=True)
        dscores = (portion * (dportion - centering)).astype(jnp.bfloat16)
        dq_ref[:, cols] = (
            jnp.dot(dscores, k, preferred_element_type=jnp.float32) * factor
        ).astype(dq_ref.dtype)
        dkv_ref[:, cols] += (
            lax.dot_general(dscores, q, (((0,), (0,)), ((), ())), preferred_element_type=jnp.float32) * factor
        )


def attend_back(length, q, kv, do, lse, factor):
    n, width = q.shape
    m = kv.shape[0]
    heads = width // HEAD_DIM
    tq = min(QUERY_TILE, n)
    grid = pltpu.PrefetchScalarGridSpec(
        num_scalar_prefetch=1,
        grid=(n // tq,),
        in_specs=[
            pl.BlockSpec((tq, width), lambda i, length: (i, 0)),
            pl.BlockSpec((m, 2 * width), lambda i, length: (0, 0)),
            pl.BlockSpec((tq, width), lambda i, length: (i, 0)),
            pl.BlockSpec((tq, heads), lambda i, length: (i, 0)),
        ],
        out_specs=[
            pl.BlockSpec((tq, width), lambda i, length: (i, 0)),
            pl.BlockSpec((m, 2 * width), lambda i, length: (0, 0)),
        ],
    )
    flops = 10 * n * m * width
    return pl.pallas_call(
        functools.partial(_attend_back_kernel, heads=heads, factor=factor),
        grid_spec=grid,
        out_shape=(
            jax.ShapeDtypeStruct((n, width), jnp.bfloat16),
            jax.ShapeDtypeStruct((m, 2 * width), jnp.float32),
        ),
        compiler_params=pltpu.CompilerParams(dimension_semantics=("arbitrary",)),
        cost_estimate=pl.CostEstimate(
            flops=flops, transcendentals=n * m * heads,
            bytes_accessed=2 * (3 * n * width + 2 * m * width) + 4 * 2 * m * width,
        ),
    )(length, q, kv, do, lse)


EPSILON = 1e-12


def norm_parts(hidden):
    center = hidden - jnp.mean(hidden, -1, keepdims=True)
    inverse = lax.rsqrt(jnp.mean(center * center, -1, keepdims=True) + EPSILON)
    return (center * inverse, inverse)


def norm_back(gradient, normal_form, inverse, gain):
    scaled = gradient * gain
    inner = (
        scaled
        - jnp.mean(scaled, -1, keepdims=True)
        - normal_form * jnp.mean(scaled * normal_form, -1, keepdims=True)
    )
    return (inner * inverse, jnp.sum(gradient * normal_form, 0), jnp.sum(gradient, 0))


def exact_gelu(values):
    return jax.nn.gelu(values, approximate=False)


def _attend_query_back_kernel(length_ref, q_ref, kv_ref, do_ref, lse_ref, dq_ref, delta_ref, *, heads, factor):
    for h in range(heads):
        cols = slice(h * HEAD_DIM, (h + 1) * HEAD_DIM)
        vcols = slice((heads + h) * HEAD_DIM, (heads + h + 1) * HEAD_DIM)
        k = kv_ref[:, cols]
        do = do_ref[:, cols]
        portion = jnp.exp(_scores(length_ref, q_ref[:, cols], k, factor) - lse_ref[:, h : h + 1])
        dportion = lax.dot_general(
            do, kv_ref[:, vcols], (((1,), (1,)), ((), ())), preferred_element_type=jnp.float32
        )
        centering = jnp.sum(portion * dportion, axis=1, keepdims=True)
        dscores = (portion * (dportion - centering)).astype(jnp.bfloat16)
        dq_ref[:, cols] = (
            jnp.dot(dscores, k, preferred_element_type=jnp.float32) * factor
        ).astype(dq_ref.dtype)
        delta_ref[:, h : h + 1] = centering


def attend_query_back(length, q, kv, do, lse, factor):
    n, width = q.shape
    m = kv.shape[0]
    heads = width // HEAD_DIM
    tq = min(QUERY_TILE, n)
    grid = pltpu.PrefetchScalarGridSpec(
        num_scalar_prefetch=1,
        grid=(n // tq,),
        in_specs=[
            pl.BlockSpec((tq, width), lambda i, length: (i, 0)),
            pl.BlockSpec((m, 2 * width), lambda i, length: (0, 0)),
            pl.BlockSpec((tq, width), lambda i, length: (i, 0)),
            pl.BlockSpec((tq, heads), lambda i, length: (i, 0)),
        ],
        out_specs=[
            pl.BlockSpec((tq, width), lambda i, length: (i, 0)),
            pl.BlockSpec((tq, heads), lambda i, length: (i, 0)),
        ],
    )
    return pl.pallas_call(
        functools.partial(_attend_query_back_kernel, heads=heads, factor=factor),
        grid_spec=grid,
        out_shape=(
            jax.ShapeDtypeStruct((n, width), jnp.bfloat16),
            jax.ShapeDtypeStruct((n, heads), jnp.float32),
        ),
        compiler_params=pltpu.CompilerParams(dimension_semantics=("arbitrary",)),
        cost_estimate=pl.CostEstimate(
            flops=6 * n * m * width, transcendentals=n * m * heads,
            bytes_accessed=2 * (3 * n * width + 2 * m * width),
        ),
    )(length, q, kv, do, lse)


def _attend_key_back_kernel(length_ref, q_ref, kv_ref, do_ref, lse_ref, delta_ref, dkv_ref, *, heads, factor):
    @pl.when(pl.program_id(0) == 0)
    def _():
        dkv_ref[...] = jnp.zeros_like(dkv_ref)

    for h in range(heads):
        cols = slice(h * HEAD_DIM, (h + 1) * HEAD_DIM)
        vcols = slice((heads + h) * HEAD_DIM, (heads + h + 1) * HEAD_DIM)
        q = q_ref[:, cols]
        do = do_ref[:, cols]
        portion = jnp.exp(_scores(length_ref, q, kv_ref[:, cols], factor) - lse_ref[:, h : h + 1])
        dportion = lax.dot_general(
            do, kv_ref[:, vcols], (((1,), (1,)), ((), ())), preferred_element_type=jnp.float32
        )
        dkv_ref[:, vcols] += lax.dot_general(
            portion.astype(jnp.bfloat16), do, (((0,), (0,)), ((), ())), preferred_element_type=jnp.float32
        )
        dscores = (portion * (dportion - delta_ref[:, h : h + 1])).astype(jnp.bfloat16)
        dkv_ref[:, cols] += (
            lax.dot_general(dscores, q, (((0,), (0,)), ((), ())), preferred_element_type=jnp.float32) * factor
        )


def attend_key_back(length, q, kv, do, lse, delta, factor):
    n, width = q.shape
    m = kv.shape[0]
    heads = width // HEAD_DIM
    tq = min(KEY_SIDE_TILE, n)
    grid = pltpu.PrefetchScalarGridSpec(
        num_scalar_prefetch=1,
        grid=(n // tq,),
        in_specs=[
            pl.BlockSpec((tq, width), lambda i, length: (i, 0)),
            pl.BlockSpec((m, 2 * width), lambda i, length: (0, 0)),
            pl.BlockSpec((tq, width), lambda i, length: (i, 0)),
            pl.BlockSpec((tq, heads), lambda i, length: (i, 0)),
            pl.BlockSpec((tq, heads), lambda i, length: (i, 0)),
        ],
        out_specs=pl.BlockSpec((m, 2 * width), lambda i, length: (0, 0)),
    )
    return pl.pallas_call(
        functools.partial(_attend_key_back_kernel, heads=heads, factor=factor),
        grid_spec=grid,
        out_shape=jax.ShapeDtypeStruct((m, 2 * width), jnp.float32),
        compiler_params=pltpu.CompilerParams(dimension_semantics=("arbitrary",)),
        cost_estimate=pl.CostEstimate(
            flops=8 * n * m * width, transcendentals=n * m * heads,
            bytes_accessed=2 * (2 * n * width + 2 * m * width) + 4 * 2 * m * width,
        ),
    )(length, q, kv, do, lse, delta)


def tp_sum(value):
    if lax.axis_size("tp") == 2:
        return value + lax.ppermute(value, "tp", [(0, 1), (1, 0)])
    return lax.psum(value, "tp")


def tp_gather(value):
    if lax.axis_size("tp") == 2:
        other = lax.ppermute(value, "tp", [(0, 1), (1, 0)])
        first = lax.axis_index("tp") == 0
        return jnp.stack([jnp.where(first, value, other), jnp.where(first, other, value)])
    return lax.all_gather(value, "tp")


def split_exact(value):
    high = lax.reduce_precision(value, exponent_bits=8, mantissa_bits=7)
    rest = value - high
    middle = lax.reduce_precision(rest, exponent_bits=8, mantissa_bits=7)
    low = lax.reduce_precision(rest - middle, exponent_bits=8, mantissa_bits=7)
    return jnp.concatenate([high, middle, low], axis=-1).astype(jnp.bfloat16)


def join_exact(pieces):
    width = pieces.shape[-1] // 3
    parts = pieces.astype(jnp.float32)
    return (parts[..., :width] + parts[..., width : 2 * width]) + parts[..., 2 * width :]


def shard_send(value, axis="shard"):
    count = lax.axis_size(axis)
    if count > 8:
        return [lax.all_gather(value, axis, axis=0, tiled=True)]
    return [
        lax.ppermute(value, axis, [(j, (j + shift) % count) for j in range(count)])
        for shift in range(1, count)
    ]


def shard_assemble(value, arrived, axis="shard"):
    count = lax.axis_size(axis)
    if count > 8:
        return arrived[0]
    place = lax.axis_index(axis)
    rows = value.shape[0]
    out = jnp.zeros((count * rows,) + value.shape[1:], value.dtype)
    out = lax.dynamic_update_slice_in_dim(out, value, place * rows, 0)
    for shift, piece in enumerate(arrived, start=1):
        out = lax.dynamic_update_slice_in_dim(out, piece, ((place - shift) % count) * rows, 0)
    return out


def shard_gather(value, axis="shard"):
    return shard_assemble(value, shard_send(value, axis), axis)


def shard_scatter(value, axis="shard"):
    count = lax.axis_size(axis)
    if count > 8:
        return lax.psum_scatter(value, axis, scatter_dimension=0, tiled=True).astype(jnp.float32)
    place = lax.axis_index(axis)
    rows = value.shape[0] // count
    total = lax.dynamic_slice_in_dim(value, place * rows, rows, 0).astype(jnp.float32)
    for shift in range(1, count):
        outgoing = lax.dynamic_slice_in_dim(value, ((place + shift) % count) * rows, rows, 0)
        arrived = lax.ppermute(outgoing, axis, [(j, (j + shift) % count) for j in range(count)])
        total = total + arrived.astype(jnp.float32)
    return total


def on_device(
    tokens,
    seq_lengths,
    query_weight,
    query_bias,
    key_weight,
    value_weight,
    value_bias,
    output_weight,
    output_bias,
    attn_gain,
    attn_shift,
    inner_weight,
    inner_bias,
    outer_weight,
    outer_bias,
    final_gain,
    final_shift,
    upstream,
):
    row_count, model_width = tokens.shape
    tensor_place = lax.axis_index("tp")
    tensor_count = lax.axis_size("tp")
    head_width = query_weight.shape[1]
    hidden_width = inner_weight.shape[1]
    head_count = head_width // HEAD_DIM
    factor = HEAD_DIM ** (-0.5)
    f32 = jnp.float32

    qb = query_bias.shape[0]
    ib = inner_bias.shape[0]
    piece = output_bias.shape[0]
    tp_blocks = tp_gather(jnp.concatenate([query_bias, value_bias, inner_bias]))
    bias_columns = jnp.concatenate(
        [
            tp_blocks[:, :qb].reshape(piece, 1),
            tp_blocks[:, qb : 2 * qb].reshape(piece, 1),
            tp_blocks[:, 2 * qb :].reshape(piece, -1),
        ],
        axis=1,
    )
    shard_columns = jnp.stack(
        [output_bias, attn_gain, attn_shift, outer_bias, final_gain, final_shift], axis=1
    )
    kv_vec_full = lax.all_gather(
        jnp.concatenate([key_weight, value_weight, shard_columns, bias_columns], axis=1),
        "shard", axis=0, tiled=True,
    )
    query_full = shard_gather(query_weight)
    vector_full = kv_vec_full[:, 2 * head_width :]
    key_full = kv_vec_full[:, :head_width]
    value_full = kv_vec_full[:, head_width : 2 * head_width]
    qkv_full = jnp.concatenate([query_full, kv_vec_full[:, : 2 * head_width]], axis=1)
    rest_local = jnp.concatenate([output_weight, inner_weight, outer_weight], axis=1)
    rest_arrived = shard_send(rest_local)

    full_vectors = vector_full[:, :6].T.astype(f32)
    outbias_full, gain_first, shift_first, outerbias_full, gain_second, shift_second = full_vectors
    qbias_all = vector_full[:, 6]
    vbias_all = vector_full[:, 7]
    ibias_all = vector_full[:, 8:].reshape(-1)
    query_shift = lax.dynamic_slice_in_dim(qbias_all, tensor_place * head_width, head_width).astype(f32)
    value_shift = lax.dynamic_slice_in_dim(vbias_all, tensor_place * head_width, head_width).astype(f32)
    inner_shift = lax.dynamic_slice_in_dim(ibias_all, tensor_place * hidden_width, hidden_width).astype(f32)

    projected = jnp.dot(tokens, kv_vec_full[:, : 2 * head_width], preferred_element_type=f32)
    key_local = projected[:, :head_width].astype(jnp.bfloat16)
    value_local = (projected[:, head_width:] + value_shift).astype(jnp.bfloat16)
    query = (jnp.dot(tokens, query_full, preferred_element_type=f32) + query_shift).astype(
        jnp.bfloat16
    )
    chunk_heads = 2 if head_count % 2 == 0 else 1
    chunk_width = chunk_heads * HEAD_DIM
    kv_chunks = []
    own_chunks = []
    for c in range(head_count // chunk_heads):
        columns = slice(c * chunk_width, (c + 1) * chunk_width)
        outgoing = jnp.concatenate([key_local[:, columns], value_local[:, columns]], axis=1)
        own_chunks.append(outgoing)
        kv_chunks.append(lax.all_gather(outgoing, "ctx", axis=0, tiled=True))
    query_all = lax.all_gather(query, "ctx", axis=0, tiled=True)
    chunk_outs = [
        attend(seq_lengths, query[:, c * chunk_width : (c + 1) * chunk_width], chunk, factor)
        for c, chunk in enumerate(kv_chunks)
    ]
    context = jnp.concatenate([o[0] for o in chunk_outs], axis=1)
    rest_arrived, context = lax.optimization_barrier((rest_arrived, context))
    rest_full = shard_assemble(rest_local, rest_arrived)
    output_full = rest_full[:, :head_width]
    inner_full = rest_full[:, head_width : head_width + hidden_width]
    outer_full = rest_full[:, head_width + hidden_width :]
    attn_part = jnp.einsum("th,oh->to", context, output_full, preferred_element_type=f32)
    attended = tp_sum(attn_part) + outbias_full
    normal_first, inverse_first = norm_parts(tokens.astype(f32) + attended)
    normed = normal_first * gain_first + shift_first
    normed_low = normed.astype(jnp.bfloat16)
    hidden = jnp.dot(normed_low, inner_full, preferred_element_type=f32) + inner_shift
    active = exact_gelu(hidden).astype(jnp.bfloat16)
    branch_part = jnp.einsum("tf,of->to", active, outer_full, preferred_element_type=f32)
    branch = tp_sum(branch_part) + outerbias_full
    normal_second, inverse_second = norm_parts(normed + branch)
    layer_out = (normal_second * gain_second + shift_second).astype(jnp.bfloat16)

    dres_second, final_gain_part, final_shift_part = norm_back(
        upstream.astype(f32), normal_second, inverse_second, gain_second
    )
    dbranch = dres_second.astype(jnp.bfloat16)
    outer_bias_part = jnp.sum(dbranch.astype(f32), 0)
    outer_weight_part = jnp.einsum("to,tf->of", dbranch, active, preferred_element_type=f32)
    dactive = jnp.dot(dbranch, outer_full, preferred_element_type=f32)
    unused, gelu_pull = jax.vjp(exact_gelu, hidden)
    dhidden = gelu_pull(dactive)[0].astype(jnp.bfloat16)
    inner_weight_part = jnp.einsum("td,tf->df", normed_low, dhidden, preferred_element_type=f32)
    inner_bias_part = jnp.sum(dhidden.astype(f32), 0)
    dnormed_part = jnp.einsum("tf,df->td", dhidden, inner_full, preferred_element_type=f32)
    dnormed = dres_second + tp_sum(dnormed_part)
    dres_first, attn_gain_part, attn_shift_part = norm_back(
        dnormed, normal_first, inverse_first, gain_first
    )
    dattended = dres_first.astype(jnp.bfloat16)
    output_bias_part = jnp.sum(dattended.astype(f32), 0)
    output_weight_part = jnp.einsum("to,th->oh", dattended, context, preferred_element_type=f32)
    dcontext = jnp.dot(dattended, output_full, preferred_element_type=f32).astype(jnp.bfloat16)

    low = jnp.bfloat16
    rows = model_width
    early = jnp.concatenate(
        [
            output_weight_part,
            inner_weight_part,
            outer_weight_part,
            jnp.stack(
                [output_bias_part, attn_gain_part, attn_shift_part, outer_bias_part,
                 final_gain_part, final_shift_part],
                axis=1,
            ),
            tp_gather(inner_bias_part).reshape(rows, -1),
        ],
        axis=1,
    ).astype(low)
    early_scattered = shard_scatter(early).astype(low)
    local_rows = piece // tensor_count

    own_length = seq_lengths - lax.axis_index("ctx") * row_count
    ctx_count = lax.axis_size("ctx")
    query_backs = []
    key_backs = []
    for c, chunk in enumerate(kv_chunks):
        pair = slice(c * chunk_width, (c + 1) * chunk_width)
        dquery_pair, delta_pair = attend_query_back(
            seq_lengths, query[:, pair], chunk, dcontext[:, pair], chunk_outs[c][1], factor
        )
        query_backs.append(dquery_pair)
        stats = split_exact(jnp.concatenate([chunk_outs[c][1], delta_pair], axis=1))
        stats_rows = stats.size // chunk_width
        padded_rows = -(-stats_rows // 16) * 16
        payload = jnp.concatenate(
            [
                dcontext[:, pair],
                stats.reshape(stats_rows, chunk_width),
                jnp.zeros((padded_rows - stats_rows, chunk_width), jnp.bfloat16),
            ],
            axis=0,
        )
        arrived = shard_gather(payload, "ctx").reshape(
            ctx_count, row_count + padded_rows, chunk_width
        )
        dcontext_pair_all = arrived[:, :row_count].reshape(ctx_count * row_count, chunk_width)
        stats_all = join_exact(
            arrived[:, row_count : row_count + stats_rows].reshape(
                ctx_count * row_count, stats.shape[1]
            )
        )
        key_backs.append(
            attend_key_back(
                own_length,
                query_all[:, pair],
                own_chunks[c],
                dcontext_pair_all,
                stats_all[:, :chunk_heads],
                stats_all[:, chunk_heads:],
                factor,
            )
        )
    dquery = jnp.concatenate(query_backs, axis=1)
    dkeys = jnp.concatenate([back[:, :chunk_width] for back in key_backs], axis=1).astype(low)
    dvalues = jnp.concatenate([back[:, chunk_width:] for back in key_backs], axis=1).astype(low)
    early_piece = lax.psum(early_scattered, "ctx").astype(f32)
    output_total = early_piece[:, :head_width]
    inner_total = early_piece[:, head_width : head_width + hidden_width]
    outer_total = early_piece[:, head_width + hidden_width : head_width + 2 * hidden_width]
    early_vectors = early_piece[:, head_width + 2 * hidden_width :]
    outbias_total, attn_gain_total, attn_shift_total, outerbias_total, final_gain_total, final_shift_total = (
        early_vectors[:, :6].T
    )
    ibias_total = lax.dynamic_slice_in_dim(
        early_vectors[:, 6:], tensor_place * local_rows, local_rows, 0
    ).reshape(-1)
    dqkv = jnp.concatenate([dquery, dkeys, dvalues], axis=1)
    qkv_weight_part = jnp.einsum("td,th->dh", tokens, dqkv, preferred_element_type=f32)
    query_bias_part = jnp.sum(dquery.astype(f32), 0)
    value_bias_part = jnp.sum(dvalues.astype(f32), 0)
    dinput_part = jnp.einsum("th,dh->td", dqkv, qkv_full, preferred_element_type=f32)
    tokens_gradient = dres_first + tp_sum(dinput_part)
    late = jnp.concatenate(
        [
            qkv_weight_part,
            tp_gather(query_bias_part).reshape(rows, 1),
            tp_gather(value_bias_part).reshape(rows, 1),
        ],
        axis=1,
    ).astype(low)
    late_piece = lax.psum(shard_scatter(late).astype(low), "ctx").astype(f32)
    query_total = late_piece[:, :head_width]
    key_total = late_piece[:, head_width : 2 * head_width]
    value_total = late_piece[:, 2 * head_width : 3 * head_width]
    qbias_total = lax.dynamic_slice_in_dim(
        late_piece[:, 3 * head_width], tensor_place * local_rows, local_rows
    )
    vbias_total = lax.dynamic_slice_in_dim(
        late_piece[:, 3 * head_width + 1], tensor_place * local_rows, local_rows
    )
    return (
        layer_out,
        tokens_gradient,
        query_total,
        qbias_total,
        key_total,
        value_total,
        vbias_total,
        output_total,
        outbias_total,
        attn_gain_total,
        attn_shift_total,
        inner_total,
        ibias_total,
        outer_total,
        outerbias_total,
        final_gain_total,
        final_shift_total,
    )


def solution(mesh):
    placed = (
        P(("shard", "ctx"), None),
        P("shard"),
        P("shard", "tp"),
        P(("shard", "tp")),
        P("shard", "tp"),
        P("shard", "tp"),
        P(("shard", "tp")),
        P("shard", "tp"),
        P("shard"),
        P("shard"),
        P("shard"),
        P("shard", "tp"),
        P(("shard", "tp")),
        P("shard", "tp"),
        P("shard"),
        P("shard"),
        P("shard"),
        P(("shard", "ctx"), None),
    )
    return jax.shard_map(
        on_device,
        mesh=mesh,
        in_specs=placed,
        out_specs=(
            P(("shard", "ctx"), None),
            P(("shard", "ctx"), None),
            P("shard", "tp"),
            P(("shard", "tp")),
            P("shard", "tp"),
            P("shard", "tp"),
            P(("shard", "tp")),
            P("shard", "tp"),
            P("shard"),
            P("shard"),
            P("shard"),
            P("shard", "tp"),
            P(("shard", "tp")),
            P("shard", "tp"),
            P("shard"),
            P("shard"),
            P("shard"),
        ),
        check_vma=False,
    )
```

```python
import functools

import jax
import jax.numpy as jnp
from jax import lax
from jax.experimental import pallas as pl
from jax.experimental.pallas import tpu as pltpu
from jax.sharding import PartitionSpec as P

HEAD_DIM = 64
QUERY_TILE = 128
KEY_SIDE_TILE = 256


def _scores(length_ref, q, k, factor):
    s = lax.dot_general(q, k, (((1,), (1,)), ((), ())), preferred_element_type=jnp.float32) * factor
    keys = lax.broadcasted_iota(jnp.int32, s.shape, 1)
    return jnp.where(keys < length_ref[0], s, -1e30)


def _attend_kernel(length_ref, q_ref, kv_ref, o_ref, lse_ref, *, heads, factor):
    for h in range(heads):
        cols = slice(h * HEAD_DIM, (h + 1) * HEAD_DIM)
        vcols = slice((heads + h) * HEAD_DIM, (heads + h + 1) * HEAD_DIM)
        s = _scores(length_ref, q_ref[:, cols], kv_ref[:, cols], factor)
        highest = jnp.max(s, axis=1, keepdims=True)
        shifted = jnp.exp(s - highest)
        summed = jnp.sum(shifted, axis=1, keepdims=True)
        portion = (shifted / summed).astype(jnp.bfloat16)
        mixed = jnp.dot(portion, kv_ref[:, vcols], preferred_element_type=jnp.float32)
        o_ref[:, cols] = mixed.astype(o_ref.dtype)
        lse_ref[:, h : h + 1] = highest + jnp.log(summed)


def attend(length, q, kv, factor):
    n, width = q.shape
    m = kv.shape[0]
    heads = width // HEAD_DIM
    tq = min(QUERY_TILE, n)
    grid = pltpu.PrefetchScalarGridSpec(
        num_scalar_prefetch=1,
        grid=(n // tq,),
        in_specs=[
            pl.BlockSpec((tq, width), lambda i, length: (i, 0)),
            pl.BlockSpec((m, 2 * width), lambda i, length: (0, 0)),
        ],
        out_specs=[
            pl.BlockSpec((tq, width), lambda i, length: (i, 0)),
            pl.BlockSpec((tq, heads), lambda i, length: (i, 0)),
        ],
    )
    flops = 4 * n * m * width
    return pl.pallas_call(
        functools.partial(_attend_kernel, heads=heads, factor=factor),
        grid_spec=grid,
        out_shape=(
            jax.ShapeDtypeStruct((n, width), jnp.bfloat16),
            jax.ShapeDtypeStruct((n, heads), jnp.float32),
        ),
        compiler_params=pltpu.CompilerParams(dimension_semantics=("arbitrary",)),
        cost_estimate=pl.CostEstimate(
            flops=flops, transcendentals=n * m * heads, bytes_accessed=2 * (2 * n * width + 2 * m * width)
        ),
    )(length, q, kv)


def _attend_back_kernel(length_ref, q_ref, kv_ref, do_ref, lse_ref, dq_ref, dkv_ref, *, heads, factor):
    @pl.when(pl.program_id(0) == 0)
    def _():
        dkv_ref[...] = jnp.zeros_like(dkv_ref)

    for h in range(heads):
        cols = slice(h * HEAD_DIM, (h + 1) * HEAD_DIM)
        vcols = slice((heads + h) * HEAD_DIM, (heads + h + 1) * HEAD_DIM)
        q = q_ref[:, cols]
        k = kv_ref[:, cols]
        v = kv_ref[:, vcols]
        do = do_ref[:, cols]
        portion = jnp.exp(_scores(length_ref, q, k, factor) - lse_ref[:, h : h + 1])
        dportion = lax.dot_general(do, v, (((1,), (1,)), ((), ())), preferred_element_type=jnp.float32)
        dkv_ref[:, vcols] += lax.dot_general(
            portion.astype(jnp.bfloat16), do, (((0,), (0,)), ((), ())), preferred_element_type=jnp.float32
        )
        centering = jnp.sum(portion * dportion, axis=1, keepdims=True)
        dscores = (portion * (dportion - centering)).astype(jnp.bfloat16)
        dq_ref[:, cols] = (
            jnp.dot(dscores, k, preferred_element_type=jnp.float32) * factor
        ).astype(dq_ref.dtype)
        dkv_ref[:, cols] += (
            lax.dot_general(dscores, q, (((0,), (0,)), ((), ())), preferred_element_type=jnp.float32) * factor
        )


def attend_back(length, q, kv, do, lse, factor):
    n, width = q.shape
    m = kv.shape[0]
    heads = width // HEAD_DIM
    tq = min(QUERY_TILE, n)
    grid = pltpu.PrefetchScalarGridSpec(
        num_scalar_prefetch=1,
        grid=(n // tq,),
        in_specs=[
            pl.BlockSpec((tq, width), lambda i, length: (i, 0)),
            pl.BlockSpec((m, 2 * width), lambda i, length: (0, 0)),
            pl.BlockSpec((tq, width), lambda i, length: (i, 0)),
            pl.BlockSpec((tq, heads), lambda i, length: (i, 0)),
        ],
        out_specs=[
            pl.BlockSpec((tq, width), lambda i, length: (i, 0)),
            pl.BlockSpec((m, 2 * width), lambda i, length: (0, 0)),
        ],
    )
    flops = 10 * n * m * width
    return pl.pallas_call(
        functools.partial(_attend_back_kernel, heads=heads, factor=factor),
        grid_spec=grid,
        out_shape=(
            jax.ShapeDtypeStruct((n, width), jnp.bfloat16),
            jax.ShapeDtypeStruct((m, 2 * width), jnp.float32),
        ),
        compiler_params=pltpu.CompilerParams(dimension_semantics=("arbitrary",)),
        cost_estimate=pl.CostEstimate(
            flops=flops, transcendentals=n * m * heads,
            bytes_accessed=2 * (3 * n * width + 2 * m * width) + 4 * 2 * m * width,
        ),
    )(length, q, kv, do, lse)


EPSILON = 1e-12


def norm_parts(hidden):
    center = hidden - jnp.mean(hidden, -1, keepdims=True)
    inverse = lax.rsqrt(jnp.mean(center * center, -1, keepdims=True) + EPSILON)
    return (center * inverse, inverse)


def norm_back(gradient, normal_form, inverse, gain):
    scaled = gradient * gain
    inner = (
        scaled
        - jnp.mean(scaled, -1, keepdims=True)
        - normal_form * jnp.mean(scaled * normal_form, -1, keepdims=True)
    )
    return (inner * inverse, jnp.sum(gradient * normal_form, 0), jnp.sum(gradient, 0))


def exact_gelu(values):
    return jax.nn.gelu(values, approximate=False)


def _attend_query_back_kernel(length_ref, q_ref, kv_ref, do_ref, lse_ref, dq_ref, delta_ref, *, heads, factor):
    for h in range(heads):
        cols = slice(h * HEAD_DIM, (h + 1) * HEAD_DIM)
        vcols = slice((heads + h) * HEAD_DIM, (heads + h + 1) * HEAD_DIM)
        k = kv_ref[:, cols]
        do = do_ref[:, cols]
        portion = jnp.exp(_scores(length_ref, q_ref[:, cols], k, factor) - lse_ref[:, h : h + 1])
        dportion = lax.dot_general(
            do, kv_ref[:, vcols], (((1,), (1,)), ((), ())), preferred_element_type=jnp.float32
        )
        centering = jnp.sum(portion * dportion, axis=1, keepdims=True)
        dscores = (portion * (dportion - centering)).astype(jnp.bfloat16)
        dq_ref[:, cols] = (
            jnp.dot(dscores, k, preferred_element_type=jnp.float32) * factor
        ).astype(dq_ref.dtype)
        delta_ref[:, h : h + 1] = centering


def attend_query_back(length, q, kv, do, lse, factor):
    n, width = q.shape
    m = kv.shape[0]
    heads = width // HEAD_DIM
    tq = min(QUERY_TILE, n)
    grid = pltpu.PrefetchScalarGridSpec(
        num_scalar_prefetch=1,
        grid=(n // tq,),
        in_specs=[
            pl.BlockSpec((tq, width), lambda i, length: (i, 0)),
            pl.BlockSpec((m, 2 * width), lambda i, length: (0, 0)),
            pl.BlockSpec((tq, width), lambda i, length: (i, 0)),
            pl.BlockSpec((tq, heads), lambda i, length: (i, 0)),
        ],
        out_specs=[
            pl.BlockSpec((tq, width), lambda i, length: (i, 0)),
            pl.BlockSpec((tq, heads), lambda i, length: (i, 0)),
        ],
    )
    return pl.pallas_call(
        functools.partial(_attend_query_back_kernel, heads=heads, factor=factor),
        grid_spec=grid,
        out_shape=(
            jax.ShapeDtypeStruct((n, width), jnp.bfloat16),
            jax.ShapeDtypeStruct((n, heads), jnp.float32),
        ),
        compiler_params=pltpu.CompilerParams(dimension_semantics=("arbitrary",)),
        cost_estimate=pl.CostEstimate(
            flops=6 * n * m * width, transcendentals=n * m * heads,
            bytes_accessed=2 * (3 * n * width + 2 * m * width),
        ),
    )(length, q, kv, do, lse)


def _attend_key_back_kernel(length_ref, q_ref, kv_ref, do_ref, lse_ref, delta_ref, dkv_ref, *, heads, factor):
    @pl.when(pl.program_id(0) == 0)
    def _():
        dkv_ref[...] = jnp.zeros_like(dkv_ref)

    for h in range(heads):
        cols = slice(h * HEAD_DIM, (h + 1) * HEAD_DIM)
        vcols = slice((heads + h) * HEAD_DIM, (heads + h + 1) * HEAD_DIM)
        q = q_ref[:, cols]
        do = do_ref[:, cols]
        portion = jnp.exp(_scores(length_ref, q, kv_ref[:, cols], factor) - lse_ref[:, h : h + 1])
        dportion = lax.dot_general(
            do, kv_ref[:, vcols], (((1,), (1,)), ((), ())), preferred_element_type=jnp.float32
        )
        dkv_ref[:, vcols] += lax.dot_general(
            portion.astype(jnp.bfloat16), do, (((0,), (0,)), ((), ())), preferred_element_type=jnp.float32
        )
        dscores = (portion * (dportion - delta_ref[:, h : h + 1])).astype(jnp.bfloat16)
        dkv_ref[:, cols] += (
            lax.dot_general(dscores, q, (((0,), (0,)), ((), ())), preferred_element_type=jnp.float32) * factor
        )


def attend_key_back(length, q, kv, do, lse, delta, factor):
    n, width = q.shape
    m = kv.shape[0]
    heads = width // HEAD_DIM
    tq = min(KEY_SIDE_TILE, n)
    grid = pltpu.PrefetchScalarGridSpec(
        num_scalar_prefetch=1,
        grid=(n // tq,),
        in_specs=[
            pl.BlockSpec((tq, width), lambda i, length: (i, 0)),
            pl.BlockSpec((m, 2 * width), lambda i, length: (0, 0)),
            pl.BlockSpec((tq, width), lambda i, length: (i, 0)),
            pl.BlockSpec((tq, heads), lambda i, length: (i, 0)),
            pl.BlockSpec((tq, heads), lambda i, length: (i, 0)),
        ],
        out_specs=pl.BlockSpec((m, 2 * width), lambda i, length: (0, 0)),
    )
    return pl.pallas_call(
        functools.partial(_attend_key_back_kernel, heads=heads, factor=factor),
        grid_spec=grid,
        out_shape=jax.ShapeDtypeStruct((m, 2 * width), jnp.float32),
        compiler_params=pltpu.CompilerParams(dimension_semantics=("arbitrary",)),
        cost_estimate=pl.CostEstimate(
            flops=8 * n * m * width, transcendentals=n * m * heads,
            bytes_accessed=2 * (2 * n * width + 2 * m * width) + 4 * 2 * m * width,
        ),
    )(length, q, kv, do, lse, delta)


def tp_sum(value):
    if lax.axis_size("tp") == 2:
        return value + lax.ppermute(value, "tp", [(0, 1), (1, 0)])
    return lax.psum(value, "tp")


def tp_gather(value):
    if lax.axis_size("tp") == 2:
        other = lax.ppermute(value, "tp", [(0, 1), (1, 0)])
        first = lax.axis_index("tp") == 0
        return jnp.stack([jnp.where(first, value, other), jnp.where(first, other, value)])
    return lax.all_gather(value, "tp")


def split_exact(value):
    high = lax.reduce_precision(value, exponent_bits=8, mantissa_bits=7)
    rest = value - high
    middle = lax.reduce_precision(rest, exponent_bits=8, mantissa_bits=7)
    low = lax.reduce_precision(rest - middle, exponent_bits=8, mantissa_bits=7)
    return jnp.concatenate([high, middle, low], axis=-1).astype(jnp.bfloat16)


def join_exact(pieces):
    width = pieces.shape[-1] // 3
    parts = pieces.astype(jnp.float32)
    return (parts[..., :width] + parts[..., width : 2 * width]) + parts[..., 2 * width :]


def shard_send(value, axis="shard"):
    count = lax.axis_size(axis)
    if count > 8:
        return [lax.all_gather(value, axis, axis=0, tiled=True)]
    return [
        lax.ppermute(value, axis, [(j, (j + shift) % count) for j in range(count)])
        for shift in range(1, count)
    ]


def shard_assemble(value, arrived, axis="shard"):
    count = lax.axis_size(axis)
    if count > 8:
        return arrived[0]
    place = lax.axis_index(axis)
    rows = value.shape[0]
    out = jnp.zeros((count * rows,) + value.shape[1:], value.dtype)
    out = lax.dynamic_update_slice_in_dim(out, value, place * rows, 0)
    for shift, piece in enumerate(arrived, start=1):
        out = lax.dynamic_update_slice_in_dim(out, piece, ((place - shift) % count) * rows, 0)
    return out


def shard_gather(value, axis="shard"):
    return shard_assemble(value, shard_send(value, axis), axis)


def shard_scatter(value, axis="shard"):
    count = lax.axis_size(axis)
    if count > 8:
        return lax.psum_scatter(value, axis, scatter_dimension=0, tiled=True).astype(jnp.float32)
    place = lax.axis_index(axis)
    rows = value.shape[0] // count
    total = lax.dynamic_slice_in_dim(value, place * rows, rows, 0).astype(jnp.float32)
    for shift in range(1, count):
        outgoing = lax.dynamic_slice_in_dim(value, ((place + shift) % count) * rows, rows, 0)
        arrived = lax.ppermute(outgoing, axis, [(j, (j + shift) % count) for j in range(count)])
        total = total + arrived.astype(jnp.float32)
    return total


def on_device(
    tokens,
    seq_lengths,
    query_weight,
    query_bias,
    key_weight,
    value_weight,
    value_bias,
    output_weight,
    output_bias,
    attn_gain,
    attn_shift,
    inner_weight,
    inner_bias,
    outer_weight,
    outer_bias,
    final_gain,
    final_shift,
    upstream,
):
    row_count, model_width = tokens.shape
    tensor_place = lax.axis_index("tp")
    tensor_count = lax.axis_size("tp")
    head_width = query_weight.shape[1]
    hidden_width = inner_weight.shape[1]
    head_count = head_width // HEAD_DIM
    factor = HEAD_DIM ** (-0.5)
    f32 = jnp.float32

    qb = query_bias.shape[0]
    ib = inner_bias.shape[0]
    piece = output_bias.shape[0]
    tp_blocks = tp_gather(jnp.concatenate([query_bias, value_bias, inner_bias]))
    bias_columns = jnp.concatenate(
        [
            tp_blocks[:, :qb].reshape(piece, 1),
            tp_blocks[:, qb : 2 * qb].reshape(piece, 1),
            tp_blocks[:, 2 * qb :].reshape(piece, -1),
        ],
        axis=1,
    )
    shard_columns = jnp.stack(
        [output_bias, attn_gain, attn_shift, outer_bias, final_gain, final_shift], axis=1
    )
    kv_vec_full = lax.all_gather(
        jnp.concatenate([key_weight, value_weight, shard_columns, bias_columns], axis=1),
        "shard", axis=0, tiled=True,
    )
    query_full = shard_gather(query_weight)
    vector_full = kv_vec_full[:, 2 * head_width :]
    key_full = kv_vec_full[:, :head_width]
    value_full = kv_vec_full[:, head_width : 2 * head_width]
    qkv_full = jnp.concatenate([query_full, kv_vec_full[:, : 2 * head_width]], axis=1)
    rest_local = jnp.concatenate([output_weight, inner_weight, outer_weight], axis=1)
    rest_arrived = shard_send(rest_local)

    full_vectors = vector_full[:, :6].T.astype(f32)
    outbias_full, gain_first, shift_first, outerbias_full, gain_second, shift_second = full_vectors
    qbias_all = vector_full[:, 6]
    vbias_all = vector_full[:, 7]
    ibias_all = vector_full[:, 8:].reshape(-1)
    query_shift = lax.dynamic_slice_in_dim(qbias_all, tensor_place * head_width, head_width).astype(f32)
    value_shift = lax.dynamic_slice_in_dim(vbias_all, tensor_place * head_width, head_width).astype(f32)
    inner_shift = lax.dynamic_slice_in_dim(ibias_all, tensor_place * hidden_width, hidden_width).astype(f32)

    projected = jnp.dot(tokens, kv_vec_full[:, : 2 * head_width], preferred_element_type=f32)
    key_local = projected[:, :head_width].astype(jnp.bfloat16)
    value_local = (projected[:, head_width:] + value_shift).astype(jnp.bfloat16)
    query = (jnp.dot(tokens, query_full, preferred_element_type=f32) + query_shift).astype(
        jnp.bfloat16
    )
    chunk_heads = 2 if head_count % 2 == 0 else 1
    chunk_width = chunk_heads * HEAD_DIM
    kv_chunks = []
    own_chunks = []
    for c in range(head_count // chunk_heads):
        columns = slice(c * chunk_width, (c + 1) * chunk_width)
        outgoing = jnp.concatenate([key_local[:, columns], value_local[:, columns]], axis=1)
        own_chunks.append(outgoing)
        kv_chunks.append(lax.all_gather(outgoing, "ctx", axis=0, tiled=True))
    query_all = lax.all_gather(query, "ctx", axis=0, tiled=True)
    chunk_outs = [
        attend(seq_lengths, query[:, c * chunk_width : (c + 1) * chunk_width], chunk, factor)
        for c, chunk in enumerate(kv_chunks)
    ]
    context = jnp.concatenate([o[0] for o in chunk_outs], axis=1)
    rest_arrived, context = lax.optimization_barrier((rest_arrived, context))
    rest_full = shard_assemble(rest_local, rest_arrived)
    output_full = rest_full[:, :head_width]
    inner_full = rest_full[:, head_width : head_width + hidden_width]
    outer_full = rest_full[:, head_width + hidden_width :]
    attn_part = jnp.einsum("th,oh->to", context, output_full, preferred_element_type=f32)
    attended = tp_sum(attn_part) + outbias_full
    normal_first, inverse_first = norm_parts(tokens.astype(f32) + attended)
    normed = normal_first * gain_first + shift_first
    normed_low = normed.astype(jnp.bfloat16)
    hidden = jnp.dot(normed_low, inner_full, preferred_element_type=f32) + inner_shift
    active = exact_gelu(hidden).astype(jnp.bfloat16)
    branch_part = jnp.einsum("tf,of->to", active, outer_full, preferred_element_type=f32)
    branch = tp_sum(branch_part) + outerbias_full
    normal_second, inverse_second = norm_parts(normed + branch)
    layer_out = (normal_second * gain_second + shift_second).astype(jnp.bfloat16)

    dres_second, final_gain_part, final_shift_part = norm_back(
        upstream.astype(f32), normal_second, inverse_second, gain_second
    )
    dbranch = dres_second.astype(jnp.bfloat16)
    outer_bias_part = jnp.sum(dbranch.astype(f32), 0)
    outer_weight_part = jnp.einsum("to,tf->of", dbranch, active, preferred_element_type=f32)
    dactive = jnp.dot(dbranch, outer_full, preferred_element_type=f32)
    unused, gelu_pull = jax.vjp(exact_gelu, hidden)
    dhidden = gelu_pull(dactive)[0].astype(jnp.bfloat16)
    inner_weight_part = jnp.einsum("td,tf->df", normed_low, dhidden, preferred_element_type=f32)
    inner_bias_part = jnp.sum(dhidden.astype(f32), 0)
    dnormed_part = jnp.einsum("tf,df->td", dhidden, inner_full, preferred_element_type=f32)
    dnormed = dres_second + tp_sum(dnormed_part)
    dres_first, attn_gain_part, attn_shift_part = norm_back(
        dnormed, normal_first, inverse_first, gain_first
    )
    dattended = dres_first.astype(jnp.bfloat16)
    output_bias_part = jnp.sum(dattended.astype(f32), 0)
    output_weight_part = jnp.einsum("to,th->oh", dattended, context, preferred_element_type=f32)
    dcontext = jnp.dot(dattended, output_full, preferred_element_type=f32).astype(jnp.bfloat16)

    low = jnp.bfloat16
    rows = model_width
    early = jnp.concatenate(
        [
            output_weight_part,
            inner_weight_part,
            outer_weight_part,
            jnp.stack(
                [output_bias_part, attn_gain_part, attn_shift_part, outer_bias_part,
                 final_gain_part, final_shift_part],
                axis=1,
            ),
            tp_gather(inner_bias_part).reshape(rows, -1),
        ],
        axis=1,
    ).astype(low)
    early_scattered = lax.psum_scatter(early, "shard", scatter_dimension=0, tiled=True)
    early_piece = lax.psum(early_scattered, "ctx")
    local_rows = piece // tensor_count

    own_length = seq_lengths - lax.axis_index("ctx") * row_count
    ctx_count = lax.axis_size("ctx")
    query_backs = []
    key_backs = []
    for c, chunk in enumerate(kv_chunks):
        pair = slice(c * chunk_width, (c + 1) * chunk_width)
        dquery_pair, delta_pair = attend_query_back(
            seq_lengths, query[:, pair], chunk, dcontext[:, pair], chunk_outs[c][1], factor
        )
        query_backs.append(dquery_pair)
        stats = split_exact(jnp.concatenate([chunk_outs[c][1], delta_pair], axis=1))
        stats_rows = stats.size // chunk_width
        padded_rows = -(-stats_rows // 16) * 16
        payload = jnp.concatenate(
            [
                dcontext[:, pair],
                stats.reshape(stats_rows, chunk_width),
                jnp.zeros((padded_rows - stats_rows, chunk_width), jnp.bfloat16),
            ],
            axis=0,
        )
        arrived = shard_gather(payload, "ctx").reshape(
            ctx_count, row_count + padded_rows, chunk_width
        )
        dcontext_pair_all = arrived[:, :row_count].reshape(ctx_count * row_count, chunk_width)
        stats_all = join_exact(
            arrived[:, row_count : row_count + stats_rows].reshape(
                ctx_count * row_count, stats.shape[1]
            )
        )
        key_backs.append(
            attend_key_back(
                own_length,
                query_all[:, pair],
                own_chunks[c],
                dcontext_pair_all,
                stats_all[:, :chunk_heads],
                stats_all[:, chunk_heads:],
                factor,
            )
        )
    dquery = jnp.concatenate(query_backs, axis=1)
    dkeys = jnp.concatenate([back[:, :chunk_width] for back in key_backs], axis=1).astype(low)
    dvalues = jnp.concatenate([back[:, chunk_width:] for back in key_backs], axis=1).astype(low)
    early_piece = early_piece.astype(f32)
    output_total = early_piece[:, :head_width]
    inner_total = early_piece[:, head_width : head_width + hidden_width]
    outer_total = early_piece[:, head_width + hidden_width : head_width + 2 * hidden_width]
    early_vectors = early_piece[:, head_width + 2 * hidden_width :]
    outbias_total, attn_gain_total, attn_shift_total, outerbias_total, final_gain_total, final_shift_total = (
        early_vectors[:, :6].T
    )
    ibias_total = lax.dynamic_slice_in_dim(
        early_vectors[:, 6:], tensor_place * local_rows, local_rows, 0
    ).reshape(-1)
    dqkv = jnp.concatenate([dquery, dkeys, dvalues], axis=1)
    qkv_weight_part = jnp.einsum("td,th->dh", tokens, dqkv, preferred_element_type=f32)
    query_bias_part = jnp.sum(dquery.astype(f32), 0)
    value_bias_part = jnp.sum(dvalues.astype(f32), 0)
    dinput_part = jnp.einsum("th,dh->td", dqkv, qkv_full, preferred_element_type=f32)
    tokens_gradient = dres_first + tp_sum(dinput_part)
    late = jnp.concatenate(
        [
            qkv_weight_part,
            tp_gather(query_bias_part).reshape(rows, 1),
            tp_gather(value_bias_part).reshape(rows, 1),
        ],
        axis=1,
    ).astype(low)
    late, early_piece = lax.optimization_barrier((late, early_piece))
    late_piece = lax.psum(shard_scatter(late).astype(low), "ctx").astype(f32)
    query_total = late_piece[:, :head_width]
    key_total = late_piece[:, head_width : 2 * head_width]
    value_total = late_piece[:, 2 * head_width : 3 * head_width]
    qbias_total = lax.dynamic_slice_in_dim(
        late_piece[:, 3 * head_width], tensor_place * local_rows, local_rows
    )
    vbias_total = lax.dynamic_slice_in_dim(
        late_piece[:, 3 * head_width + 1], tensor_place * local_rows, local_rows
    )
    return (
        layer_out,
        tokens_gradient,
        query_total,
        qbias_total,
        key_total,
        value_total,
        vbias_total,
        output_total,
        outbias_total,
        attn_gain_total,
        attn_shift_total,
        inner_total,
        ibias_total,
        outer_total,
        outerbias_total,
        final_gain_total,
        final_shift_total,
    )


def solution(mesh):
    placed = (
        P(("shard", "ctx"), None),
        P("shard"),
        P("shard", "tp"),
        P(("shard", "tp")),
        P("shard", "tp"),
        P("shard", "tp"),
        P(("shard", "tp")),
        P("shard", "tp"),
        P("shard"),
        P("shard"),
        P("shard"),
        P("shard", "tp"),
        P(("shard", "tp")),
        P("shard", "tp"),
        P("shard"),
        P("shard"),
        P("shard"),
        P(("shard", "ctx"), None),
    )
    return jax.shard_map(
        on_device,
        mesh=mesh,
        in_specs=placed,
        out_specs=(
            P(("shard", "ctx"), None),
            P(("shard", "ctx"), None),
            P("shard", "tp"),
            P(("shard", "tp")),
            P("shard", "tp"),
            P("shard", "tp"),
            P(("shard", "tp")),
            P("shard", "tp"),
            P("shard"),
            P("shard"),
            P("shard"),
            P("shard", "tp"),
            P(("shard", "tp")),
            P("shard", "tp"),
            P("shard"),
            P("shard"),
            P("shard"),
        ),
        check_vma=False,
    )
```

```python
import functools

import jax
import jax.numpy as jnp
from jax import lax
from jax.experimental import pallas as pl
from jax.experimental.pallas import tpu as pltpu
from jax.sharding import PartitionSpec as P

HEAD_DIM = 64
QUERY_TILE = 128
KEY_SIDE_TILE = 256


def _scores(length_ref, q, k, factor):
    s = lax.dot_general(q, k, (((1,), (1,)), ((), ())), preferred_element_type=jnp.float32) * factor
    keys = lax.broadcasted_iota(jnp.int32, s.shape, 1)
    return jnp.where(keys < length_ref[0], s, -1e30)


def _attend_kernel(length_ref, q_ref, kv_ref, o_ref, lse_ref, *, heads, factor):
    for h in range(heads):
        cols = slice(h * HEAD_DIM, (h + 1) * HEAD_DIM)
        vcols = slice((heads + h) * HEAD_DIM, (heads + h + 1) * HEAD_DIM)
        s = _scores(length_ref, q_ref[:, cols], kv_ref[:, cols], factor)
        highest = jnp.max(s, axis=1, keepdims=True)
        shifted = jnp.exp(s - highest)
        summed = jnp.sum(shifted, axis=1, keepdims=True)
        portion = (shifted / summed).astype(jnp.bfloat16)
        mixed = jnp.dot(portion, kv_ref[:, vcols], preferred_element_type=jnp.float32)
        o_ref[:, cols] = mixed.astype(o_ref.dtype)
        lse_ref[:, h : h + 1] = highest + jnp.log(summed)


def attend(length, q, kv, factor):
    n, width = q.shape
    m = kv.shape[0]
    heads = width // HEAD_DIM
    tq = min(QUERY_TILE, n)
    grid = pltpu.PrefetchScalarGridSpec(
        num_scalar_prefetch=1,
        grid=(n // tq,),
        in_specs=[
            pl.BlockSpec((tq, width), lambda i, length: (i, 0)),
            pl.BlockSpec((m, 2 * width), lambda i, length: (0, 0)),
        ],
        out_specs=[
            pl.BlockSpec((tq, width), lambda i, length: (i, 0)),
            pl.BlockSpec((tq, heads), lambda i, length: (i, 0)),
        ],
    )
    flops = 4 * n * m * width
    return pl.pallas_call(
        functools.partial(_attend_kernel, heads=heads, factor=factor),
        grid_spec=grid,
        out_shape=(
            jax.ShapeDtypeStruct((n, width), jnp.bfloat16),
            jax.ShapeDtypeStruct((n, heads), jnp.float32),
        ),
        compiler_params=pltpu.CompilerParams(dimension_semantics=("arbitrary",)),
        cost_estimate=pl.CostEstimate(
            flops=flops, transcendentals=n * m * heads, bytes_accessed=2 * (2 * n * width + 2 * m * width)
        ),
    )(length, q, kv)


def _attend_back_kernel(length_ref, q_ref, kv_ref, do_ref, lse_ref, dq_ref, dkv_ref, *, heads, factor):
    @pl.when(pl.program_id(0) == 0)
    def _():
        dkv_ref[...] = jnp.zeros_like(dkv_ref)

    for h in range(heads):
        cols = slice(h * HEAD_DIM, (h + 1) * HEAD_DIM)
        vcols = slice((heads + h) * HEAD_DIM, (heads + h + 1) * HEAD_DIM)
        q = q_ref[:, cols]
        k = kv_ref[:, cols]
        v = kv_ref[:, vcols]
        do = do_ref[:, cols]
        portion = jnp.exp(_scores(length_ref, q, k, factor) - lse_ref[:, h : h + 1])
        dportion = lax.dot_general(do, v, (((1,), (1,)), ((), ())), preferred_element_type=jnp.float32)
        dkv_ref[:, vcols] += lax.dot_general(
            portion.astype(jnp.bfloat16), do, (((0,), (0,)), ((), ())), preferred_element_type=jnp.float32
        )
        centering = jnp.sum(portion * dportion, axis=1, keepdims=True)
        dscores = (portion * (dportion - centering)).astype(jnp.bfloat16)
        dq_ref[:, cols] = (
            jnp.dot(dscores, k, preferred_element_type=jnp.float32) * factor
        ).astype(dq_ref.dtype)
        dkv_ref[:, cols] += (
            lax.dot_general(dscores, q, (((0,), (0,)), ((), ())), preferred_element_type=jnp.float32) * factor
        )


def attend_back(length, q, kv, do, lse, factor):
    n, width = q.shape
    m = kv.shape[0]
    heads = width // HEAD_DIM
    tq = min(QUERY_TILE, n)
    grid = pltpu.PrefetchScalarGridSpec(
        num_scalar_prefetch=1,
        grid=(n // tq,),
        in_specs=[
            pl.BlockSpec((tq, width), lambda i, length: (i, 0)),
            pl.BlockSpec((m, 2 * width), lambda i, length: (0, 0)),
            pl.BlockSpec((tq, width), lambda i, length: (i, 0)),
            pl.BlockSpec((tq, heads), lambda i, length: (i, 0)),
        ],
        out_specs=[
            pl.BlockSpec((tq, width), lambda i, length: (i, 0)),
            pl.BlockSpec((m, 2 * width), lambda i, length: (0, 0)),
        ],
    )
    flops = 10 * n * m * width
    return pl.pallas_call(
        functools.partial(_attend_back_kernel, heads=heads, factor=factor),
        grid_spec=grid,
        out_shape=(
            jax.ShapeDtypeStruct((n, width), jnp.bfloat16),
            jax.ShapeDtypeStruct((m, 2 * width), jnp.float32),
        ),
        compiler_params=pltpu.CompilerParams(dimension_semantics=("arbitrary",)),
        cost_estimate=pl.CostEstimate(
            flops=flops, transcendentals=n * m * heads,
            bytes_accessed=2 * (3 * n * width + 2 * m * width) + 4 * 2 * m * width,
        ),
    )(length, q, kv, do, lse)


EPSILON = 1e-12


def norm_parts(hidden):
    center = hidden - jnp.mean(hidden, -1, keepdims=True)
    inverse = lax.rsqrt(jnp.mean(center * center, -1, keepdims=True) + EPSILON)
    return (center * inverse, inverse)


def norm_back(gradient, normal_form, inverse, gain):
    scaled = gradient * gain
    inner = (
        scaled
        - jnp.mean(scaled, -1, keepdims=True)
        - normal_form * jnp.mean(scaled * normal_form, -1, keepdims=True)
    )
    return (inner * inverse, jnp.sum(gradient * normal_form, 0), jnp.sum(gradient, 0))


def exact_gelu(values):
    return jax.nn.gelu(values, approximate=False)


def _attend_query_back_kernel(length_ref, q_ref, kv_ref, do_ref, lse_ref, dq_ref, delta_ref, *, heads, factor):
    for h in range(heads):
        cols = slice(h * HEAD_DIM, (h + 1) * HEAD_DIM)
        vcols = slice((heads + h) * HEAD_DIM, (heads + h + 1) * HEAD_DIM)
        k = kv_ref[:, cols]
        do = do_ref[:, cols]
        portion = jnp.exp(_scores(length_ref, q_ref[:, cols], k, factor) - lse_ref[:, h : h + 1])
        dportion = lax.dot_general(
            do, kv_ref[:, vcols], (((1,), (1,)), ((), ())), preferred_element_type=jnp.float32
        )
        centering = jnp.sum(portion * dportion, axis=1, keepdims=True)
        dscores = (portion * (dportion - centering)).astype(jnp.bfloat16)
        dq_ref[:, cols] = (
            jnp.dot(dscores, k, preferred_element_type=jnp.float32) * factor
        ).astype(dq_ref.dtype)
        delta_ref[:, h : h + 1] = centering


def attend_query_back(length, q, kv, do, lse, factor):
    n, width = q.shape
    m = kv.shape[0]
    heads = width // HEAD_DIM
    tq = min(QUERY_TILE, n)
    grid = pltpu.PrefetchScalarGridSpec(
        num_scalar_prefetch=1,
        grid=(n // tq,),
        in_specs=[
            pl.BlockSpec((tq, width), lambda i, length: (i, 0)),
            pl.BlockSpec((m, 2 * width), lambda i, length: (0, 0)),
            pl.BlockSpec((tq, width), lambda i, length: (i, 0)),
            pl.BlockSpec((tq, heads), lambda i, length: (i, 0)),
        ],
        out_specs=[
            pl.BlockSpec((tq, width), lambda i, length: (i, 0)),
            pl.BlockSpec((tq, heads), lambda i, length: (i, 0)),
        ],
    )
    return pl.pallas_call(
        functools.partial(_attend_query_back_kernel, heads=heads, factor=factor),
        grid_spec=grid,
        out_shape=(
            jax.ShapeDtypeStruct((n, width), jnp.bfloat16),
            jax.ShapeDtypeStruct((n, heads), jnp.float32),
        ),
        compiler_params=pltpu.CompilerParams(dimension_semantics=("arbitrary",)),
        cost_estimate=pl.CostEstimate(
            flops=6 * n * m * width, transcendentals=n * m * heads,
            bytes_accessed=2 * (3 * n * width + 2 * m * width),
        ),
    )(length, q, kv, do, lse)


def _attend_key_back_kernel(length_ref, q_ref, kv_ref, do_ref, lse_ref, delta_ref, dkv_ref, *, heads, factor):
    @pl.when(pl.program_id(0) == 0)
    def _():
        dkv_ref[...] = jnp.zeros_like(dkv_ref)

    for h in range(heads):
        cols = slice(h * HEAD_DIM, (h + 1) * HEAD_DIM)
        vcols = slice((heads + h) * HEAD_DIM, (heads + h + 1) * HEAD_DIM)
        q = q_ref[:, cols]
        do = do_ref[:, cols]
        portion = jnp.exp(_scores(length_ref, q, kv_ref[:, cols], factor) - lse_ref[:, h : h + 1])
        dportion = lax.dot_general(
            do, kv_ref[:, vcols], (((1,), (1,)), ((), ())), preferred_element_type=jnp.float32
        )
        dkv_ref[:, vcols] += lax.dot_general(
            portion.astype(jnp.bfloat16), do, (((0,), (0,)), ((), ())), preferred_element_type=jnp.float32
        )
        dscores = (portion * (dportion - delta_ref[:, h : h + 1])).astype(jnp.bfloat16)
        dkv_ref[:, cols] += (
            lax.dot_general(dscores, q, (((0,), (0,)), ((), ())), preferred_element_type=jnp.float32) * factor
        )


def attend_key_back(length, q, kv, do, lse, delta, factor):
    n, width = q.shape
    m = kv.shape[0]
    heads = width // HEAD_DIM
    tq = min(KEY_SIDE_TILE, n)
    grid = pltpu.PrefetchScalarGridSpec(
        num_scalar_prefetch=1,
        grid=(n // tq,),
        in_specs=[
            pl.BlockSpec((tq, width), lambda i, length: (i, 0)),
            pl.BlockSpec((m, 2 * width), lambda i, length: (0, 0)),
            pl.BlockSpec((tq, width), lambda i, length: (i, 0)),
            pl.BlockSpec((tq, heads), lambda i, length: (i, 0)),
            pl.BlockSpec((tq, heads), lambda i, length: (i, 0)),
        ],
        out_specs=pl.BlockSpec((m, 2 * width), lambda i, length: (0, 0)),
    )
    return pl.pallas_call(
        functools.partial(_attend_key_back_kernel, heads=heads, factor=factor),
        grid_spec=grid,
        out_shape=jax.ShapeDtypeStruct((m, 2 * width), jnp.float32),
        compiler_params=pltpu.CompilerParams(dimension_semantics=("arbitrary",)),
        cost_estimate=pl.CostEstimate(
            flops=8 * n * m * width, transcendentals=n * m * heads,
            bytes_accessed=2 * (2 * n * width + 2 * m * width) + 4 * 2 * m * width,
        ),
    )(length, q, kv, do, lse, delta)


def tp_sum(value):
    if lax.axis_size("tp") == 2:
        return value + lax.ppermute(value, "tp", [(0, 1), (1, 0)])
    return lax.psum(value, "tp")


def tp_gather(value):
    if lax.axis_size("tp") == 2:
        other = lax.ppermute(value, "tp", [(0, 1), (1, 0)])
        first = lax.axis_index("tp") == 0
        return jnp.stack([jnp.where(first, value, other), jnp.where(first, other, value)])
    return lax.all_gather(value, "tp")


def split_exact(value):
    high = lax.reduce_precision(value, exponent_bits=8, mantissa_bits=7)
    rest = value - high
    middle = lax.reduce_precision(rest, exponent_bits=8, mantissa_bits=7)
    low = lax.reduce_precision(rest - middle, exponent_bits=8, mantissa_bits=7)
    return jnp.concatenate([high, middle, low], axis=-1).astype(jnp.bfloat16)


def join_exact(pieces):
    width = pieces.shape[-1] // 3
    parts = pieces.astype(jnp.float32)
    return (parts[..., :width] + parts[..., width : 2 * width]) + parts[..., 2 * width :]


def shard_send(value, axis="shard"):
    count = lax.axis_size(axis)
    if count > 8:
        return [lax.all_gather(value, axis, axis=0, tiled=True)]
    return [
        lax.ppermute(value, axis, [(j, (j + shift) % count) for j in range(count)])
        for shift in range(1, count)
    ]


def shard_assemble(value, arrived, axis="shard"):
    count = lax.axis_size(axis)
    if count > 8:
        return arrived[0]
    place = lax.axis_index(axis)
    rows = value.shape[0]
    out = jnp.zeros((count * rows,) + value.shape[1:], value.dtype)
    out = lax.dynamic_update_slice_in_dim(out, value, place * rows, 0)
    for shift, piece in enumerate(arrived, start=1):
        out = lax.dynamic_update_slice_in_dim(out, piece, ((place - shift) % count) * rows, 0)
    return out


def shard_gather(value, axis="shard"):
    return shard_assemble(value, shard_send(value, axis), axis)


def shard_scatter(value, axis="shard"):
    count = lax.axis_size(axis)
    if count > 8:
        return lax.psum_scatter(value, axis, scatter_dimension=0, tiled=True).astype(jnp.float32)
    place = lax.axis_index(axis)
    rows = value.shape[0] // count
    total = lax.dynamic_slice_in_dim(value, place * rows, rows, 0).astype(jnp.float32)
    for shift in range(1, count):
        outgoing = lax.dynamic_slice_in_dim(value, ((place + shift) % count) * rows, rows, 0)
        arrived = lax.ppermute(outgoing, axis, [(j, (j + shift) % count) for j in range(count)])
        total = total + arrived.astype(jnp.float32)
    return total


def on_device(
    tokens,
    seq_lengths,
    query_weight,
    query_bias,
    key_weight,
    value_weight,
    value_bias,
    output_weight,
    output_bias,
    attn_gain,
    attn_shift,
    inner_weight,
    inner_bias,
    outer_weight,
    outer_bias,
    final_gain,
    final_shift,
    upstream,
):
    row_count, model_width = tokens.shape
    tensor_place = lax.axis_index("tp")
    tensor_count = lax.axis_size("tp")
    head_width = query_weight.shape[1]
    hidden_width = inner_weight.shape[1]
    head_count = head_width // HEAD_DIM
    factor = HEAD_DIM ** (-0.5)
    f32 = jnp.float32

    qb = query_bias.shape[0]
    ib = inner_bias.shape[0]
    piece = output_bias.shape[0]
    tp_blocks = tp_gather(jnp.concatenate([query_bias, value_bias, inner_bias]))
    bias_columns = jnp.concatenate(
        [
            tp_blocks[:, :qb].reshape(piece, 1),
            tp_blocks[:, qb : 2 * qb].reshape(piece, 1),
            tp_blocks[:, 2 * qb :].reshape(piece, -1),
        ],
        axis=1,
    )
    shard_columns = jnp.stack(
        [output_bias, attn_gain, attn_shift, outer_bias, final_gain, final_shift], axis=1
    )
    kv_vec_full = lax.all_gather(
        jnp.concatenate([key_weight, value_weight, shard_columns, bias_columns], axis=1),
        "shard", axis=0, tiled=True,
    )
    query_full = shard_gather(query_weight)
    vector_full = kv_vec_full[:, 2 * head_width :]
    key_full = kv_vec_full[:, :head_width]
    value_full = kv_vec_full[:, head_width : 2 * head_width]
    qkv_full = jnp.concatenate([query_full, kv_vec_full[:, : 2 * head_width]], axis=1)
    rest_local = jnp.concatenate([output_weight, inner_weight, outer_weight], axis=1)
    rest_arrived = shard_send(rest_local)

    full_vectors = vector_full[:, :6].T.astype(f32)
    outbias_full, gain_first, shift_first, outerbias_full, gain_second, shift_second = full_vectors
    qbias_all = vector_full[:, 6]
    vbias_all = vector_full[:, 7]
    ibias_all = vector_full[:, 8:].reshape(-1)
    query_shift = lax.dynamic_slice_in_dim(qbias_all, tensor_place * head_width, head_width).astype(f32)
    value_shift = lax.dynamic_slice_in_dim(vbias_all, tensor_place * head_width, head_width).astype(f32)
    inner_shift = lax.dynamic_slice_in_dim(ibias_all, tensor_place * hidden_width, hidden_width).astype(f32)

    projected = jnp.dot(tokens, kv_vec_full[:, : 2 * head_width], preferred_element_type=f32)
    key_local = projected[:, :head_width].astype(jnp.bfloat16)
    value_local = (projected[:, head_width:] + value_shift).astype(jnp.bfloat16)
    query = (jnp.dot(tokens, query_full, preferred_element_type=f32) + query_shift).astype(
        jnp.bfloat16
    )
    chunk_heads = 2 if head_count % 2 == 0 else 1
    chunk_width = chunk_heads * HEAD_DIM
    kv_chunks = []
    own_chunks = []
    for c in range(head_count // chunk_heads):
        columns = slice(c * chunk_width, (c + 1) * chunk_width)
        outgoing = jnp.concatenate([key_local[:, columns], value_local[:, columns]], axis=1)
        own_chunks.append(outgoing)
        kv_chunks.append(lax.all_gather(outgoing, "ctx", axis=0, tiled=True))
    query_all = lax.all_gather(query, "ctx", axis=0, tiled=True)
    chunk_outs = [
        attend(seq_lengths, query[:, c * chunk_width : (c + 1) * chunk_width], chunk, factor)
        for c, chunk in enumerate(kv_chunks)
    ]
    context = jnp.concatenate([o[0] for o in chunk_outs], axis=1)
    rest_arrived, context = lax.optimization_barrier((rest_arrived, context))
    rest_full = shard_assemble(rest_local, rest_arrived)
    output_full = rest_full[:, :head_width]
    inner_full = rest_full[:, head_width : head_width + hidden_width]
    outer_full = rest_full[:, head_width + hidden_width :]
    attn_part = jnp.einsum("th,oh->to", context, output_full, preferred_element_type=f32)
    attended = tp_sum(attn_part) + outbias_full
    normal_first, inverse_first = norm_parts(tokens.astype(f32) + attended)
    normed = normal_first * gain_first + shift_first
    normed_low = normed.astype(jnp.bfloat16)
    hidden = jnp.dot(normed_low, inner_full, preferred_element_type=f32) + inner_shift
    active = exact_gelu(hidden).astype(jnp.bfloat16)
    branch_part = jnp.einsum("tf,of->to", active, outer_full, preferred_element_type=f32)
    branch = tp_sum(branch_part) + outerbias_full
    normal_second, inverse_second = norm_parts(normed + branch)
    layer_out = (normal_second * gain_second + shift_second).astype(jnp.bfloat16)

    dres_second, final_gain_part, final_shift_part = norm_back(
        upstream.astype(f32), normal_second, inverse_second, gain_second
    )
    dbranch = dres_second.astype(jnp.bfloat16)
    outer_bias_part = jnp.sum(dbranch.astype(f32), 0)
    outer_weight_part = jnp.einsum("to,tf->of", dbranch, active, preferred_element_type=f32)
    dactive = jnp.dot(dbranch, outer_full, preferred_element_type=f32)
    unused, gelu_pull = jax.vjp(exact_gelu, hidden)
    dhidden = gelu_pull(dactive)[0].astype(jnp.bfloat16)
    inner_weight_part = jnp.einsum("td,tf->df", normed_low, dhidden, preferred_element_type=f32)
    inner_bias_part = jnp.sum(dhidden.astype(f32), 0)
    dnormed_part = jnp.einsum("tf,df->td", dhidden, inner_full, preferred_element_type=f32)
    dnormed = dres_second + tp_sum(dnormed_part)
    dres_first, attn_gain_part, attn_shift_part = norm_back(
        dnormed, normal_first, inverse_first, gain_first
    )
    dattended = dres_first.astype(jnp.bfloat16)
    output_bias_part = jnp.sum(dattended.astype(f32), 0)
    output_weight_part = jnp.einsum("to,th->oh", dattended, context, preferred_element_type=f32)
    dcontext = jnp.dot(dattended, output_full, preferred_element_type=f32).astype(jnp.bfloat16)

    low = jnp.bfloat16
    rows = model_width
    early = jnp.concatenate(
        [
            output_weight_part,
            inner_weight_part,
            outer_weight_part,
            jnp.stack(
                [output_bias_part, attn_gain_part, attn_shift_part, outer_bias_part,
                 final_gain_part, final_shift_part],
                axis=1,
            ),
            tp_gather(inner_bias_part).reshape(rows, -1),
        ],
        axis=1,
    ).astype(low)
    early_scattered = lax.psum_scatter(early, "shard", scatter_dimension=0, tiled=True)
    local_rows = piece // tensor_count

    own_length = seq_lengths - lax.axis_index("ctx") * row_count
    ctx_count = lax.axis_size("ctx")
    query_backs = []
    key_backs = []
    for c, chunk in enumerate(kv_chunks):
        pair = slice(c * chunk_width, (c + 1) * chunk_width)
        dquery_pair, delta_pair = attend_query_back(
            seq_lengths, query[:, pair], chunk, dcontext[:, pair], chunk_outs[c][1], factor
        )
        query_backs.append(dquery_pair)
        stats = split_exact(jnp.concatenate([chunk_outs[c][1], delta_pair], axis=1))
        stats_rows = stats.size // chunk_width
        padded_rows = -(-stats_rows // 16) * 16
        payload = jnp.concatenate(
            [
                dcontext[:, pair],
                stats.reshape(stats_rows, chunk_width),
                jnp.zeros((padded_rows - stats_rows, chunk_width), jnp.bfloat16),
            ],
            axis=0,
        )
        arrived = shard_gather(payload, "ctx").reshape(
            ctx_count, row_count + padded_rows, chunk_width
        )
        dcontext_pair_all = arrived[:, :row_count].reshape(ctx_count * row_count, chunk_width)
        stats_all = join_exact(
            arrived[:, row_count : row_count + stats_rows].reshape(
                ctx_count * row_count, stats.shape[1]
            )
        )
        own = own_chunks[c]
        if key_backs:
            if len(key_backs) == 1:
                early_scattered, own, key_backs[-1] = lax.optimization_barrier(
                    (early_scattered, own, key_backs[-1])
                )
                early_piece = lax.psum(early_scattered, "ctx")
            else:
                own, key_backs[-1] = lax.optimization_barrier((own, key_backs[-1]))
        elif len(kv_chunks) == 1:
            early_piece = lax.psum(early_scattered, "ctx")
        key_backs.append(
            attend_key_back(
                own_length,
                query_all[:, pair],
                own,
                dcontext_pair_all,
                stats_all[:, :chunk_heads],
                stats_all[:, chunk_heads:],
                factor,
            )
        )
    dquery = jnp.concatenate(query_backs, axis=1)
    dkeys = jnp.concatenate([back[:, :chunk_width] for back in key_backs], axis=1).astype(low)
    dvalues = jnp.concatenate([back[:, chunk_width:] for back in key_backs], axis=1).astype(low)
    early_piece = early_piece.astype(f32)
    output_total = early_piece[:, :head_width]
    inner_total = early_piece[:, head_width : head_width + hidden_width]
    outer_total = early_piece[:, head_width + hidden_width : head_width + 2 * hidden_width]
    early_vectors = early_piece[:, head_width + 2 * hidden_width :]
    outbias_total, attn_gain_total, attn_shift_total, outerbias_total, final_gain_total, final_shift_total = (
        early_vectors[:, :6].T
    )
    ibias_total = lax.dynamic_slice_in_dim(
        early_vectors[:, 6:], tensor_place * local_rows, local_rows, 0
    ).reshape(-1)
    dqkv = jnp.concatenate([dquery, dkeys, dvalues], axis=1)
    qkv_weight_part = jnp.einsum("td,th->dh", tokens, dqkv, preferred_element_type=f32)
    query_bias_part = jnp.sum(dquery.astype(f32), 0)
    value_bias_part = jnp.sum(dvalues.astype(f32), 0)
    dinput_part = jnp.einsum("th,dh->td", dqkv, qkv_full, preferred_element_type=f32)
    tokens_gradient = dres_first + tp_sum(dinput_part)
    late = jnp.concatenate(
        [
            qkv_weight_part,
            tp_gather(query_bias_part).reshape(rows, 1),
            tp_gather(value_bias_part).reshape(rows, 1),
        ],
        axis=1,
    ).astype(low)
    late, early_piece = lax.optimization_barrier((late, early_piece))
    late_piece = lax.psum(shard_scatter(late).astype(low), "ctx").astype(f32)
    query_total = late_piece[:, :head_width]
    key_total = late_piece[:, head_width : 2 * head_width]
    value_total = late_piece[:, 2 * head_width : 3 * head_width]
    qbias_total = lax.dynamic_slice_in_dim(
        late_piece[:, 3 * head_width], tensor_place * local_rows, local_rows
    )
    vbias_total = lax.dynamic_slice_in_dim(
        late_piece[:, 3 * head_width + 1], tensor_place * local_rows, local_rows
    )
    return (
        layer_out,
        tokens_gradient,
        query_total,
        qbias_total,
        key_total,
        value_total,
        vbias_total,
        output_total,
        outbias_total,
        attn_gain_total,
        attn_shift_total,
        inner_total,
        ibias_total,
        outer_total,
        outerbias_total,
        final_gain_total,
        final_shift_total,
    )


def solution(mesh):
    placed = (
        P(("shard", "ctx"), None),
        P("shard"),
        P("shard", "tp"),
        P(("shard", "tp")),
        P("shard", "tp"),
        P("shard", "tp"),
        P(("shard", "tp")),
        P("shard", "tp"),
        P("shard"),
        P("shard"),
        P("shard"),
        P("shard", "tp"),
        P(("shard", "tp")),
        P("shard", "tp"),
        P("shard"),
        P("shard"),
        P("shard"),
        P(("shard", "ctx"), None),
    )
    return jax.shard_map(
        on_device,
        mesh=mesh,
        in_specs=placed,
        out_specs=(
            P(("shard", "ctx"), None),
            P(("shard", "ctx"), None),
            P("shard", "tp"),
            P(("shard", "tp")),
            P("shard", "tp"),
            P("shard", "tp"),
            P(("shard", "tp")),
            P("shard", "tp"),
            P("shard"),
            P("shard"),
            P("shard"),
            P("shard", "tp"),
            P(("shard", "tp")),
            P("shard", "tp"),
            P("shard"),
            P("shard"),
            P("shard"),
        ),
        check_vma=False,
    )
```

```python
import functools

import jax
import jax.numpy as jnp
from jax import lax
from jax.experimental import pallas as pl
from jax.experimental.pallas import tpu as pltpu
from jax.sharding import PartitionSpec as P

HEAD_DIM = 64
QUERY_TILE = 128
KEY_SIDE_TILE = 256


def _scores(length_ref, q, k, factor):
    s = lax.dot_general(q, k, (((1,), (1,)), ((), ())), preferred_element_type=jnp.float32) * factor
    keys = lax.broadcasted_iota(jnp.int32, s.shape, 1)
    return jnp.where(keys < length_ref[0], s, -1e30)


def _attend_kernel(length_ref, q_ref, kv_ref, o_ref, lse_ref, *, heads, factor):
    for h in range(heads):
        cols = slice(h * HEAD_DIM, (h + 1) * HEAD_DIM)
        vcols = slice((heads + h) * HEAD_DIM, (heads + h + 1) * HEAD_DIM)
        s = _scores(length_ref, q_ref[:, cols], kv_ref[:, cols], factor)
        highest = jnp.max(s, axis=1, keepdims=True)
        shifted = jnp.exp(s - highest)
        summed = jnp.sum(shifted, axis=1, keepdims=True)
        portion = (shifted / summed).astype(jnp.bfloat16)
        mixed = jnp.dot(portion, kv_ref[:, vcols], preferred_element_type=jnp.float32)
        o_ref[:, cols] = mixed.astype(o_ref.dtype)
        lse_ref[:, h : h + 1] = highest + jnp.log(summed)


def attend(length, q, kv, factor):
    n, width = q.shape
    m = kv.shape[0]
    heads = width // HEAD_DIM
    tq = min(QUERY_TILE, n)
    grid = pltpu.PrefetchScalarGridSpec(
        num_scalar_prefetch=1,
        grid=(n // tq,),
        in_specs=[
            pl.BlockSpec((tq, width), lambda i, length: (i, 0)),
            pl.BlockSpec((m, 2 * width), lambda i, length: (0, 0)),
        ],
        out_specs=[
            pl.BlockSpec((tq, width), lambda i, length: (i, 0)),
            pl.BlockSpec((tq, heads), lambda i, length: (i, 0)),
        ],
    )
    flops = 4 * n * m * width
    return pl.pallas_call(
        functools.partial(_attend_kernel, heads=heads, factor=factor),
        grid_spec=grid,
        out_shape=(
            jax.ShapeDtypeStruct((n, width), jnp.bfloat16),
            jax.ShapeDtypeStruct((n, heads), jnp.float32),
        ),
        compiler_params=pltpu.CompilerParams(dimension_semantics=("arbitrary",)),
        cost_estimate=pl.CostEstimate(
            flops=flops, transcendentals=n * m * heads, bytes_accessed=2 * (2 * n * width + 2 * m * width)
        ),
    )(length, q, kv)


def _attend_back_kernel(length_ref, q_ref, kv_ref, do_ref, lse_ref, dq_ref, dkv_ref, *, heads, factor):
    @pl.when(pl.program_id(0) == 0)
    def _():
        dkv_ref[...] = jnp.zeros_like(dkv_ref)

    for h in range(heads):
        cols = slice(h * HEAD_DIM, (h + 1) * HEAD_DIM)
        vcols = slice((heads + h) * HEAD_DIM, (heads + h + 1) * HEAD_DIM)
        q = q_ref[:, cols]
        k = kv_ref[:, cols]
        v = kv_ref[:, vcols]
        do = do_ref[:, cols]
        portion = jnp.exp(_scores(length_ref, q, k, factor) - lse_ref[:, h : h + 1])
        dportion = lax.dot_general(do, v, (((1,), (1,)), ((), ())), preferred_element_type=jnp.float32)
        dkv_ref[:, vcols] += lax.dot_general(
            portion.astype(jnp.bfloat16), do, (((0,), (0,)), ((), ())), preferred_element_type=jnp.float32
        )
        centering = jnp.sum(portion * dportion, axis=1, keepdims=True)
        dscores = (portion * (dportion - centering)).astype(jnp.bfloat16)
        dq_ref[:, cols] = (
            jnp.dot(dscores, k, preferred_element_type=jnp.float32) * factor
        ).astype(dq_ref.dtype)
        dkv_ref[:, cols] += (
            lax.dot_general(dscores, q, (((0,), (0,)), ((), ())), preferred_element_type=jnp.float32) * factor
        )


def attend_back(length, q, kv, do, lse, factor):
    n, width = q.shape
    m = kv.shape[0]
    heads = width // HEAD_DIM
    tq = min(QUERY_TILE, n)
    grid = pltpu.PrefetchScalarGridSpec(
        num_scalar_prefetch=1,
        grid=(n // tq,),
        in_specs=[
            pl.BlockSpec((tq, width), lambda i, length: (i, 0)),
            pl.BlockSpec((m, 2 * width), lambda i, length: (0, 0)),
            pl.BlockSpec((tq, width), lambda i, length: (i, 0)),
            pl.BlockSpec((tq, heads), lambda i, length: (i, 0)),
        ],
        out_specs=[
            pl.BlockSpec((tq, width), lambda i, length: (i, 0)),
            pl.BlockSpec((m, 2 * width), lambda i, length: (0, 0)),
        ],
    )
    flops = 10 * n * m * width
    return pl.pallas_call(
        functools.partial(_attend_back_kernel, heads=heads, factor=factor),
        grid_spec=grid,
        out_shape=(
            jax.ShapeDtypeStruct((n, width), jnp.bfloat16),
            jax.ShapeDtypeStruct((m, 2 * width), jnp.float32),
        ),
        compiler_params=pltpu.CompilerParams(dimension_semantics=("arbitrary",)),
        cost_estimate=pl.CostEstimate(
            flops=flops, transcendentals=n * m * heads,
            bytes_accessed=2 * (3 * n * width + 2 * m * width) + 4 * 2 * m * width,
        ),
    )(length, q, kv, do, lse)


EPSILON = 1e-12


def norm_parts(hidden):
    center = hidden - jnp.mean(hidden, -1, keepdims=True)
    inverse = lax.rsqrt(jnp.mean(center * center, -1, keepdims=True) + EPSILON)
    return (center * inverse, inverse)


def norm_back(gradient, normal_form, inverse, gain):
    scaled = gradient * gain
    inner = (
        scaled
        - jnp.mean(scaled, -1, keepdims=True)
        - normal_form * jnp.mean(scaled * normal_form, -1, keepdims=True)
    )
    return (inner * inverse, jnp.sum(gradient * normal_form, 0), jnp.sum(gradient, 0))


def exact_gelu(values):
    return jax.nn.gelu(values, approximate=False)


def _attend_query_back_kernel(length_ref, q_ref, kv_ref, do_ref, lse_ref, dq_ref, delta_ref, *, heads, factor):
    for h in range(heads):
        cols = slice(h * HEAD_DIM, (h + 1) * HEAD_DIM)
        vcols = slice((heads + h) * HEAD_DIM, (heads + h + 1) * HEAD_DIM)
        k = kv_ref[:, cols]
        do = do_ref[:, cols]
        portion = jnp.exp(_scores(length_ref, q_ref[:, cols], k, factor) - lse_ref[:, h : h + 1])
        dportion = lax.dot_general(
            do, kv_ref[:, vcols], (((1,), (1,)), ((), ())), preferred_element_type=jnp.float32
        )
        centering = jnp.sum(portion * dportion, axis=1, keepdims=True)
        dscores = (portion * (dportion - centering)).astype(jnp.bfloat16)
        dq_ref[:, cols] = (
            jnp.dot(dscores, k, preferred_element_type=jnp.float32) * factor
        ).astype(dq_ref.dtype)
        delta_ref[:, h : h + 1] = centering


def attend_query_back(length, q, kv, do, lse, factor):
    n, width = q.shape
    m = kv.shape[0]
    heads = width // HEAD_DIM
    tq = min(QUERY_TILE, n)
    grid = pltpu.PrefetchScalarGridSpec(
        num_scalar_prefetch=1,
        grid=(n // tq,),
        in_specs=[
            pl.BlockSpec((tq, width), lambda i, length: (i, 0)),
            pl.BlockSpec((m, 2 * width), lambda i, length: (0, 0)),
            pl.BlockSpec((tq, width), lambda i, length: (i, 0)),
            pl.BlockSpec((tq, heads), lambda i, length: (i, 0)),
        ],
        out_specs=[
            pl.BlockSpec((tq, width), lambda i, length: (i, 0)),
            pl.BlockSpec((tq, heads), lambda i, length: (i, 0)),
        ],
    )
    return pl.pallas_call(
        functools.partial(_attend_query_back_kernel, heads=heads, factor=factor),
        grid_spec=grid,
        out_shape=(
            jax.ShapeDtypeStruct((n, width), jnp.bfloat16),
            jax.ShapeDtypeStruct((n, heads), jnp.float32),
        ),
        compiler_params=pltpu.CompilerParams(dimension_semantics=("arbitrary",)),
        cost_estimate=pl.CostEstimate(
            flops=6 * n * m * width, transcendentals=n * m * heads,
            bytes_accessed=2 * (3 * n * width + 2 * m * width),
        ),
    )(length, q, kv, do, lse)


def _attend_key_back_kernel(length_ref, q_ref, kv_ref, do_ref, lse_ref, delta_ref, dkv_ref, *, heads, factor):
    @pl.when(pl.program_id(0) == 0)
    def _():
        dkv_ref[...] = jnp.zeros_like(dkv_ref)

    for h in range(heads):
        cols = slice(h * HEAD_DIM, (h + 1) * HEAD_DIM)
        vcols = slice((heads + h) * HEAD_DIM, (heads + h + 1) * HEAD_DIM)
        q = q_ref[:, cols]
        do = do_ref[:, cols]
        portion = jnp.exp(_scores(length_ref, q, kv_ref[:, cols], factor) - lse_ref[:, h : h + 1])
        dportion = lax.dot_general(
            do, kv_ref[:, vcols], (((1,), (1,)), ((), ())), preferred_element_type=jnp.float32
        )
        dkv_ref[:, vcols] += lax.dot_general(
            portion.astype(jnp.bfloat16), do, (((0,), (0,)), ((), ())), preferred_element_type=jnp.float32
        )
        dscores = (portion * (dportion - delta_ref[:, h : h + 1])).astype(jnp.bfloat16)
        dkv_ref[:, cols] += (
            lax.dot_general(dscores, q, (((0,), (0,)), ((), ())), preferred_element_type=jnp.float32) * factor
        )


def attend_key_back(length, q, kv, do, lse, delta, factor):
    n, width = q.shape
    m = kv.shape[0]
    heads = width // HEAD_DIM
    tq = min(KEY_SIDE_TILE, n)
    grid = pltpu.PrefetchScalarGridSpec(
        num_scalar_prefetch=1,
        grid=(n // tq,),
        in_specs=[
            pl.BlockSpec((tq, width), lambda i, length: (i, 0)),
            pl.BlockSpec((m, 2 * width), lambda i, length: (0, 0)),
            pl.BlockSpec((tq, width), lambda i, length: (i, 0)),
            pl.BlockSpec((tq, heads), lambda i, length: (i, 0)),
            pl.BlockSpec((tq, heads), lambda i, length: (i, 0)),
        ],
        out_specs=pl.BlockSpec((m, 2 * width), lambda i, length: (0, 0)),
    )
    return pl.pallas_call(
        functools.partial(_attend_key_back_kernel, heads=heads, factor=factor),
        grid_spec=grid,
        out_shape=jax.ShapeDtypeStruct((m, 2 * width), jnp.float32),
        compiler_params=pltpu.CompilerParams(dimension_semantics=("arbitrary",)),
        cost_estimate=pl.CostEstimate(
            flops=8 * n * m * width, transcendentals=n * m * heads,
            bytes_accessed=2 * (2 * n * width + 2 * m * width) + 4 * 2 * m * width,
        ),
    )(length, q, kv, do, lse, delta)


def tp_sum(value):
    if lax.axis_size("tp") == 2:
        return value + lax.ppermute(value, "tp", [(0, 1), (1, 0)])
    return lax.psum(value, "tp")


def tp_gather(value):
    if lax.axis_size("tp") == 2:
        other = lax.ppermute(value, "tp", [(0, 1), (1, 0)])
        first = lax.axis_index("tp") == 0
        return jnp.stack([jnp.where(first, value, other), jnp.where(first, other, value)])
    return lax.all_gather(value, "tp")


def split_exact(value):
    high = lax.reduce_precision(value, exponent_bits=8, mantissa_bits=7)
    rest = value - high
    middle = lax.reduce_precision(rest, exponent_bits=8, mantissa_bits=7)
    low = lax.reduce_precision(rest - middle, exponent_bits=8, mantissa_bits=7)
    return jnp.concatenate([high, middle, low], axis=-1).astype(jnp.bfloat16)


def join_exact(pieces):
    width = pieces.shape[-1] // 3
    parts = pieces.astype(jnp.float32)
    return (parts[..., :width] + parts[..., width : 2 * width]) + parts[..., 2 * width :]


def shard_send(value, axis="shard"):
    count = lax.axis_size(axis)
    if count > 8:
        return [lax.all_gather(value, axis, axis=0, tiled=True)]
    return [
        lax.ppermute(value, axis, [(j, (j + shift) % count) for j in range(count)])
        for shift in range(1, count)
    ]


def shard_assemble(value, arrived, axis="shard"):
    count = lax.axis_size(axis)
    if count > 8:
        return arrived[0]
    place = lax.axis_index(axis)
    rows = value.shape[0]
    out = jnp.zeros((count * rows,) + value.shape[1:], value.dtype)
    out = lax.dynamic_update_slice_in_dim(out, value, place * rows, 0)
    for shift, piece in enumerate(arrived, start=1):
        out = lax.dynamic_update_slice_in_dim(out, piece, ((place - shift) % count) * rows, 0)
    return out


def shard_gather(value, axis="shard"):
    return shard_assemble(value, shard_send(value, axis), axis)


def shard_scatter(value, axis="shard"):
    count = lax.axis_size(axis)
    if count > 8:
        return lax.psum_scatter(value, axis, scatter_dimension=0, tiled=True).astype(jnp.float32)
    place = lax.axis_index(axis)
    rows = value.shape[0] // count
    total = lax.dynamic_slice_in_dim(value, place * rows, rows, 0).astype(jnp.float32)
    for shift in range(1, count):
        outgoing = lax.dynamic_slice_in_dim(value, ((place + shift) % count) * rows, rows, 0)
        arrived = lax.ppermute(outgoing, axis, [(j, (j + shift) % count) for j in range(count)])
        total = total + arrived.astype(jnp.float32)
    return total


def on_device(
    tokens,
    seq_lengths,
    query_weight,
    query_bias,
    key_weight,
    value_weight,
    value_bias,
    output_weight,
    output_bias,
    attn_gain,
    attn_shift,
    inner_weight,
    inner_bias,
    outer_weight,
    outer_bias,
    final_gain,
    final_shift,
    upstream,
):
    row_count, model_width = tokens.shape
    tensor_place = lax.axis_index("tp")
    tensor_count = lax.axis_size("tp")
    head_width = query_weight.shape[1]
    hidden_width = inner_weight.shape[1]
    head_count = head_width // HEAD_DIM
    factor = HEAD_DIM ** (-0.5)
    f32 = jnp.float32

    qb = query_bias.shape[0]
    ib = inner_bias.shape[0]
    piece = output_bias.shape[0]
    tp_blocks = tp_gather(jnp.concatenate([query_bias, value_bias, inner_bias]))
    bias_columns = jnp.concatenate(
        [
            tp_blocks[:, :qb].reshape(piece, 1),
            tp_blocks[:, qb : 2 * qb].reshape(piece, 1),
            tp_blocks[:, 2 * qb :].reshape(piece, -1),
        ],
        axis=1,
    )
    shard_columns = jnp.stack(
        [output_bias, attn_gain, attn_shift, outer_bias, final_gain, final_shift], axis=1
    )
    kv_vec_full = shard_gather(
        jnp.concatenate([key_weight, value_weight, shard_columns, bias_columns], axis=1)
    )
    query_full = shard_gather(query_weight)
    vector_full = kv_vec_full[:, 2 * head_width :]
    key_full = kv_vec_full[:, :head_width]
    value_full = kv_vec_full[:, head_width : 2 * head_width]
    qkv_full = jnp.concatenate([query_full, kv_vec_full[:, : 2 * head_width]], axis=1)
    rest_local = jnp.concatenate([output_weight, inner_weight, outer_weight], axis=1)
    rest_arrived = shard_send(rest_local)

    full_vectors = vector_full[:, :6].T.astype(f32)
    outbias_full, gain_first, shift_first, outerbias_full, gain_second, shift_second = full_vectors
    qbias_all = vector_full[:, 6]
    vbias_all = vector_full[:, 7]
    ibias_all = vector_full[:, 8:].reshape(-1)
    query_shift = lax.dynamic_slice_in_dim(qbias_all, tensor_place * head_width, head_width).astype(f32)
    value_shift = lax.dynamic_slice_in_dim(vbias_all, tensor_place * head_width, head_width).astype(f32)
    inner_shift = lax.dynamic_slice_in_dim(ibias_all, tensor_place * hidden_width, hidden_width).astype(f32)

    projected = jnp.dot(tokens, kv_vec_full[:, : 2 * head_width], preferred_element_type=f32)
    key_local = projected[:, :head_width].astype(jnp.bfloat16)
    value_local = (projected[:, head_width:] + value_shift).astype(jnp.bfloat16)
    query = (jnp.dot(tokens, query_full, preferred_element_type=f32) + query_shift).astype(
        jnp.bfloat16
    )
    chunk_heads = 2 if head_count % 2 == 0 else 1
    chunk_width = chunk_heads * HEAD_DIM
    kv_chunks = []
    own_chunks = []
    for c in range(head_count // chunk_heads):
        columns = slice(c * chunk_width, (c + 1) * chunk_width)
        outgoing = jnp.concatenate([key_local[:, columns], value_local[:, columns]], axis=1)
        own_chunks.append(outgoing)
        kv_chunks.append(lax.all_gather(outgoing, "ctx", axis=0, tiled=True))
    query_all = lax.all_gather(query, "ctx", axis=0, tiled=True)
    chunk_outs = [
        attend(seq_lengths, query[:, c * chunk_width : (c + 1) * chunk_width], chunk, factor)
        for c, chunk in enumerate(kv_chunks)
    ]
    context = jnp.concatenate([o[0] for o in chunk_outs], axis=1)
    rest_arrived, context = lax.optimization_barrier((rest_arrived, context))
    rest_full = shard_assemble(rest_local, rest_arrived)
    output_full = rest_full[:, :head_width]
    inner_full = rest_full[:, head_width : head_width + hidden_width]
    outer_full = rest_full[:, head_width + hidden_width :]
    attn_part = jnp.einsum("th,oh->to", context, output_full, preferred_element_type=f32)
    attended = tp_sum(attn_part) + outbias_full
    normal_first, inverse_first = norm_parts(tokens.astype(f32) + attended)
    normed = normal_first * gain_first + shift_first
    normed_low = normed.astype(jnp.bfloat16)
    hidden = jnp.dot(normed_low, inner_full, preferred_element_type=f32) + inner_shift
    active = exact_gelu(hidden).astype(jnp.bfloat16)
    branch_part = jnp.einsum("tf,of->to", active, outer_full, preferred_element_type=f32)
    branch = tp_sum(branch_part) + outerbias_full
    normal_second, inverse_second = norm_parts(normed + branch)
    layer_out = (normal_second * gain_second + shift_second).astype(jnp.bfloat16)

    dres_second, final_gain_part, final_shift_part = norm_back(
        upstream.astype(f32), normal_second, inverse_second, gain_second
    )
    dbranch = dres_second.astype(jnp.bfloat16)
    outer_bias_part = jnp.sum(dbranch.astype(f32), 0)
    outer_weight_part = jnp.einsum("to,tf->of", dbranch, active, preferred_element_type=f32)
    dactive = jnp.dot(dbranch, outer_full, preferred_element_type=f32)
    unused, gelu_pull = jax.vjp(exact_gelu, hidden)
    dhidden = gelu_pull(dactive)[0].astype(jnp.bfloat16)
    inner_weight_part = jnp.einsum("td,tf->df", normed_low, dhidden, preferred_element_type=f32)
    inner_bias_part = jnp.sum(dhidden.astype(f32), 0)
    dnormed_part = jnp.einsum("tf,df->td", dhidden, inner_full, preferred_element_type=f32)
    dnormed = dres_second + tp_sum(dnormed_part)
    dres_first, attn_gain_part, attn_shift_part = norm_back(
        dnormed, normal_first, inverse_first, gain_first
    )
    dattended = dres_first.astype(jnp.bfloat16)
    output_bias_part = jnp.sum(dattended.astype(f32), 0)
    output_weight_part = jnp.einsum("to,th->oh", dattended, context, preferred_element_type=f32)
    dcontext = jnp.dot(dattended, output_full, preferred_element_type=f32).astype(jnp.bfloat16)

    low = jnp.bfloat16
    rows = model_width
    early = jnp.concatenate(
        [
            output_weight_part,
            inner_weight_part,
            outer_weight_part,
            jnp.stack(
                [output_bias_part, attn_gain_part, attn_shift_part, outer_bias_part,
                 final_gain_part, final_shift_part],
                axis=1,
            ),
            tp_gather(inner_bias_part).reshape(rows, -1),
        ],
        axis=1,
    ).astype(low)
    early_scattered = lax.psum_scatter(early, "shard", scatter_dimension=0, tiled=True)
    local_rows = piece // tensor_count

    own_length = seq_lengths - lax.axis_index("ctx") * row_count
    ctx_count = lax.axis_size("ctx")
    query_backs = []
    key_backs = []
    for c, chunk in enumerate(kv_chunks):
        pair = slice(c * chunk_width, (c + 1) * chunk_width)
        dquery_pair, delta_pair = attend_query_back(
            seq_lengths, query[:, pair], chunk, dcontext[:, pair], chunk_outs[c][1], factor
        )
        query_backs.append(dquery_pair)
        stats = split_exact(jnp.concatenate([chunk_outs[c][1], delta_pair], axis=1))
        stats_rows = stats.size // chunk_width
        padded_rows = -(-stats_rows // 16) * 16
        payload = jnp.concatenate(
            [
                dcontext[:, pair],
                stats.reshape(stats_rows, chunk_width),
                jnp.zeros((padded_rows - stats_rows, chunk_width), jnp.bfloat16),
            ],
            axis=0,
        )
        arrived = shard_gather(payload, "ctx").reshape(
            ctx_count, row_count + padded_rows, chunk_width
        )
        dcontext_pair_all = arrived[:, :row_count].reshape(ctx_count * row_count, chunk_width)
        stats_all = join_exact(
            arrived[:, row_count : row_count + stats_rows].reshape(
                ctx_count * row_count, stats.shape[1]
            )
        )
        own = own_chunks[c]
        if key_backs:
            if len(key_backs) == 1:
                early_scattered, own, key_backs[-1] = lax.optimization_barrier(
                    (early_scattered, own, key_backs[-1])
                )
                early_piece = lax.psum(early_scattered, "ctx")
            else:
                own, key_backs[-1] = lax.optimization_barrier((own, key_backs[-1]))
        elif len(kv_chunks) == 1:
            early_piece = lax.psum(early_scattered, "ctx")
        key_backs.append(
            attend_key_back(
                own_length,
                query_all[:, pair],
                own,
                dcontext_pair_all,
                stats_all[:, :chunk_heads],
                stats_all[:, chunk_heads:],
                factor,
            )
        )
    dquery = jnp.concatenate(query_backs, axis=1)
    dkeys = jnp.concatenate([back[:, :chunk_width] for back in key_backs], axis=1).astype(low)
    dvalues = jnp.concatenate([back[:, chunk_width:] for back in key_backs], axis=1).astype(low)
    early_piece = early_piece.astype(f32)
    output_total = early_piece[:, :head_width]
    inner_total = early_piece[:, head_width : head_width + hidden_width]
    outer_total = early_piece[:, head_width + hidden_width : head_width + 2 * hidden_width]
    early_vectors = early_piece[:, head_width + 2 * hidden_width :]
    outbias_total, attn_gain_total, attn_shift_total, outerbias_total, final_gain_total, final_shift_total = (
        early_vectors[:, :6].T
    )
    ibias_total = lax.dynamic_slice_in_dim(
        early_vectors[:, 6:], tensor_place * local_rows, local_rows, 0
    ).reshape(-1)
    dqkv = jnp.concatenate([dquery, dkeys, dvalues], axis=1)
    query_bias_part = jnp.sum(dquery.astype(f32), 0)
    value_bias_part = jnp.sum(dvalues.astype(f32), 0)
    dinput_part = jnp.einsum("th,dh->td", dqkv, qkv_full, preferred_element_type=f32)
    tokens_gradient = dres_first + tp_sum(dinput_part)
    query_side = jnp.concatenate(
        [
            jnp.einsum("td,th->dh", tokens, dquery, preferred_element_type=f32),
            tp_gather(query_bias_part).reshape(rows, 1),
        ],
        axis=1,
    ).astype(low)
    query_scattered = shard_scatter(query_side).astype(low)
    query_scattered, early_piece = lax.optimization_barrier((query_scattered, early_piece))
    query_piece = lax.psum(query_scattered, "ctx").astype(f32)
    key_side = jnp.concatenate(
        [
            jnp.einsum("td,th->dh", tokens, jnp.concatenate([dkeys, dvalues], axis=1),
                       preferred_element_type=f32),
            tp_gather(value_bias_part).reshape(rows, 1),
        ],
        axis=1,
    ).astype(low)
    key_scattered = shard_scatter(key_side).astype(low)
    key_scattered, query_piece = lax.optimization_barrier((key_scattered, query_piece))
    key_piece = lax.psum(key_scattered, "ctx").astype(f32)
    query_total = query_piece[:, :head_width]
    key_total = key_piece[:, :head_width]
    value_total = key_piece[:, head_width : 2 * head_width]
    qbias_total = lax.dynamic_slice_in_dim(
        query_piece[:, head_width], tensor_place * local_rows, local_rows
    )
    vbias_total = lax.dynamic_slice_in_dim(
        key_piece[:, 2 * head_width], tensor_place * local_rows, local_rows
    )
    return (
        layer_out,
        tokens_gradient,
        query_total,
        qbias_total,
        key_total,
        value_total,
        vbias_total,
        output_total,
        outbias_total,
        attn_gain_total,
        attn_shift_total,
        inner_total,
        ibias_total,
        outer_total,
        outerbias_total,
        final_gain_total,
        final_shift_total,
    )


def solution(mesh):
    placed = (
        P(("shard", "ctx"), None),
        P("shard"),
        P("shard", "tp"),
        P(("shard", "tp")),
        P("shard", "tp"),
        P("shard", "tp"),
        P(("shard", "tp")),
        P("shard", "tp"),
        P("shard"),
        P("shard"),
        P("shard"),
        P("shard", "tp"),
        P(("shard", "tp")),
        P("shard", "tp"),
        P("shard"),
        P("shard"),
        P("shard"),
        P(("shard", "ctx"), None),
    )
    return jax.shard_map(
        on_device,
        mesh=mesh,
        in_specs=placed,
        out_specs=(
            P(("shard", "ctx"), None),
            P(("shard", "ctx"), None),
            P("shard", "tp"),
            P(("shard", "tp")),
            P("shard", "tp"),
            P("shard", "tp"),
            P(("shard", "tp")),
            P("shard", "tp"),
            P("shard"),
            P("shard"),
            P("shard"),
            P("shard", "tp"),
            P(("shard", "tp")),
            P("shard", "tp"),
            P("shard"),
            P("shard"),
            P("shard"),
        ),
        check_vma=False,
    )
```

```python
import functools

import jax
import jax.numpy as jnp
from jax import lax
from jax.experimental import pallas as pl
from jax.experimental.pallas import tpu as pltpu
from jax.sharding import PartitionSpec as P

HEAD_DIM = 64
QUERY_TILE = 128
KEY_SIDE_TILE = 256


def _scores(length_ref, q, k, factor):
    s = lax.dot_general(q, k, (((1,), (1,)), ((), ())), preferred_element_type=jnp.float32) * factor
    keys = lax.broadcasted_iota(jnp.int32, s.shape, 1)
    return jnp.where(keys < length_ref[0], s, -1e30)


def _attend_kernel(length_ref, q_ref, kv_ref, o_ref, lse_ref, *, heads, factor):
    for h in range(heads):
        cols = slice(h * HEAD_DIM, (h + 1) * HEAD_DIM)
        vcols = slice((heads + h) * HEAD_DIM, (heads + h + 1) * HEAD_DIM)
        s = _scores(length_ref, q_ref[:, cols], kv_ref[:, cols], factor)
        highest = jnp.max(s, axis=1, keepdims=True)
        shifted = jnp.exp(s - highest)
        summed = jnp.sum(shifted, axis=1, keepdims=True)
        portion = (shifted / summed).astype(jnp.bfloat16)
        mixed = jnp.dot(portion, kv_ref[:, vcols], preferred_element_type=jnp.float32)
        o_ref[:, cols] = mixed.astype(o_ref.dtype)
        lse_ref[:, h : h + 1] = highest + jnp.log(summed)


def attend(length, q, kv, factor):
    n, width = q.shape
    m = kv.shape[0]
    heads = width // HEAD_DIM
    tq = min(QUERY_TILE, n)
    grid = pltpu.PrefetchScalarGridSpec(
        num_scalar_prefetch=1,
        grid=(n // tq,),
        in_specs=[
            pl.BlockSpec((tq, width), lambda i, length: (i, 0)),
            pl.BlockSpec((m, 2 * width), lambda i, length: (0, 0)),
        ],
        out_specs=[
            pl.BlockSpec((tq, width), lambda i, length: (i, 0)),
            pl.BlockSpec((tq, heads), lambda i, length: (i, 0)),
        ],
    )
    flops = 4 * n * m * width
    return pl.pallas_call(
        functools.partial(_attend_kernel, heads=heads, factor=factor),
        grid_spec=grid,
        out_shape=(
            jax.ShapeDtypeStruct((n, width), jnp.bfloat16),
            jax.ShapeDtypeStruct((n, heads), jnp.float32),
        ),
        compiler_params=pltpu.CompilerParams(dimension_semantics=("arbitrary",)),
        cost_estimate=pl.CostEstimate(
            flops=flops, transcendentals=n * m * heads, bytes_accessed=2 * (2 * n * width + 2 * m * width)
        ),
    )(length, q, kv)


def _attend_back_kernel(length_ref, q_ref, kv_ref, do_ref, lse_ref, dq_ref, dkv_ref, *, heads, factor):
    @pl.when(pl.program_id(0) == 0)
    def _():
        dkv_ref[...] = jnp.zeros_like(dkv_ref)

    for h in range(heads):
        cols = slice(h * HEAD_DIM, (h + 1) * HEAD_DIM)
        vcols = slice((heads + h) * HEAD_DIM, (heads + h + 1) * HEAD_DIM)
        q = q_ref[:, cols]
        k = kv_ref[:, cols]
        v = kv_ref[:, vcols]
        do = do_ref[:, cols]
        portion = jnp.exp(_scores(length_ref, q, k, factor) - lse_ref[:, h : h + 1])
        dportion = lax.dot_general(do, v, (((1,), (1,)), ((), ())), preferred_element_type=jnp.float32)
        dkv_ref[:, vcols] += lax.dot_general(
            portion.astype(jnp.bfloat16), do, (((0,), (0,)), ((), ())), preferred_element_type=jnp.float32
        )
        centering = jnp.sum(portion * dportion, axis=1, keepdims=True)
        dscores = (portion * (dportion - centering)).astype(jnp.bfloat16)
        dq_ref[:, cols] = (
            jnp.dot(dscores, k, preferred_element_type=jnp.float32) * factor
        ).astype(dq_ref.dtype)
        dkv_ref[:, cols] += (
            lax.dot_general(dscores, q, (((0,), (0,)), ((), ())), preferred_element_type=jnp.float32) * factor
        )


def attend_back(length, q, kv, do, lse, factor):
    n, width = q.shape
    m = kv.shape[0]
    heads = width // HEAD_DIM
    tq = min(QUERY_TILE, n)
    grid = pltpu.PrefetchScalarGridSpec(
        num_scalar_prefetch=1,
        grid=(n // tq,),
        in_specs=[
            pl.BlockSpec((tq, width), lambda i, length: (i, 0)),
            pl.BlockSpec((m, 2 * width), lambda i, length: (0, 0)),
            pl.BlockSpec((tq, width), lambda i, length: (i, 0)),
            pl.BlockSpec((tq, heads), lambda i, length: (i, 0)),
        ],
        out_specs=[
            pl.BlockSpec((tq, width), lambda i, length: (i, 0)),
            pl.BlockSpec((m, 2 * width), lambda i, length: (0, 0)),
        ],
    )
    flops = 10 * n * m * width
    return pl.pallas_call(
        functools.partial(_attend_back_kernel, heads=heads, factor=factor),
        grid_spec=grid,
        out_shape=(
            jax.ShapeDtypeStruct((n, width), jnp.bfloat16),
            jax.ShapeDtypeStruct((m, 2 * width), jnp.float32),
        ),
        compiler_params=pltpu.CompilerParams(dimension_semantics=("arbitrary",)),
        cost_estimate=pl.CostEstimate(
            flops=flops, transcendentals=n * m * heads,
            bytes_accessed=2 * (3 * n * width + 2 * m * width) + 4 * 2 * m * width,
        ),
    )(length, q, kv, do, lse)


EPSILON = 1e-12


def norm_parts(hidden):
    center = hidden - jnp.mean(hidden, -1, keepdims=True)
    inverse = lax.rsqrt(jnp.mean(center * center, -1, keepdims=True) + EPSILON)
    return (center * inverse, inverse)


def norm_back(gradient, normal_form, inverse, gain):
    scaled = gradient * gain
    inner = (
        scaled
        - jnp.mean(scaled, -1, keepdims=True)
        - normal_form * jnp.mean(scaled * normal_form, -1, keepdims=True)
    )
    return (inner * inverse, jnp.sum(gradient * normal_form, 0), jnp.sum(gradient, 0))


def exact_gelu(values):
    return jax.nn.gelu(values, approximate=False)


def _attend_query_back_kernel(length_ref, q_ref, kv_ref, do_ref, lse_ref, dq_ref, delta_ref, *, heads, factor):
    for h in range(heads):
        cols = slice(h * HEAD_DIM, (h + 1) * HEAD_DIM)
        vcols = slice((heads + h) * HEAD_DIM, (heads + h + 1) * HEAD_DIM)
        k = kv_ref[:, cols]
        do = do_ref[:, cols]
        portion = jnp.exp(_scores(length_ref, q_ref[:, cols], k, factor) - lse_ref[:, h : h + 1])
        dportion = lax.dot_general(
            do, kv_ref[:, vcols], (((1,), (1,)), ((), ())), preferred_element_type=jnp.float32
        )
        centering = jnp.sum(portion * dportion, axis=1, keepdims=True)
        dscores = (portion * (dportion - centering)).astype(jnp.bfloat16)
        dq_ref[:, cols] = (
            jnp.dot(dscores, k, preferred_element_type=jnp.float32) * factor
        ).astype(dq_ref.dtype)
        delta_ref[:, h : h + 1] = centering


def attend_query_back(length, q, kv, do, lse, factor):
    n, width = q.shape
    m = kv.shape[0]
    heads = width // HEAD_DIM
    tq = min(QUERY_TILE, n)
    grid = pltpu.PrefetchScalarGridSpec(
        num_scalar_prefetch=1,
        grid=(n // tq,),
        in_specs=[
            pl.BlockSpec((tq, width), lambda i, length: (i, 0)),
            pl.BlockSpec((m, 2 * width), lambda i, length: (0, 0)),
            pl.BlockSpec((tq, width), lambda i, length: (i, 0)),
            pl.BlockSpec((tq, heads), lambda i, length: (i, 0)),
        ],
        out_specs=[
            pl.BlockSpec((tq, width), lambda i, length: (i, 0)),
            pl.BlockSpec((tq, heads), lambda i, length: (i, 0)),
        ],
    )
    return pl.pallas_call(
        functools.partial(_attend_query_back_kernel, heads=heads, factor=factor),
        grid_spec=grid,
        out_shape=(
            jax.ShapeDtypeStruct((n, width), jnp.bfloat16),
            jax.ShapeDtypeStruct((n, heads), jnp.float32),
        ),
        compiler_params=pltpu.CompilerParams(dimension_semantics=("arbitrary",)),
        cost_estimate=pl.CostEstimate(
            flops=6 * n * m * width, transcendentals=n * m * heads,
            bytes_accessed=2 * (3 * n * width + 2 * m * width),
        ),
    )(length, q, kv, do, lse)


def _attend_key_back_kernel(length_ref, q_ref, kv_ref, do_ref, lse_ref, delta_ref, dkv_ref, *, heads, factor):
    @pl.when(pl.program_id(0) == 0)
    def _():
        dkv_ref[...] = jnp.zeros_like(dkv_ref)

    for h in range(heads):
        cols = slice(h * HEAD_DIM, (h + 1) * HEAD_DIM)
        vcols = slice((heads + h) * HEAD_DIM, (heads + h + 1) * HEAD_DIM)
        q = q_ref[:, cols]
        do = do_ref[:, cols]
        portion = jnp.exp(_scores(length_ref, q, kv_ref[:, cols], factor) - lse_ref[:, h : h + 1])
        dportion = lax.dot_general(
            do, kv_ref[:, vcols], (((1,), (1,)), ((), ())), preferred_element_type=jnp.float32
        )
        dkv_ref[:, vcols] += lax.dot_general(
            portion.astype(jnp.bfloat16), do, (((0,), (0,)), ((), ())), preferred_element_type=jnp.float32
        )
        dscores = (portion * (dportion - delta_ref[:, h : h + 1])).astype(jnp.bfloat16)
        dkv_ref[:, cols] += (
            lax.dot_general(dscores, q, (((0,), (0,)), ((), ())), preferred_element_type=jnp.float32) * factor
        )


def attend_key_back(length, q, kv, do, lse, delta, factor):
    n, width = q.shape
    m = kv.shape[0]
    heads = width // HEAD_DIM
    tq = min(KEY_SIDE_TILE, n)
    grid = pltpu.PrefetchScalarGridSpec(
        num_scalar_prefetch=1,
        grid=(n // tq,),
        in_specs=[
            pl.BlockSpec((tq, width), lambda i, length: (i, 0)),
            pl.BlockSpec((m, 2 * width), lambda i, length: (0, 0)),
            pl.BlockSpec((tq, width), lambda i, length: (i, 0)),
            pl.BlockSpec((tq, heads), lambda i, length: (i, 0)),
            pl.BlockSpec((tq, heads), lambda i, length: (i, 0)),
        ],
        out_specs=pl.BlockSpec((m, 2 * width), lambda i, length: (0, 0)),
    )
    return pl.pallas_call(
        functools.partial(_attend_key_back_kernel, heads=heads, factor=factor),
        grid_spec=grid,
        out_shape=jax.ShapeDtypeStruct((m, 2 * width), jnp.float32),
        compiler_params=pltpu.CompilerParams(dimension_semantics=("arbitrary",)),
        cost_estimate=pl.CostEstimate(
            flops=8 * n * m * width, transcendentals=n * m * heads,
            bytes_accessed=2 * (2 * n * width + 2 * m * width) + 4 * 2 * m * width,
        ),
    )(length, q, kv, do, lse, delta)


def tp_sum(value):
    if lax.axis_size("tp") == 2:
        return value + lax.ppermute(value, "tp", [(0, 1), (1, 0)])
    return lax.psum(value, "tp")


def tp_gather(value):
    if lax.axis_size("tp") == 2:
        other = lax.ppermute(value, "tp", [(0, 1), (1, 0)])
        first = lax.axis_index("tp") == 0
        return jnp.stack([jnp.where(first, value, other), jnp.where(first, other, value)])
    return lax.all_gather(value, "tp")


def split_exact(value):
    high = lax.reduce_precision(value, exponent_bits=8, mantissa_bits=7)
    rest = value - high
    middle = lax.reduce_precision(rest, exponent_bits=8, mantissa_bits=7)
    low = lax.reduce_precision(rest - middle, exponent_bits=8, mantissa_bits=7)
    return jnp.concatenate([high, middle, low], axis=-1).astype(jnp.bfloat16)


def join_exact(pieces):
    width = pieces.shape[-1] // 3
    parts = pieces.astype(jnp.float32)
    return (parts[..., :width] + parts[..., width : 2 * width]) + parts[..., 2 * width :]


def shard_send(value, axis="shard"):
    count = lax.axis_size(axis)
    if count > 8:
        return [lax.all_gather(value, axis, axis=0, tiled=True)]
    return [
        lax.ppermute(value, axis, [(j, (j + shift) % count) for j in range(count)])
        for shift in range(1, count)
    ]


def shard_assemble(value, arrived, axis="shard"):
    count = lax.axis_size(axis)
    if count > 8:
        return arrived[0]
    place = lax.axis_index(axis)
    rows = value.shape[0]
    out = jnp.zeros((count * rows,) + value.shape[1:], value.dtype)
    out = lax.dynamic_update_slice_in_dim(out, value, place * rows, 0)
    for shift, piece in enumerate(arrived, start=1):
        out = lax.dynamic_update_slice_in_dim(out, piece, ((place - shift) % count) * rows, 0)
    return out


def shard_gather(value, axis="shard"):
    return shard_assemble(value, shard_send(value, axis), axis)


def shard_scatter(value, axis="shard"):
    count = lax.axis_size(axis)
    if count > 8:
        return lax.psum_scatter(value, axis, scatter_dimension=0, tiled=True).astype(jnp.float32)
    place = lax.axis_index(axis)
    rows = value.shape[0] // count
    total = lax.dynamic_slice_in_dim(value, place * rows, rows, 0).astype(jnp.float32)
    for shift in range(1, count):
        outgoing = lax.dynamic_slice_in_dim(value, ((place + shift) % count) * rows, rows, 0)
        arrived = lax.ppermute(outgoing, axis, [(j, (j + shift) % count) for j in range(count)])
        total = total + arrived.astype(jnp.float32)
    return total


def on_device(
    tokens,
    seq_lengths,
    query_weight,
    query_bias,
    key_weight,
    value_weight,
    value_bias,
    output_weight,
    output_bias,
    attn_gain,
    attn_shift,
    inner_weight,
    inner_bias,
    outer_weight,
    outer_bias,
    final_gain,
    final_shift,
    upstream,
):
    row_count, model_width = tokens.shape
    tensor_place = lax.axis_index("tp")
    tensor_count = lax.axis_size("tp")
    head_width = query_weight.shape[1]
    hidden_width = inner_weight.shape[1]
    head_count = head_width // HEAD_DIM
    factor = HEAD_DIM ** (-0.5)
    f32 = jnp.float32

    qb = query_bias.shape[0]
    ib = inner_bias.shape[0]
    piece = output_bias.shape[0]
    tp_blocks = tp_gather(jnp.concatenate([query_bias, value_bias, inner_bias]))
    bias_columns = jnp.concatenate(
        [
            tp_blocks[:, :qb].reshape(piece, 1),
            tp_blocks[:, qb : 2 * qb].reshape(piece, 1),
            tp_blocks[:, 2 * qb :].reshape(piece, -1),
        ],
        axis=1,
    )
    shard_columns = jnp.stack(
        [output_bias, attn_gain, attn_shift, outer_bias, final_gain, final_shift], axis=1
    )
    piece_rows = key_weight.shape[0]
    kv_local = jnp.concatenate(
        [key_weight, value_weight, shard_columns, bias_columns], axis=1
    )
    kv_arrived = shard_send(kv_local)
    query_full = shard_gather(query_weight)
    kv_vec_full = shard_assemble(kv_local, kv_arrived)
    vector_full = shard_assemble(
        kv_local[:, 2 * head_width :], [arrived[:, 2 * head_width :] for arrived in kv_arrived]
    ) if lax.axis_size("shard") <= 8 else kv_vec_full[:, 2 * head_width :]
    qkv_full = jnp.concatenate([query_full, kv_vec_full[:, : 2 * head_width]], axis=1)
    rest_local = jnp.concatenate([output_weight, inner_weight, outer_weight], axis=1)
    rest_arrived = shard_send(rest_local)

    full_vectors = vector_full[:, :6].T.astype(f32)
    outbias_full, gain_first, shift_first, outerbias_full, gain_second, shift_second = full_vectors
    qbias_all = vector_full[:, 6]
    vbias_all = vector_full[:, 7]
    ibias_all = vector_full[:, 8:].reshape(-1)
    query_shift = lax.dynamic_slice_in_dim(qbias_all, tensor_place * head_width, head_width).astype(f32)
    value_shift = lax.dynamic_slice_in_dim(vbias_all, tensor_place * head_width, head_width).astype(f32)
    inner_shift = lax.dynamic_slice_in_dim(ibias_all, tensor_place * hidden_width, hidden_width).astype(f32)

    shard_count = lax.axis_size("shard")
    if shard_count <= 8:
        shard_place = lax.axis_index("shard")
        projected = None
        for shift, weight_piece in enumerate([kv_local] + kv_arrived):
            inputs = lax.dynamic_slice_in_dim(
                tokens, ((shard_place - shift) % shard_count) * piece_rows, piece_rows, 1
            )
            term = jnp.dot(inputs, weight_piece[:, : 2 * head_width], preferred_element_type=f32)
            projected = term if projected is None else projected + term
    else:
        projected = jnp.dot(tokens, kv_vec_full[:, : 2 * head_width], preferred_element_type=f32)
    key_local = projected[:, :head_width].astype(jnp.bfloat16)
    value_local = (projected[:, head_width:] + value_shift).astype(jnp.bfloat16)
    query = (jnp.dot(tokens, query_full, preferred_element_type=f32) + query_shift).astype(
        jnp.bfloat16
    )
    chunk_heads = 2 if head_count % 2 == 0 else 1
    chunk_width = chunk_heads * HEAD_DIM
    kv_chunks = []
    own_chunks = []
    for c in range(head_count // chunk_heads):
        columns = slice(c * chunk_width, (c + 1) * chunk_width)
        outgoing = jnp.concatenate([key_local[:, columns], value_local[:, columns]], axis=1)
        own_chunks.append(outgoing)
        kv_chunks.append(lax.all_gather(outgoing, "ctx", axis=0, tiled=True))
    query_all = lax.all_gather(query, "ctx", axis=0, tiled=True)
    chunk_outs = [
        attend(seq_lengths, query[:, c * chunk_width : (c + 1) * chunk_width], chunk, factor)
        for c, chunk in enumerate(kv_chunks)
    ]
    context = jnp.concatenate([o[0] for o in chunk_outs], axis=1)
    rest_arrived, context = lax.optimization_barrier((rest_arrived, context))
    rest_full = shard_assemble(rest_local, rest_arrived)
    output_full = rest_full[:, :head_width]
    inner_full = rest_full[:, head_width : head_width + hidden_width]
    outer_full = rest_full[:, head_width + hidden_width :]
    attn_part = jnp.einsum("th,oh->to", context, output_full, preferred_element_type=f32)
    attended = tp_sum(attn_part) + outbias_full
    normal_first, inverse_first = norm_parts(tokens.astype(f32) + attended)
    normed = normal_first * gain_first + shift_first
    normed_low = normed.astype(jnp.bfloat16)
    hidden = jnp.dot(normed_low, inner_full, preferred_element_type=f32) + inner_shift
    active = exact_gelu(hidden).astype(jnp.bfloat16)
    branch_part = jnp.einsum("tf,of->to", active, outer_full, preferred_element_type=f32)
    branch = tp_sum(branch_part) + outerbias_full
    normal_second, inverse_second = norm_parts(normed + branch)
    layer_out = (normal_second * gain_second + shift_second).astype(jnp.bfloat16)

    dres_second, final_gain_part, final_shift_part = norm_back(
        upstream.astype(f32), normal_second, inverse_second, gain_second
    )
    dbranch = dres_second.astype(jnp.bfloat16)
    outer_bias_part = jnp.sum(dbranch.astype(f32), 0)
    outer_weight_part = jnp.einsum("to,tf->of", dbranch, active, preferred_element_type=f32)
    dactive = jnp.dot(dbranch, outer_full, preferred_element_type=f32)
    unused, gelu_pull = jax.vjp(exact_gelu, hidden)
    dhidden = gelu_pull(dactive)[0].astype(jnp.bfloat16)
    inner_weight_part = jnp.einsum("td,tf->df", normed_low, dhidden, preferred_element_type=f32)
    inner_bias_part = jnp.sum(dhidden.astype(f32), 0)
    dnormed_part = jnp.einsum("tf,df->td", dhidden, inner_full, preferred_element_type=f32)
    dnormed = dres_second + tp_sum(dnormed_part)
    dres_first, attn_gain_part, attn_shift_part = norm_back(
        dnormed, normal_first, inverse_first, gain_first
    )
    dattended = dres_first.astype(jnp.bfloat16)
    output_bias_part = jnp.sum(dattended.astype(f32), 0)
    output_weight_part = jnp.einsum("to,th->oh", dattended, context, preferred_element_type=f32)
    dcontext = jnp.dot(dattended, output_full, preferred_element_type=f32).astype(jnp.bfloat16)

    low = jnp.bfloat16
    rows = model_width
    early = jnp.concatenate(
        [
            output_weight_part,
            inner_weight_part,
            outer_weight_part,
            jnp.stack(
                [output_bias_part, attn_gain_part, attn_shift_part, outer_bias_part,
                 final_gain_part, final_shift_part],
                axis=1,
            ),
            tp_gather(inner_bias_part).reshape(rows, -1),
        ],
        axis=1,
    ).astype(low)
    early_scattered = lax.psum_scatter(early, "shard", scatter_dimension=0, tiled=True)
    local_rows = piece // tensor_count

    own_length = seq_lengths - lax.axis_index("ctx") * row_count
    ctx_count = lax.axis_size("ctx")
    query_backs = []
    key_backs = []
    for c, chunk in enumerate(kv_chunks):
        pair = slice(c * chunk_width, (c + 1) * chunk_width)
        dquery_pair, delta_pair = attend_query_back(
            seq_lengths, query[:, pair], chunk, dcontext[:, pair], chunk_outs[c][1], factor
        )
        query_backs.append(dquery_pair)
        stats = split_exact(jnp.concatenate([chunk_outs[c][1], delta_pair], axis=1))
        stats_rows = stats.size // chunk_width
        padded_rows = -(-stats_rows // 16) * 16
        payload = jnp.concatenate(
            [
                dcontext[:, pair],
                stats.reshape(stats_rows, chunk_width),
                jnp.zeros((padded_rows - stats_rows, chunk_width), jnp.bfloat16),
            ],
            axis=0,
        )
        arrived = shard_gather(payload, "ctx").reshape(
            ctx_count, row_count + padded_rows, chunk_width
        )
        dcontext_pair_all = arrived[:, :row_count].reshape(ctx_count * row_count, chunk_width)
        stats_all = join_exact(
            arrived[:, row_count : row_count + stats_rows].reshape(
                ctx_count * row_count, stats.shape[1]
            )
        )
        own = own_chunks[c]
        if key_backs:
            if len(key_backs) == 1:
                early_scattered, own, key_backs[-1] = lax.optimization_barrier(
                    (early_scattered, own, key_backs[-1])
                )
                early_piece = lax.psum(early_scattered, "ctx")
            else:
                own, key_backs[-1] = lax.optimization_barrier((own, key_backs[-1]))
        elif len(kv_chunks) == 1:
            early_piece = lax.psum(early_scattered, "ctx")
        key_backs.append(
            attend_key_back(
                own_length,
                query_all[:, pair],
                own,
                dcontext_pair_all,
                stats_all[:, :chunk_heads],
                stats_all[:, chunk_heads:],
                factor,
            )
        )
    dquery = jnp.concatenate(query_backs, axis=1)
    dkeys = jnp.concatenate([back[:, :chunk_width] for back in key_backs], axis=1).astype(low)
    dvalues = jnp.concatenate([back[:, chunk_width:] for back in key_backs], axis=1).astype(low)
    early_piece = early_piece.astype(f32)
    output_total = early_piece[:, :head_width]
    inner_total = early_piece[:, head_width : head_width + hidden_width]
    outer_total = early_piece[:, head_width + hidden_width : head_width + 2 * hidden_width]
    early_vectors = early_piece[:, head_width + 2 * hidden_width :]
    outbias_total, attn_gain_total, attn_shift_total, outerbias_total, final_gain_total, final_shift_total = (
        early_vectors[:, :6].T
    )
    ibias_total = lax.dynamic_slice_in_dim(
        early_vectors[:, 6:], tensor_place * local_rows, local_rows, 0
    ).reshape(-1)
    dqkv = jnp.concatenate([dquery, dkeys, dvalues], axis=1)
    qkv_weight_part = jnp.einsum("td,th->dh", tokens, dqkv, preferred_element_type=f32)
    query_bias_part = jnp.sum(dquery.astype(f32), 0)
    value_bias_part = jnp.sum(dvalues.astype(f32), 0)
    dinput_part = jnp.einsum("th,dh->td", dqkv, qkv_full, preferred_element_type=f32)
    tokens_gradient = dres_first + tp_sum(dinput_part)
    late = jnp.concatenate(
        [
            qkv_weight_part,
            tp_gather(query_bias_part).reshape(rows, 1),
            tp_gather(value_bias_part).reshape(rows, 1),
        ],
        axis=1,
    ).astype(low)
    late, early_piece = lax.optimization_barrier((late, early_piece))
    late_piece = lax.psum(shard_scatter(late).astype(low), "ctx").astype(f32)
    query_total = late_piece[:, :head_width]
    key_total = late_piece[:, head_width : 2 * head_width]
    value_total = late_piece[:, 2 * head_width : 3 * head_width]
    qbias_total = lax.dynamic_slice_in_dim(
        late_piece[:, 3 * head_width], tensor_place * local_rows, local_rows
    )
    vbias_total = lax.dynamic_slice_in_dim(
        late_piece[:, 3 * head_width + 1], tensor_place * local_rows, local_rows
    )
    return (
        layer_out,
        tokens_gradient,
        query_total,
        qbias_total,
        key_total,
        value_total,
        vbias_total,
        output_total,
        outbias_total,
        attn_gain_total,
        attn_shift_total,
        inner_total,
        ibias_total,
        outer_total,
        outerbias_total,
        final_gain_total,
        final_shift_total,
    )


def solution(mesh):
    placed = (
        P(("shard", "ctx"), None),
        P("shard"),
        P("shard", "tp"),
        P(("shard", "tp")),
        P("shard", "tp"),
        P("shard", "tp"),
        P(("shard", "tp")),
        P("shard", "tp"),
        P("shard"),
        P("shard"),
        P("shard"),
        P("shard", "tp"),
        P(("shard", "tp")),
        P("shard", "tp"),
        P("shard"),
        P("shard"),
        P("shard"),
        P(("shard", "ctx"), None),
    )
    return jax.shard_map(
        on_device,
        mesh=mesh,
        in_specs=placed,
        out_specs=(
            P(("shard", "ctx"), None),
            P(("shard", "ctx"), None),
            P("shard", "tp"),
            P(("shard", "tp")),
            P("shard", "tp"),
            P("shard", "tp"),
            P(("shard", "tp")),
            P("shard", "tp"),
            P("shard"),
            P("shard"),
            P("shard"),
            P("shard", "tp"),
            P(("shard", "tp")),
            P("shard", "tp"),
            P("shard"),
            P("shard"),
            P("shard"),
        ),
        check_vma=False,
    )
```

```python
import functools

import jax
import jax.numpy as jnp
from jax import lax
from jax.experimental import pallas as pl
from jax.experimental.pallas import tpu as pltpu
from jax.sharding import PartitionSpec as P

HEAD_DIM = 64
QUERY_TILE = 128
KEY_SIDE_TILE = 256


def _scores(length_ref, q, k, factor):
    s = lax.dot_general(q, k, (((1,), (1,)), ((), ())), preferred_element_type=jnp.float32) * factor
    keys = lax.broadcasted_iota(jnp.int32, s.shape, 1)
    return jnp.where(keys < length_ref[0], s, -1e30)


def _attend_kernel(length_ref, q_ref, kv_ref, o_ref, lse_ref, *, heads, factor):
    for h in range(heads):
        cols = slice(h * HEAD_DIM, (h + 1) * HEAD_DIM)
        vcols = slice((heads + h) * HEAD_DIM, (heads + h + 1) * HEAD_DIM)
        s = _scores(length_ref, q_ref[:, cols], kv_ref[:, cols], factor)
        highest = jnp.max(s, axis=1, keepdims=True)
        shifted = jnp.exp(s - highest)
        summed = jnp.sum(shifted, axis=1, keepdims=True)
        portion = (shifted / summed).astype(jnp.bfloat16)
        mixed = jnp.dot(portion, kv_ref[:, vcols], preferred_element_type=jnp.float32)
        o_ref[:, cols] = mixed.astype(o_ref.dtype)
        lse_ref[:, h : h + 1] = highest + jnp.log(summed)


def attend(length, q, kv, factor):
    n, width = q.shape
    m = kv.shape[0]
    heads = width // HEAD_DIM
    tq = min(QUERY_TILE, n)
    grid = pltpu.PrefetchScalarGridSpec(
        num_scalar_prefetch=1,
        grid=(n // tq,),
        in_specs=[
            pl.BlockSpec((tq, width), lambda i, length: (i, 0)),
            pl.BlockSpec((m, 2 * width), lambda i, length: (0, 0)),
        ],
        out_specs=[
            pl.BlockSpec((tq, width), lambda i, length: (i, 0)),
            pl.BlockSpec((tq, heads), lambda i, length: (i, 0)),
        ],
    )
    flops = 4 * n * m * width
    return pl.pallas_call(
        functools.partial(_attend_kernel, heads=heads, factor=factor),
        grid_spec=grid,
        out_shape=(
            jax.ShapeDtypeStruct((n, width), jnp.bfloat16),
            jax.ShapeDtypeStruct((n, heads), jnp.float32),
        ),
        compiler_params=pltpu.CompilerParams(dimension_semantics=("arbitrary",)),
        cost_estimate=pl.CostEstimate(
            flops=flops, transcendentals=n * m * heads, bytes_accessed=2 * (2 * n * width + 2 * m * width)
        ),
    )(length, q, kv)


def _attend_back_kernel(length_ref, q_ref, kv_ref, do_ref, lse_ref, dq_ref, dkv_ref, *, heads, factor):
    @pl.when(pl.program_id(0) == 0)
    def _():
        dkv_ref[...] = jnp.zeros_like(dkv_ref)

    for h in range(heads):
        cols = slice(h * HEAD_DIM, (h + 1) * HEAD_DIM)
        vcols = slice((heads + h) * HEAD_DIM, (heads + h + 1) * HEAD_DIM)
        q = q_ref[:, cols]
        k = kv_ref[:, cols]
        v = kv_ref[:, vcols]
        do = do_ref[:, cols]
        portion = jnp.exp(_scores(length_ref, q, k, factor) - lse_ref[:, h : h + 1])
        dportion = lax.dot_general(do, v, (((1,), (1,)), ((), ())), preferred_element_type=jnp.float32)
        dkv_ref[:, vcols] += lax.dot_general(
            portion.astype(jnp.bfloat16), do, (((0,), (0,)), ((), ())), preferred_element_type=jnp.float32
        )
        centering = jnp.sum(portion * dportion, axis=1, keepdims=True)
        dscores = (portion * (dportion - centering)).astype(jnp.bfloat16)
        dq_ref[:, cols] = (
            jnp.dot(dscores, k, preferred_element_type=jnp.float32) * factor
        ).astype(dq_ref.dtype)
        dkv_ref[:, cols] += (
            lax.dot_general(dscores, q, (((0,), (0,)), ((), ())), preferred_element_type=jnp.float32) * factor
        )


def attend_back(length, q, kv, do, lse, factor):
    n, width = q.shape
    m = kv.shape[0]
    heads = width // HEAD_DIM
    tq = min(QUERY_TILE, n)
    grid = pltpu.PrefetchScalarGridSpec(
        num_scalar_prefetch=1,
        grid=(n // tq,),
        in_specs=[
            pl.BlockSpec((tq, width), lambda i, length: (i, 0)),
            pl.BlockSpec((m, 2 * width), lambda i, length: (0, 0)),
            pl.BlockSpec((tq, width), lambda i, length: (i, 0)),
            pl.BlockSpec((tq, heads), lambda i, length: (i, 0)),
        ],
        out_specs=[
            pl.BlockSpec((tq, width), lambda i, length: (i, 0)),
            pl.BlockSpec((m, 2 * width), lambda i, length: (0, 0)),
        ],
    )
    flops = 10 * n * m * width
    return pl.pallas_call(
        functools.partial(_attend_back_kernel, heads=heads, factor=factor),
        grid_spec=grid,
        out_shape=(
            jax.ShapeDtypeStruct((n, width), jnp.bfloat16),
            jax.ShapeDtypeStruct((m, 2 * width), jnp.float32),
        ),
        compiler_params=pltpu.CompilerParams(dimension_semantics=("arbitrary",)),
        cost_estimate=pl.CostEstimate(
            flops=flops, transcendentals=n * m * heads,
            bytes_accessed=2 * (3 * n * width + 2 * m * width) + 4 * 2 * m * width,
        ),
    )(length, q, kv, do, lse)


EPSILON = 1e-12


def norm_parts(hidden):
    center = hidden - jnp.mean(hidden, -1, keepdims=True)
    inverse = lax.rsqrt(jnp.mean(center * center, -1, keepdims=True) + EPSILON)
    return (center * inverse, inverse)


def norm_back(gradient, normal_form, inverse, gain):
    scaled = gradient * gain
    inner = (
        scaled
        - jnp.mean(scaled, -1, keepdims=True)
        - normal_form * jnp.mean(scaled * normal_form, -1, keepdims=True)
    )
    return (inner * inverse, jnp.sum(gradient * normal_form, 0), jnp.sum(gradient, 0))


def exact_gelu(values):
    return jax.nn.gelu(values, approximate=False)


def _attend_query_back_kernel(length_ref, q_ref, kv_ref, do_ref, lse_ref, dq_ref, delta_ref, *, heads, factor):
    for h in range(heads):
        cols = slice(h * HEAD_DIM, (h + 1) * HEAD_DIM)
        vcols = slice((heads + h) * HEAD_DIM, (heads + h + 1) * HEAD_DIM)
        k = kv_ref[:, cols]
        do = do_ref[:, cols]
        portion = jnp.exp(_scores(length_ref, q_ref[:, cols], k, factor) - lse_ref[:, h : h + 1])
        dportion = lax.dot_general(
            do, kv_ref[:, vcols], (((1,), (1,)), ((), ())), preferred_element_type=jnp.float32
        )
        centering = jnp.sum(portion * dportion, axis=1, keepdims=True)
        dscores = (portion * (dportion - centering)).astype(jnp.bfloat16)
        dq_ref[:, cols] = (
            jnp.dot(dscores, k, preferred_element_type=jnp.float32) * factor
        ).astype(dq_ref.dtype)
        delta_ref[:, h : h + 1] = centering


def attend_query_back(length, q, kv, do, lse, factor):
    n, width = q.shape
    m = kv.shape[0]
    heads = width // HEAD_DIM
    tq = min(QUERY_TILE, n)
    grid = pltpu.PrefetchScalarGridSpec(
        num_scalar_prefetch=1,
        grid=(n // tq,),
        in_specs=[
            pl.BlockSpec((tq, width), lambda i, length: (i, 0)),
            pl.BlockSpec((m, 2 * width), lambda i, length: (0, 0)),
            pl.BlockSpec((tq, width), lambda i, length: (i, 0)),
            pl.BlockSpec((tq, heads), lambda i, length: (i, 0)),
        ],
        out_specs=[
            pl.BlockSpec((tq, width), lambda i, length: (i, 0)),
            pl.BlockSpec((tq, heads), lambda i, length: (i, 0)),
        ],
    )
    return pl.pallas_call(
        functools.partial(_attend_query_back_kernel, heads=heads, factor=factor),
        grid_spec=grid,
        out_shape=(
            jax.ShapeDtypeStruct((n, width), jnp.bfloat16),
            jax.ShapeDtypeStruct((n, heads), jnp.float32),
        ),
        compiler_params=pltpu.CompilerParams(dimension_semantics=("arbitrary",)),
        cost_estimate=pl.CostEstimate(
            flops=6 * n * m * width, transcendentals=n * m * heads,
            bytes_accessed=2 * (3 * n * width + 2 * m * width),
        ),
    )(length, q, kv, do, lse)


def _attend_key_back_kernel(length_ref, q_ref, kv_ref, do_ref, lse_ref, delta_ref, dkv_ref, *, heads, factor):
    @pl.when(pl.program_id(0) == 0)
    def _():
        dkv_ref[...] = jnp.zeros_like(dkv_ref)

    for h in range(heads):
        cols = slice(h * HEAD_DIM, (h + 1) * HEAD_DIM)
        vcols = slice((heads + h) * HEAD_DIM, (heads + h + 1) * HEAD_DIM)
        q = q_ref[:, cols]
        do = do_ref[:, cols]
        portion = jnp.exp(_scores(length_ref, q, kv_ref[:, cols], factor) - lse_ref[:, h : h + 1])
        dportion = lax.dot_general(
            do, kv_ref[:, vcols], (((1,), (1,)), ((), ())), preferred_element_type=jnp.float32
        )
        dkv_ref[:, vcols] += lax.dot_general(
            portion.astype(jnp.bfloat16), do, (((0,), (0,)), ((), ())), preferred_element_type=jnp.float32
        )
        dscores = (portion * (dportion - delta_ref[:, h : h + 1])).astype(jnp.bfloat16)
        dkv_ref[:, cols] += (
            lax.dot_general(dscores, q, (((0,), (0,)), ((), ())), preferred_element_type=jnp.float32) * factor
        )


def attend_key_back(length, q, kv, do, lse, delta, factor):
    n, width = q.shape
    m = kv.shape[0]
    heads = width // HEAD_DIM
    tq = min(KEY_SIDE_TILE, n)
    grid = pltpu.PrefetchScalarGridSpec(
        num_scalar_prefetch=1,
        grid=(n // tq,),
        in_specs=[
            pl.BlockSpec((tq, width), lambda i, length: (i, 0)),
            pl.BlockSpec((m, 2 * width), lambda i, length: (0, 0)),
            pl.BlockSpec((tq, width), lambda i, length: (i, 0)),
            pl.BlockSpec((tq, heads), lambda i, length: (i, 0)),
            pl.BlockSpec((tq, heads), lambda i, length: (i, 0)),
        ],
        out_specs=pl.BlockSpec((m, 2 * width), lambda i, length: (0, 0)),
    )
    return pl.pallas_call(
        functools.partial(_attend_key_back_kernel, heads=heads, factor=factor),
        grid_spec=grid,
        out_shape=jax.ShapeDtypeStruct((m, 2 * width), jnp.float32),
        compiler_params=pltpu.CompilerParams(dimension_semantics=("arbitrary",)),
        cost_estimate=pl.CostEstimate(
            flops=8 * n * m * width, transcendentals=n * m * heads,
            bytes_accessed=2 * (2 * n * width + 2 * m * width) + 4 * 2 * m * width,
        ),
    )(length, q, kv, do, lse, delta)


def tp_sum(value):
    if lax.axis_size("tp") == 2:
        return value + lax.ppermute(value, "tp", [(0, 1), (1, 0)])
    return lax.psum(value, "tp")


def tp_gather(value):
    if lax.axis_size("tp") == 2:
        other = lax.ppermute(value, "tp", [(0, 1), (1, 0)])
        first = lax.axis_index("tp") == 0
        return jnp.stack([jnp.where(first, value, other), jnp.where(first, other, value)])
    return lax.all_gather(value, "tp")


def split_exact(value):
    high = lax.reduce_precision(value, exponent_bits=8, mantissa_bits=7)
    rest = value - high
    middle = lax.reduce_precision(rest, exponent_bits=8, mantissa_bits=7)
    low = lax.reduce_precision(rest - middle, exponent_bits=8, mantissa_bits=7)
    return jnp.concatenate([high, middle, low], axis=-1).astype(jnp.bfloat16)


def join_exact(pieces):
    width = pieces.shape[-1] // 3
    parts = pieces.astype(jnp.float32)
    return (parts[..., :width] + parts[..., width : 2 * width]) + parts[..., 2 * width :]


def line_gather(value, axis="ctx"):
    count = lax.axis_size(axis)
    if count > 8 or count < 2:
        return lax.all_gather(value, axis, axis=0, tiled=True)
    place = lax.axis_index(axis)
    from_left, from_right = [], []
    left_block, right_block = value, value
    for step in range(1, count):
        rightward = [(j, j + 1) for j in range(step - 1, count - 1)]
        leftward = [(j, j - 1) for j in range(1, count - step + 1)]
        left_block = lax.ppermute(left_block, axis, rightward)
        right_block = lax.ppermute(right_block, axis, leftward)
        from_left.append(left_block)
        from_right.append(right_block)
    candidates = jnp.stack([value] + from_left + from_right)
    blocks = jnp.arange(count)
    which = jnp.where(
        blocks == place,
        0,
        jnp.where(blocks < place, place - blocks, count - 1 + blocks - place),
    )
    return jnp.take(candidates, which, axis=0).reshape((count * value.shape[0],) + value.shape[1:])


def shard_send(value, axis="shard"):
    count = lax.axis_size(axis)
    if count > 8:
        return [lax.all_gather(value, axis, axis=0, tiled=True)]
    return [
        lax.ppermute(value, axis, [(j, (j + shift) % count) for j in range(count)])
        for shift in range(1, count)
    ]


def shard_assemble(value, arrived, axis="shard"):
    count = lax.axis_size(axis)
    if count > 8:
        return arrived[0]
    place = lax.axis_index(axis)
    rows = value.shape[0]
    out = jnp.zeros((count * rows,) + value.shape[1:], value.dtype)
    out = lax.dynamic_update_slice_in_dim(out, value, place * rows, 0)
    for shift, piece in enumerate(arrived, start=1):
        out = lax.dynamic_update_slice_in_dim(out, piece, ((place - shift) % count) * rows, 0)
    return out


def shard_gather(value, axis="shard"):
    return shard_assemble(value, shard_send(value, axis), axis)


def shard_scatter(value, axis="shard"):
    count = lax.axis_size(axis)
    if count > 8:
        return lax.psum_scatter(value, axis, scatter_dimension=0, tiled=True).astype(jnp.float32)
    place = lax.axis_index(axis)
    rows = value.shape[0] // count
    total = lax.dynamic_slice_in_dim(value, place * rows, rows, 0).astype(jnp.float32)
    for shift in range(1, count):
        outgoing = lax.dynamic_slice_in_dim(value, ((place + shift) % count) * rows, rows, 0)
        arrived = lax.ppermute(outgoing, axis, [(j, (j + shift) % count) for j in range(count)])
        total = total + arrived.astype(jnp.float32)
    return total


def on_device(
    tokens,
    seq_lengths,
    query_weight,
    query_bias,
    key_weight,
    value_weight,
    value_bias,
    output_weight,
    output_bias,
    attn_gain,
    attn_shift,
    inner_weight,
    inner_bias,
    outer_weight,
    outer_bias,
    final_gain,
    final_shift,
    upstream,
):
    row_count, model_width = tokens.shape
    tensor_place = lax.axis_index("tp")
    tensor_count = lax.axis_size("tp")
    head_width = query_weight.shape[1]
    hidden_width = inner_weight.shape[1]
    head_count = head_width // HEAD_DIM
    factor = HEAD_DIM ** (-0.5)
    f32 = jnp.float32

    qb = query_bias.shape[0]
    ib = inner_bias.shape[0]
    piece = output_bias.shape[0]
    tp_blocks = tp_gather(jnp.concatenate([query_bias, value_bias, inner_bias]))
    bias_columns = jnp.concatenate(
        [
            tp_blocks[:, :qb].reshape(piece, 1),
            tp_blocks[:, qb : 2 * qb].reshape(piece, 1),
            tp_blocks[:, 2 * qb :].reshape(piece, -1),
        ],
        axis=1,
    )
    shard_columns = jnp.stack(
        [output_bias, attn_gain, attn_shift, outer_bias, final_gain, final_shift], axis=1
    )
    piece_rows = key_weight.shape[0]
    kv_local = jnp.concatenate(
        [key_weight, value_weight, shard_columns, bias_columns], axis=1
    )
    kv_arrived = shard_send(kv_local)
    query_weight, kv_arrived = lax.optimization_barrier((query_weight, kv_arrived))
    query_full = shard_gather(query_weight)
    kv_vec_full = shard_assemble(kv_local, kv_arrived)
    vector_full = shard_assemble(
        kv_local[:, 2 * head_width :], [arrived[:, 2 * head_width :] for arrived in kv_arrived]
    ) if lax.axis_size("shard") <= 8 else kv_vec_full[:, 2 * head_width :]
    qkv_full = jnp.concatenate([query_full, kv_vec_full[:, : 2 * head_width]], axis=1)
    full_vectors = vector_full[:, :6].T.astype(f32)
    outbias_full, gain_first, shift_first, outerbias_full, gain_second, shift_second = full_vectors
    qbias_all = vector_full[:, 6]
    vbias_all = vector_full[:, 7]
    ibias_all = vector_full[:, 8:].reshape(-1)
    query_shift = lax.dynamic_slice_in_dim(qbias_all, tensor_place * head_width, head_width).astype(f32)
    value_shift = lax.dynamic_slice_in_dim(vbias_all, tensor_place * head_width, head_width).astype(f32)
    inner_shift = lax.dynamic_slice_in_dim(ibias_all, tensor_place * hidden_width, hidden_width).astype(f32)

    shard_count = lax.axis_size("shard")
    if shard_count <= 8:
        shard_place = lax.axis_index("shard")
        projected = None
        for shift, weight_piece in enumerate([kv_local] + kv_arrived):
            inputs = lax.dynamic_slice_in_dim(
                tokens, ((shard_place - shift) % shard_count) * piece_rows, piece_rows, 1
            )
            term = jnp.dot(inputs, weight_piece[:, : 2 * head_width], preferred_element_type=f32)
            projected = term if projected is None else projected + term
    else:
        projected = jnp.dot(tokens, kv_vec_full[:, : 2 * head_width], preferred_element_type=f32)
    rest_local = jnp.concatenate([output_weight, inner_weight, outer_weight], axis=1)
    rest_local, projected = lax.optimization_barrier((rest_local, projected))
    rest_arrived = shard_send(rest_local)
    key_local = projected[:, :head_width].astype(jnp.bfloat16)
    value_local = (projected[:, head_width:] + value_shift).astype(jnp.bfloat16)
    query = (jnp.dot(tokens, query_full, preferred_element_type=f32) + query_shift).astype(
        jnp.bfloat16
    )
    chunk_heads = 2 if head_count % 2 == 0 else 1
    chunk_width = chunk_heads * HEAD_DIM
    kv_chunks = []
    own_chunks = []
    for c in range(head_count // chunk_heads):
        columns = slice(c * chunk_width, (c + 1) * chunk_width)
        outgoing = jnp.concatenate([key_local[:, columns], value_local[:, columns]], axis=1)
        own_chunks.append(outgoing)
        kv_chunks.append(line_gather(outgoing))
    query_all = lax.all_gather(query, "ctx", axis=0, tiled=True)
    chunk_outs = [
        attend(seq_lengths, query[:, c * chunk_width : (c + 1) * chunk_width], chunk, factor)
        for c, chunk in enumerate(kv_chunks)
    ]
    context = jnp.concatenate([o[0] for o in chunk_outs], axis=1)
    rest_arrived, context = lax.optimization_barrier((rest_arrived, context))
    rest_full = shard_assemble(rest_local, rest_arrived)
    output_full = rest_full[:, :head_width]
    inner_full = rest_full[:, head_width : head_width + hidden_width]
    outer_full = rest_full[:, head_width + hidden_width :]
    attn_part = jnp.einsum("th,oh->to", context, output_full, preferred_element_type=f32)
    attended = tp_sum(attn_part) + outbias_full
    normal_first, inverse_first = norm_parts(tokens.astype(f32) + attended)
    normed = normal_first * gain_first + shift_first
    normed_low = normed.astype(jnp.bfloat16)
    hidden = jnp.dot(normed_low, inner_full, preferred_element_type=f32) + inner_shift
    active = exact_gelu(hidden).astype(jnp.bfloat16)
    branch_part = jnp.einsum("tf,of->to", active, outer_full, preferred_element_type=f32)
    branch = tp_sum(branch_part) + outerbias_full
    normal_second, inverse_second = norm_parts(normed + branch)
    layer_out = (normal_second * gain_second + shift_second).astype(jnp.bfloat16)

    dres_second, final_gain_part, final_shift_part = norm_back(
        upstream.astype(f32), normal_second, inverse_second, gain_second
    )
    dbranch = dres_second.astype(jnp.bfloat16)
    outer_bias_part = jnp.sum(dbranch.astype(f32), 0)
    outer_weight_part = jnp.einsum("to,tf->of", dbranch, active, preferred_element_type=f32)
    dactive = jnp.dot(dbranch, outer_full, preferred_element_type=f32)
    unused, gelu_pull = jax.vjp(exact_gelu, hidden)
    dhidden = gelu_pull(dactive)[0].astype(jnp.bfloat16)
    inner_weight_part = jnp.einsum("td,tf->df", normed_low, dhidden, preferred_element_type=f32)
    inner_bias_part = jnp.sum(dhidden.astype(f32), 0)
    dnormed_part = jnp.einsum("tf,df->td", dhidden, inner_full, preferred_element_type=f32)
    dnormed = dres_second + tp_sum(dnormed_part)
    dres_first, attn_gain_part, attn_shift_part = norm_back(
        dnormed, normal_first, inverse_first, gain_first
    )
    dattended = dres_first.astype(jnp.bfloat16)
    output_bias_part = jnp.sum(dattended.astype(f32), 0)
    output_weight_part = jnp.einsum("to,th->oh", dattended, context, preferred_element_type=f32)
    dcontext = jnp.dot(dattended, output_full, preferred_element_type=f32).astype(jnp.bfloat16)

    low = jnp.bfloat16
    rows = model_width
    early = jnp.concatenate(
        [
            output_weight_part,
            inner_weight_part,
            outer_weight_part,
            jnp.stack(
                [output_bias_part, attn_gain_part, attn_shift_part, outer_bias_part,
                 final_gain_part, final_shift_part],
                axis=1,
            ),
            tp_gather(inner_bias_part).reshape(rows, -1),
        ],
        axis=1,
    ).astype(low)
    early_scattered = lax.psum_scatter(early, "shard", scatter_dimension=0, tiled=True)
    local_rows = piece // tensor_count

    own_length = seq_lengths - lax.axis_index("ctx") * row_count
    ctx_count = lax.axis_size("ctx")
    query_backs = []
    key_backs = []
    for c, chunk in enumerate(kv_chunks):
        pair = slice(c * chunk_width, (c + 1) * chunk_width)
        dquery_pair, delta_pair = attend_query_back(
            seq_lengths, query[:, pair], chunk, dcontext[:, pair], chunk_outs[c][1], factor
        )
        query_backs.append(dquery_pair)
        stats = split_exact(jnp.concatenate([chunk_outs[c][1], delta_pair], axis=1))
        stats_rows = stats.size // chunk_width
        padded_rows = -(-stats_rows // 16) * 16
        payload = jnp.concatenate(
            [
                dcontext[:, pair],
                stats.reshape(stats_rows, chunk_width),
                jnp.zeros((padded_rows - stats_rows, chunk_width), jnp.bfloat16),
            ],
            axis=0,
        )
        arrived = shard_gather(payload, "ctx").reshape(
            ctx_count, row_count + padded_rows, chunk_width
        )
        dcontext_pair_all = arrived[:, :row_count].reshape(ctx_count * row_count, chunk_width)
        stats_all = join_exact(
            arrived[:, row_count : row_count + stats_rows].reshape(
                ctx_count * row_count, stats.shape[1]
            )
        )
        own = own_chunks[c]
        if key_backs:
            if len(key_backs) == 1:
                early_scattered, own, key_backs[-1] = lax.optimization_barrier(
                    (early_scattered, own, key_backs[-1])
                )
                early_piece = lax.psum(early_scattered, "ctx")
            else:
                own, key_backs[-1] = lax.optimization_barrier((own, key_backs[-1]))
        elif len(kv_chunks) == 1:
            early_piece = lax.psum(early_scattered, "ctx")
        key_backs.append(
            attend_key_back(
                own_length,
                query_all[:, pair],
                own,
                dcontext_pair_all,
                stats_all[:, :chunk_heads],
                stats_all[:, chunk_heads:],
                factor,
            )
        )
    dquery = jnp.concatenate(query_backs, axis=1)
    dkeys = jnp.concatenate([back[:, :chunk_width] for back in key_backs], axis=1).astype(low)
    dvalues = jnp.concatenate([back[:, chunk_width:] for back in key_backs], axis=1).astype(low)
    early_piece = early_piece.astype(f32)
    output_total = early_piece[:, :head_width]
    inner_total = early_piece[:, head_width : head_width + hidden_width]
    outer_total = early_piece[:, head_width + hidden_width : head_width + 2 * hidden_width]
    early_vectors = early_piece[:, head_width + 2 * hidden_width :]
    outbias_total, attn_gain_total, attn_shift_total, outerbias_total, final_gain_total, final_shift_total = (
        early_vectors[:, :6].T
    )
    ibias_total = lax.dynamic_slice_in_dim(
        early_vectors[:, 6:], tensor_place * local_rows, local_rows, 0
    ).reshape(-1)
    dqkv = jnp.concatenate([dquery, dkeys, dvalues], axis=1)
    qkv_weight_part = jnp.einsum("td,th->dh", tokens, dqkv, preferred_element_type=f32)
    query_bias_part = jnp.sum(dquery.astype(f32), 0)
    value_bias_part = jnp.sum(dvalues.astype(f32), 0)
    dinput_part = jnp.einsum("th,dh->td", dqkv, qkv_full, preferred_element_type=f32)
    tokens_gradient = dres_first + tp_sum(dinput_part)
    late = jnp.concatenate(
        [
            qkv_weight_part,
            tp_gather(query_bias_part).reshape(rows, 1),
            tp_gather(value_bias_part).reshape(rows, 1),
        ],
        axis=1,
    ).astype(low)
    late, early_piece = lax.optimization_barrier((late, early_piece))
    late_piece = lax.psum(shard_scatter(late).astype(low), "ctx").astype(f32)
    query_total = late_piece[:, :head_width]
    key_total = late_piece[:, head_width : 2 * head_width]
    value_total = late_piece[:, 2 * head_width : 3 * head_width]
    qbias_total = lax.dynamic_slice_in_dim(
        late_piece[:, 3 * head_width], tensor_place * local_rows, local_rows
    )
    vbias_total = lax.dynamic_slice_in_dim(
        late_piece[:, 3 * head_width + 1], tensor_place * local_rows, local_rows
    )
    return (
        layer_out,
        tokens_gradient,
        query_total,
        qbias_total,
        key_total,
        value_total,
        vbias_total,
        output_total,
        outbias_total,
        attn_gain_total,
        attn_shift_total,
        inner_total,
        ibias_total,
        outer_total,
        outerbias_total,
        final_gain_total,
        final_shift_total,
    )


def solution(mesh):
    placed = (
        P(("shard", "ctx"), None),
        P("shard"),
        P("shard", "tp"),
        P(("shard", "tp")),
        P("shard", "tp"),
        P("shard", "tp"),
        P(("shard", "tp")),
        P("shard", "tp"),
        P("shard"),
        P("shard"),
        P("shard"),
        P("shard", "tp"),
        P(("shard", "tp")),
        P("shard", "tp"),
        P("shard"),
        P("shard"),
        P("shard"),
        P(("shard", "ctx"), None),
    )
    return jax.shard_map(
        on_device,
        mesh=mesh,
        in_specs=placed,
        out_specs=(
            P(("shard", "ctx"), None),
            P(("shard", "ctx"), None),
            P("shard", "tp"),
            P(("shard", "tp")),
            P("shard", "tp"),
            P("shard", "tp"),
            P(("shard", "tp")),
            P("shard", "tp"),
            P("shard"),
            P("shard"),
            P("shard"),
            P("shard", "tp"),
            P(("shard", "tp")),
            P("shard", "tp"),
            P("shard"),
            P("shard"),
            P("shard"),
        ),
        check_vma=False,
    )
```

```python
import functools

import jax
import jax.numpy as jnp
from jax import lax
from jax.experimental import pallas as pl
from jax.experimental.pallas import tpu as pltpu
from jax.sharding import PartitionSpec as P

HEAD_DIM = 64
QUERY_TILE = 128
KEY_SIDE_TILE = 256


def _scores(length_ref, q, k, factor):
    s = lax.dot_general(q, k, (((1,), (1,)), ((), ())), preferred_element_type=jnp.float32) * factor
    keys = lax.broadcasted_iota(jnp.int32, s.shape, 1)
    return jnp.where(keys < length_ref[0], s, -1e30)


def _attend_kernel(length_ref, q_ref, kv_ref, o_ref, lse_ref, *, heads, factor):
    for h in range(heads):
        cols = slice(h * HEAD_DIM, (h + 1) * HEAD_DIM)
        vcols = slice((heads + h) * HEAD_DIM, (heads + h + 1) * HEAD_DIM)
        s = _scores(length_ref, q_ref[:, cols], kv_ref[:, cols], factor)
        highest = jnp.max(s, axis=1, keepdims=True)
        shifted = jnp.exp(s - highest)
        summed = jnp.sum(shifted, axis=1, keepdims=True)
        portion = (shifted / summed).astype(jnp.bfloat16)
        mixed = jnp.dot(portion, kv_ref[:, vcols], preferred_element_type=jnp.float32)
        o_ref[:, cols] = mixed.astype(o_ref.dtype)
        lse_ref[:, h : h + 1] = highest + jnp.log(summed)


def attend(length, q, kv, factor):
    n, width = q.shape
    m = kv.shape[0]
    heads = width // HEAD_DIM
    tq = min(QUERY_TILE, n)
    grid = pltpu.PrefetchScalarGridSpec(
        num_scalar_prefetch=1,
        grid=(n // tq,),
        in_specs=[
            pl.BlockSpec((tq, width), lambda i, length: (i, 0)),
            pl.BlockSpec((m, 2 * width), lambda i, length: (0, 0)),
        ],
        out_specs=[
            pl.BlockSpec((tq, width), lambda i, length: (i, 0)),
            pl.BlockSpec((tq, heads), lambda i, length: (i, 0)),
        ],
    )
    flops = 4 * n * m * width
    return pl.pallas_call(
        functools.partial(_attend_kernel, heads=heads, factor=factor),
        grid_spec=grid,
        out_shape=(
            jax.ShapeDtypeStruct((n, width), jnp.bfloat16),
            jax.ShapeDtypeStruct((n, heads), jnp.float32),
        ),
        compiler_params=pltpu.CompilerParams(dimension_semantics=("arbitrary",)),
        cost_estimate=pl.CostEstimate(
            flops=flops, transcendentals=n * m * heads, bytes_accessed=2 * (2 * n * width + 2 * m * width)
        ),
    )(length, q, kv)


def _attend_back_kernel(length_ref, q_ref, kv_ref, do_ref, lse_ref, dq_ref, dkv_ref, *, heads, factor):
    @pl.when(pl.program_id(0) == 0)
    def _():
        dkv_ref[...] = jnp.zeros_like(dkv_ref)

    for h in range(heads):
        cols = slice(h * HEAD_DIM, (h + 1) * HEAD_DIM)
        vcols = slice((heads + h) * HEAD_DIM, (heads + h + 1) * HEAD_DIM)
        q = q_ref[:, cols]
        k = kv_ref[:, cols]
        v = kv_ref[:, vcols]
        do = do_ref[:, cols]
        portion = jnp.exp(_scores(length_ref, q, k, factor) - lse_ref[:, h : h + 1])
        dportion = lax.dot_general(do, v, (((1,), (1,)), ((), ())), preferred_element_type=jnp.float32)
        dkv_ref[:, vcols] += lax.dot_general(
            portion.astype(jnp.bfloat16), do, (((0,), (0,)), ((), ())), preferred_element_type=jnp.float32
        )
        centering = jnp.sum(portion * dportion, axis=1, keepdims=True)
        dscores = (portion * (dportion - centering)).astype(jnp.bfloat16)
        dq_ref[:, cols] = (
            jnp.dot(dscores, k, preferred_element_type=jnp.float32) * factor
        ).astype(dq_ref.dtype)
        dkv_ref[:, cols] += (
            lax.dot_general(dscores, q, (((0,), (0,)), ((), ())), preferred_element_type=jnp.float32) * factor
        )


def attend_back(length, q, kv, do, lse, factor):
    n, width = q.shape
    m = kv.shape[0]
    heads = width // HEAD_DIM
    tq = min(QUERY_TILE, n)
    grid = pltpu.PrefetchScalarGridSpec(
        num_scalar_prefetch=1,
        grid=(n // tq,),
        in_specs=[
            pl.BlockSpec((tq, width), lambda i, length: (i, 0)),
            pl.BlockSpec((m, 2 * width), lambda i, length: (0, 0)),
            pl.BlockSpec((tq, width), lambda i, length: (i, 0)),
            pl.BlockSpec((tq, heads), lambda i, length: (i, 0)),
        ],
        out_specs=[
            pl.BlockSpec((tq, width), lambda i, length: (i, 0)),
            pl.BlockSpec((m, 2 * width), lambda i, length: (0, 0)),
        ],
    )
    flops = 10 * n * m * width
    return pl.pallas_call(
        functools.partial(_attend_back_kernel, heads=heads, factor=factor),
        grid_spec=grid,
        out_shape=(
            jax.ShapeDtypeStruct((n, width), jnp.bfloat16),
            jax.ShapeDtypeStruct((m, 2 * width), jnp.float32),
        ),
        compiler_params=pltpu.CompilerParams(dimension_semantics=("arbitrary",)),
        cost_estimate=pl.CostEstimate(
            flops=flops, transcendentals=n * m * heads,
            bytes_accessed=2 * (3 * n * width + 2 * m * width) + 4 * 2 * m * width,
        ),
    )(length, q, kv, do, lse)


EPSILON = 1e-12


def norm_parts(hidden):
    center = hidden - jnp.mean(hidden, -1, keepdims=True)
    inverse = lax.rsqrt(jnp.mean(center * center, -1, keepdims=True) + EPSILON)
    return (center * inverse, inverse)


def norm_back(gradient, normal_form, inverse, gain):
    scaled = gradient * gain
    inner = (
        scaled
        - jnp.mean(scaled, -1, keepdims=True)
        - normal_form * jnp.mean(scaled * normal_form, -1, keepdims=True)
    )
    return (inner * inverse, jnp.sum(gradient * normal_form, 0), jnp.sum(gradient, 0))


def exact_gelu(values):
    return jax.nn.gelu(values, approximate=False)


def _attend_query_back_kernel(length_ref, q_ref, kv_ref, do_ref, lse_ref, dq_ref, delta_ref, *, heads, factor):
    for h in range(heads):
        cols = slice(h * HEAD_DIM, (h + 1) * HEAD_DIM)
        vcols = slice((heads + h) * HEAD_DIM, (heads + h + 1) * HEAD_DIM)
        k = kv_ref[:, cols]
        do = do_ref[:, cols]
        portion = jnp.exp(_scores(length_ref, q_ref[:, cols], k, factor) - lse_ref[:, h : h + 1])
        dportion = lax.dot_general(
            do, kv_ref[:, vcols], (((1,), (1,)), ((), ())), preferred_element_type=jnp.float32
        )
        centering = jnp.sum(portion * dportion, axis=1, keepdims=True)
        dscores = (portion * (dportion - centering)).astype(jnp.bfloat16)
        dq_ref[:, cols] = (
            jnp.dot(dscores, k, preferred_element_type=jnp.float32) * factor
        ).astype(dq_ref.dtype)
        delta_ref[:, h : h + 1] = centering


def attend_query_back(length, q, kv, do, lse, factor):
    n, width = q.shape
    m = kv.shape[0]
    heads = width // HEAD_DIM
    tq = min(QUERY_TILE, n)
    grid = pltpu.PrefetchScalarGridSpec(
        num_scalar_prefetch=1,
        grid=(n // tq,),
        in_specs=[
            pl.BlockSpec((tq, width), lambda i, length: (i, 0)),
            pl.BlockSpec((m, 2 * width), lambda i, length: (0, 0)),
            pl.BlockSpec((tq, width), lambda i, length: (i, 0)),
            pl.BlockSpec((tq, heads), lambda i, length: (i, 0)),
        ],
        out_specs=[
            pl.BlockSpec((tq, width), lambda i, length: (i, 0)),
            pl.BlockSpec((tq, heads), lambda i, length: (i, 0)),
        ],
    )
    return pl.pallas_call(
        functools.partial(_attend_query_back_kernel, heads=heads, factor=factor),
        grid_spec=grid,
        out_shape=(
            jax.ShapeDtypeStruct((n, width), jnp.bfloat16),
            jax.ShapeDtypeStruct((n, heads), jnp.float32),
        ),
        compiler_params=pltpu.CompilerParams(dimension_semantics=("arbitrary",)),
        cost_estimate=pl.CostEstimate(
            flops=6 * n * m * width, transcendentals=n * m * heads,
            bytes_accessed=2 * (3 * n * width + 2 * m * width),
        ),
    )(length, q, kv, do, lse)


def _attend_key_back_kernel(
    length_ref, order_ref, q_ref, kv_ref, do_ref, stats_ref, dkv_ref, *, heads, factor
):
    @pl.when(pl.program_id(0) == 0)
    def _():
        dkv_ref[...] = jnp.zeros_like(dkv_ref)

    pieces = stats_ref[...].astype(jnp.float32)
    count = pieces.shape[0] // 3
    stats = (pieces[:count] + pieces[count : 2 * count]) + pieces[2 * count :]
    for h in range(heads):
        cols = slice(h * HEAD_DIM, (h + 1) * HEAD_DIM)
        vcols = slice((heads + h) * HEAD_DIM, (heads + h + 1) * HEAD_DIM)
        q = q_ref[:, cols]
        do = do_ref[:, cols]
        k = kv_ref[:, cols]
        scores = (
            lax.dot_general(k, q, (((1,), (1,)), ((), ())), preferred_element_type=jnp.float32)
            * factor
        )
        keys = lax.broadcasted_iota(jnp.int32, scores.shape, 0)
        scores = jnp.where(keys < length_ref[0], scores, -1e30)
        portion = jnp.exp(scores - stats[h : h + 1, :])
        dportion = lax.dot_general(
            kv_ref[:, vcols], do, (((1,), (1,)), ((), ())), preferred_element_type=jnp.float32
        )
        dkv_ref[:, vcols] += jnp.dot(
            portion.astype(jnp.bfloat16), do, preferred_element_type=jnp.float32
        )
        dscores = (portion * (dportion - stats[heads + h : heads + h + 1, :])).astype(jnp.bfloat16)
        dkv_ref[:, cols] += jnp.dot(dscores, q, preferred_element_type=jnp.float32) * factor


def attend_key_back(length, order, q_all, pair, kv, do, stats, factor):
    m, double = kv.shape
    width = double // 2
    heads = width // HEAD_DIM
    n = do.shape[0]
    tq = m
    grid = pltpu.PrefetchScalarGridSpec(
        num_scalar_prefetch=2,
        grid=(n // tq,),
        in_specs=[
            pl.BlockSpec((tq, width), lambda i, length, order: (order[i], pair)),
            pl.BlockSpec((m, 2 * width), lambda i, length, order: (0, 0)),
            pl.BlockSpec((tq, width), lambda i, length, order: (i, 0)),
            pl.BlockSpec((stats.shape[0], tq), lambda i, length, order: (0, i)),
        ],
        out_specs=pl.BlockSpec((m, 2 * width), lambda i, length, order: (0, 0)),
    )
    return pl.pallas_call(
        functools.partial(_attend_key_back_kernel, heads=heads, factor=factor),
        grid_spec=grid,
        out_shape=jax.ShapeDtypeStruct((m, 2 * width), jnp.float32),
        compiler_params=pltpu.CompilerParams(dimension_semantics=("arbitrary",)),
        cost_estimate=pl.CostEstimate(
            flops=8 * n * m * width, transcendentals=n * m * heads,
            bytes_accessed=2 * (2 * n * width + 2 * m * width) + 4 * 2 * m * width,
        ),
    )(length, order, q_all, kv, do, stats)


def tp_sum(value):
    if lax.axis_size("tp") == 2:
        return value + lax.ppermute(value, "tp", [(0, 1), (1, 0)])
    return lax.psum(value, "tp")


def tp_gather(value):
    if lax.axis_size("tp") == 2:
        other = lax.ppermute(value, "tp", [(0, 1), (1, 0)])
        first = lax.axis_index("tp") == 0
        return jnp.stack([jnp.where(first, value, other), jnp.where(first, other, value)])
    return lax.all_gather(value, "tp")


def split_exact(value):
    high = lax.reduce_precision(value, exponent_bits=8, mantissa_bits=7)
    rest = value - high
    middle = lax.reduce_precision(rest, exponent_bits=8, mantissa_bits=7)
    low = lax.reduce_precision(rest - middle, exponent_bits=8, mantissa_bits=7)
    return jnp.concatenate([high, middle, low], axis=-1).astype(jnp.bfloat16)


def join_exact(pieces):
    width = pieces.shape[-1] // 3
    parts = pieces.astype(jnp.float32)
    return (parts[..., :width] + parts[..., width : 2 * width]) + parts[..., 2 * width :]


def shard_send(value, axis="shard"):
    count = lax.axis_size(axis)
    if count > 8:
        return [lax.all_gather(value, axis, axis=0, tiled=True)]
    return [
        lax.ppermute(value, axis, [(j, (j + shift) % count) for j in range(count)])
        for shift in range(1, count)
    ]


def shard_assemble(value, arrived, axis="shard"):
    count = lax.axis_size(axis)
    if count > 8:
        return arrived[0]
    place = lax.axis_index(axis)
    rows = value.shape[0]
    out = jnp.zeros((count * rows,) + value.shape[1:], value.dtype)
    out = lax.dynamic_update_slice_in_dim(out, value, place * rows, 0)
    for shift, piece in enumerate(arrived, start=1):
        out = lax.dynamic_update_slice_in_dim(out, piece, ((place - shift) % count) * rows, 0)
    return out


def shard_gather(value, axis="shard"):
    return shard_assemble(value, shard_send(value, axis), axis)


def shard_scatter(value, axis="shard"):
    count = lax.axis_size(axis)
    if count > 8:
        return lax.psum_scatter(value, axis, scatter_dimension=0, tiled=True).astype(jnp.float32)
    place = lax.axis_index(axis)
    rows = value.shape[0] // count
    total = lax.dynamic_slice_in_dim(value, place * rows, rows, 0).astype(jnp.float32)
    for shift in range(1, count):
        outgoing = lax.dynamic_slice_in_dim(value, ((place + shift) % count) * rows, rows, 0)
        arrived = lax.ppermute(outgoing, axis, [(j, (j + shift) % count) for j in range(count)])
        total = total + arrived.astype(jnp.float32)
    return total


def on_device(
    tokens,
    seq_lengths,
    query_weight,
    query_bias,
    key_weight,
    value_weight,
    value_bias,
    output_weight,
    output_bias,
    attn_gain,
    attn_shift,
    inner_weight,
    inner_bias,
    outer_weight,
    outer_bias,
    final_gain,
    final_shift,
    upstream,
):
    row_count, model_width = tokens.shape
    tensor_place = lax.axis_index("tp")
    tensor_count = lax.axis_size("tp")
    head_width = query_weight.shape[1]
    hidden_width = inner_weight.shape[1]
    head_count = head_width // HEAD_DIM
    factor = HEAD_DIM ** (-0.5)
    f32 = jnp.float32

    qb = query_bias.shape[0]
    ib = inner_bias.shape[0]
    piece = output_bias.shape[0]
    tp_blocks = tp_gather(jnp.concatenate([query_bias, value_bias, inner_bias]))
    bias_columns = jnp.concatenate(
        [
            tp_blocks[:, :qb].reshape(piece, 1),
            tp_blocks[:, qb : 2 * qb].reshape(piece, 1),
            tp_blocks[:, 2 * qb :].reshape(piece, -1),
        ],
        axis=1,
    )
    shard_columns = jnp.stack(
        [output_bias, attn_gain, attn_shift, outer_bias, final_gain, final_shift], axis=1
    )
    piece_rows = key_weight.shape[0]
    kv_local = jnp.concatenate(
        [key_weight, value_weight, shard_columns, bias_columns], axis=1
    )
    kv_arrived = shard_send(kv_local)
    query_full = shard_gather(query_weight)
    kv_vec_full = shard_assemble(kv_local, kv_arrived)
    vector_full = shard_assemble(
        kv_local[:, 2 * head_width :], [arrived[:, 2 * head_width :] for arrived in kv_arrived]
    ) if lax.axis_size("shard") <= 8 else kv_vec_full[:, 2 * head_width :]
    qkv_full = jnp.concatenate([query_full, kv_vec_full[:, : 2 * head_width]], axis=1)
    rest_local = jnp.concatenate([output_weight, inner_weight, outer_weight], axis=1)
    rest_arrived = shard_send(rest_local)

    full_vectors = vector_full[:, :6].T.astype(f32)
    outbias_full, gain_first, shift_first, outerbias_full, gain_second, shift_second = full_vectors
    qbias_all = vector_full[:, 6]
    vbias_all = vector_full[:, 7]
    ibias_all = vector_full[:, 8:].reshape(-1)
    query_shift = lax.dynamic_slice_in_dim(qbias_all, tensor_place * head_width, head_width).astype(f32)
    value_shift = lax.dynamic_slice_in_dim(vbias_all, tensor_place * head_width, head_width).astype(f32)
    inner_shift = lax.dynamic_slice_in_dim(ibias_all, tensor_place * hidden_width, hidden_width).astype(f32)

    shard_count = lax.axis_size("shard")
    if shard_count <= 8:
        shard_place = lax.axis_index("shard")
        projected = None
        for shift, weight_piece in enumerate([kv_local] + kv_arrived):
            inputs = lax.dynamic_slice_in_dim(
                tokens, ((shard_place - shift) % shard_count) * piece_rows, piece_rows, 1
            )
            term = jnp.dot(inputs, weight_piece[:, : 2 * head_width], preferred_element_type=f32)
            projected = term if projected is None else projected + term
    else:
        projected = jnp.dot(tokens, kv_vec_full[:, : 2 * head_width], preferred_element_type=f32)
    key_local = projected[:, :head_width].astype(jnp.bfloat16)
    value_local = (projected[:, head_width:] + value_shift).astype(jnp.bfloat16)
    query = (jnp.dot(tokens, query_full, preferred_element_type=f32) + query_shift).astype(
        jnp.bfloat16
    )
    chunk_heads = 2 if head_count % 2 == 0 else 1
    chunk_width = chunk_heads * HEAD_DIM
    kv_chunks = []
    own_chunks = []
    for c in range(head_count // chunk_heads):
        columns = slice(c * chunk_width, (c + 1) * chunk_width)
        outgoing = jnp.concatenate([key_local[:, columns], value_local[:, columns]], axis=1)
        own_chunks.append(outgoing)
        kv_chunks.append(lax.all_gather(outgoing, "ctx", axis=0, tiled=True))
    query_all = lax.all_gather(query, "ctx", axis=0, tiled=True)
    chunk_outs = [
        attend(seq_lengths, query[:, c * chunk_width : (c + 1) * chunk_width], chunk, factor)
        for c, chunk in enumerate(kv_chunks)
    ]
    context = jnp.concatenate([o[0] for o in chunk_outs], axis=1)
    rest_arrived, context = lax.optimization_barrier((rest_arrived, context))
    rest_full = shard_assemble(rest_local, rest_arrived)
    output_full = rest_full[:, :head_width]
    inner_full = rest_full[:, head_width : head_width + hidden_width]
    outer_full = rest_full[:, head_width + hidden_width :]
    attn_part = jnp.einsum("th,oh->to", context, output_full, preferred_element_type=f32)
    attended = tp_sum(attn_part) + outbias_full
    normal_first, inverse_first = norm_parts(tokens.astype(f32) + attended)
    normed = normal_first * gain_first + shift_first
    normed_low = normed.astype(jnp.bfloat16)
    hidden = jnp.dot(normed_low, inner_full, preferred_element_type=f32) + inner_shift
    active = exact_gelu(hidden).astype(jnp.bfloat16)
    branch_part = jnp.einsum("tf,of->to", active, outer_full, preferred_element_type=f32)
    branch = tp_sum(branch_part) + outerbias_full
    normal_second, inverse_second = norm_parts(normed + branch)
    layer_out = (normal_second * gain_second + shift_second).astype(jnp.bfloat16)

    dres_second, final_gain_part, final_shift_part = norm_back(
        upstream.astype(f32), normal_second, inverse_second, gain_second
    )
    dbranch = dres_second.astype(jnp.bfloat16)
    outer_bias_part = jnp.sum(dbranch.astype(f32), 0)
    outer_weight_part = jnp.einsum("to,tf->of", dbranch, active, preferred_element_type=f32)
    dactive = jnp.dot(dbranch, outer_full, preferred_element_type=f32)
    unused, gelu_pull = jax.vjp(exact_gelu, hidden)
    dhidden = gelu_pull(dactive)[0].astype(jnp.bfloat16)
    inner_weight_part = jnp.einsum("td,tf->df", normed_low, dhidden, preferred_element_type=f32)
    inner_bias_part = jnp.sum(dhidden.astype(f32), 0)
    dnormed_part = jnp.einsum("tf,df->td", dhidden, inner_full, preferred_element_type=f32)
    dnormed = dres_second + tp_sum(dnormed_part)
    dres_first, attn_gain_part, attn_shift_part = norm_back(
        dnormed, normal_first, inverse_first, gain_first
    )
    dattended = dres_first.astype(jnp.bfloat16)
    output_bias_part = jnp.sum(dattended.astype(f32), 0)
    output_weight_part = jnp.einsum("to,th->oh", dattended, context, preferred_element_type=f32)
    dcontext = jnp.dot(dattended, output_full, preferred_element_type=f32).astype(jnp.bfloat16)

    low = jnp.bfloat16
    rows = model_width
    early = jnp.concatenate(
        [
            output_weight_part,
            inner_weight_part,
            outer_weight_part,
            jnp.stack(
                [output_bias_part, attn_gain_part, attn_shift_part, outer_bias_part,
                 final_gain_part, final_shift_part],
                axis=1,
            ),
            tp_gather(inner_bias_part).reshape(rows, -1),
        ],
        axis=1,
    ).astype(low)
    early_scattered = lax.psum_scatter(early, "shard", scatter_dimension=0, tiled=True)
    local_rows = piece // tensor_count

    own_length = seq_lengths - lax.axis_index("ctx") * row_count
    ctx_count = lax.axis_size("ctx")
    if ctx_count <= 8:
        arrival_order = (lax.axis_index("ctx") - jnp.arange(ctx_count, dtype=jnp.int32)) % ctx_count
    else:
        arrival_order = jnp.arange(ctx_count, dtype=jnp.int32)
    query_backs = []
    key_backs = []
    for c, chunk in enumerate(kv_chunks):
        pair = slice(c * chunk_width, (c + 1) * chunk_width)
        dquery_pair, delta_pair = attend_query_back(
            seq_lengths, query[:, pair], chunk, dcontext[:, pair], chunk_outs[c][1], factor
        )
        query_backs.append(dquery_pair)
        stats = split_exact(jnp.concatenate([chunk_outs[c][1], delta_pair], axis=1)).T
        stats_rows = stats.size // chunk_width
        padded_rows = -(-stats_rows // 16) * 16
        payload = jnp.concatenate(
            [
                dcontext[:, pair],
                stats.reshape(stats_rows, chunk_width),
                jnp.zeros((padded_rows - stats_rows, chunk_width), jnp.bfloat16),
            ],
            axis=0,
        )
        pieces = [payload] + shard_send(payload, "ctx")
        if len(pieces) == 1:
            pieces = list(pieces[0].reshape(ctx_count, -1, chunk_width))
        dcontext_pieces = jnp.concatenate([piece[:row_count] for piece in pieces], axis=0)
        stats_pieces = jnp.concatenate(
            [
                piece[row_count : row_count + stats_rows].reshape(stats.shape)
                for piece in pieces
            ],
            axis=1,
        )
        own = own_chunks[c]
        if key_backs:
            if len(key_backs) == 1:
                early_scattered, own, key_backs[-1] = lax.optimization_barrier(
                    (early_scattered, own, key_backs[-1])
                )
                early_piece = lax.psum(early_scattered, "ctx")
            else:
                own, key_backs[-1] = lax.optimization_barrier((own, key_backs[-1]))
        elif len(kv_chunks) == 1:
            early_piece = lax.psum(early_scattered, "ctx")
        key_backs.append(
            attend_key_back(
                own_length,
                arrival_order,
                query_all,
                c,
                own,
                dcontext_pieces,
                stats_pieces,
                factor,
            )
        )
    dquery = jnp.concatenate(query_backs, axis=1)
    dkeys = jnp.concatenate([back[:, :chunk_width] for back in key_backs], axis=1).astype(low)
    dvalues = jnp.concatenate([back[:, chunk_width:] for back in key_backs], axis=1).astype(low)
    early_piece = early_piece.astype(f32)
    output_total = early_piece[:, :head_width]
    inner_total = early_piece[:, head_width : head_width + hidden_width]
    outer_total = early_piece[:, head_width + hidden_width : head_width + 2 * hidden_width]
    early_vectors = early_piece[:, head_width + 2 * hidden_width :]
    outbias_total, attn_gain_total, attn_shift_total, outerbias_total, final_gain_total, final_shift_total = (
        early_vectors[:, :6].T
    )
    ibias_total = lax.dynamic_slice_in_dim(
        early_vectors[:, 6:], tensor_place * local_rows, local_rows, 0
    ).reshape(-1)
    dqkv = jnp.concatenate([dquery, dkeys, dvalues], axis=1)
    qkv_weight_part = jnp.einsum("td,th->dh", tokens, dqkv, preferred_element_type=f32)
    query_bias_part = jnp.sum(dquery.astype(f32), 0)
    value_bias_part = jnp.sum(dvalues.astype(f32), 0)
    dinput_part = jnp.einsum("th,dh->td", dqkv, qkv_full, preferred_element_type=f32)
    tokens_gradient = dres_first + tp_sum(dinput_part)
    late = jnp.concatenate(
        [
            qkv_weight_part,
            tp_gather(query_bias_part).reshape(rows, 1),
            tp_gather(value_bias_part).reshape(rows, 1),
        ],
        axis=1,
    ).astype(low)
    late, early_piece = lax.optimization_barrier((late, early_piece))
    late_piece = lax.psum(shard_scatter(late).astype(low), "ctx").astype(f32)
    query_total = late_piece[:, :head_width]
    key_total = late_piece[:, head_width : 2 * head_width]
    value_total = late_piece[:, 2 * head_width : 3 * head_width]
    qbias_total = lax.dynamic_slice_in_dim(
        late_piece[:, 3 * head_width], tensor_place * local_rows, local_rows
    )
    vbias_total = lax.dynamic_slice_in_dim(
        late_piece[:, 3 * head_width + 1], tensor_place * local_rows, local_rows
    )
    return (
        layer_out,
        tokens_gradient,
        query_total,
        qbias_total,
        key_total,
        value_total,
        vbias_total,
        output_total,
        outbias_total,
        attn_gain_total,
        attn_shift_total,
        inner_total,
        ibias_total,
        outer_total,
        outerbias_total,
        final_gain_total,
        final_shift_total,
    )


def solution(mesh):
    placed = (
        P(("shard", "ctx"), None),
        P("shard"),
        P("shard", "tp"),
        P(("shard", "tp")),
        P("shard", "tp"),
        P("shard", "tp"),
        P(("shard", "tp")),
        P("shard", "tp"),
        P("shard"),
        P("shard"),
        P("shard"),
        P("shard", "tp"),
        P(("shard", "tp")),
        P("shard", "tp"),
        P("shard"),
        P("shard"),
        P("shard"),
        P(("shard", "ctx"), None),
    )
    return jax.shard_map(
        on_device,
        mesh=mesh,
        in_specs=placed,
        out_specs=(
            P(("shard", "ctx"), None),
            P(("shard", "ctx"), None),
            P("shard", "tp"),
            P(("shard", "tp")),
            P("shard", "tp"),
            P("shard", "tp"),
            P(("shard", "tp")),
            P("shard", "tp"),
            P("shard"),
            P("shard"),
            P("shard"),
            P("shard", "tp"),
            P(("shard", "tp")),
            P("shard", "tp"),
            P("shard"),
            P("shard"),
            P("shard"),
        ),
        check_vma=False,
    )
```
